32 devices in a mesh: lat: 2 (over y), lev: 4 (over x, core), ocn: 4 (over z).
Axes of the slice: x: 2, y: 2, z: 4, core: 2. Of those that a mesh axis runs over, the one named last changes fastest.
Arguments:
- atmos_fields: bfloat16 [2, 24, 2560, 5632], P(None, 'lev', ('lat', 'ocn')), may hold values from -6 to 6
- lat_points: int32 [2560], P(('lat', 'ocn')), may hold values from 20 to 5632, as said below
- wave_order: int32 [32], replicated, may hold values from 0 to 31, each once
- legendre: bfloat16 [32, 2560, 1536], P(('lat', 'ocn'), None, 'lev'), may hold values from -0.125 to 0.125
- column_weight: bfloat16 [2, 24], P(None, 'lev'), may hold values from -1.25 to 1.25
- block_remap: int32 [2560, 44], P(('lat', 'ocn'), 'lev'), may hold values from 0 to 2175, as said below
- ocean_temp: float32 [128, 2176], P(('lat', 'ocn')), may hold values from -6 to 6
- ocean_salt: float32 [128, 2176], P(('lat', 'ocn')), may hold values from -6 to 6
- sea_mask: int32 [128, 17], P(('lat', 'ocn')), may hold values 0 or 1
Outputs:
- spectra: float32 [32, 96, 1536], P(('lat', 'ocn'), None, 'lev')
- temp_next: float32 [128, 2176], P(('lat', 'ocn'))
- salt_next: float32 [128, 2176], P(('lat', 'ocn'))
- surface_temp: float32 [2560, 5632], P(('lat', 'ocn'), 'lev')
The draws below stay inside these ranges and needn't reach their ends.
Inputs may be any that keep to these rules, and one draw needn't show every extreme that they name: `lat_points`: a multiple of 4 for every latitude row. `wave_order`: each wavenumber appears once. `block_remap`: the blocks of latitude band g (rows g * 320 onward) name tiles of ocean sections g - 1, g or g + 1 only; section g holds tiles g * 16 * 17 onward, in row order.
All inputs are finite; a program needn't handle non-finite values. No bound on the sum of `sea_mask` on one device may be relied on, other than what follows from the above.
Results may differ from the reference program's by a relative error of at most 0.0037.
Values may be sent and summed in bfloat16 or wider, within the bound.
No kernel may reach another device: no remote copies, remote signals or barrier semaphores. Data moves between devices by JAX's collectives and lax.ppermute only.
A program may use at most 192 MiB of HBM per device.

```python
import math
import jax
import jax.numpy as jnp
from jax import lax

FIELDS = 2
LEVELS = 24
BANDS = 8
NLAT = 2560
NLON = 5632
BLOCK = 128
WAVES = 32
DEGREES = 1536
OROW_DEV = 16
OCOLS = 2176
OROWS = 128
TILES = 2176


def draw_lat_points(key, part):
    row_index = jnp.arange(NLAT, dtype=jnp.int32)
    jitter = jax.random.randint(key, (NLAT,), 0, 8)
    jitter = jitter.at[0].set(0)
    return jnp.minimum(NLON, 20 + 4 * row_index + 4 * jitter).astype(jnp.int32)


def draw_block_remap(key, part):
    blocks_row = NLON // BLOCK
    per_band = NLAT // BANDS
    tile_count = OROW_DEV * OCOLS // BLOCK
    band_of = (jnp.arange(NLAT, dtype=jnp.int32) // per_band)[:, None]
    key_step = jax.random.fold_in(key, 11)
    key_tile = jax.random.fold_in(key, 23)
    offset = jax.random.randint(key_step, (NLAT, blocks_row), -1, 2)
    target = jnp.clip(band_of + offset, 0, BANDS - 1)
    within = jax.random.randint(key_tile, (NLAT, blocks_row), 0, tile_count)
    result = target * tile_count + within
    result = result.at[0, 0].set(0)
    result = result.at[NLAT - 1, blocks_row - 1].set(BANDS * tile_count - 1)
    return result.astype(jnp.int32)


def plant(values, key, least, top_value):
    longest = values.shape.index(max(values.shape))
    spots = []
    for shift in (0, 1):
        where = [jax.random.randint(jax.random.fold_in(key, axis), (), 0, length) for axis, length in enumerate(values.shape)]
        where[longest] = (where[longest] + shift) % values.shape[longest]
        spots.append(tuple(where))
    return values.at[spots[0]].set(least).at[spots[1]].set(top_value)


def level_of(key, shape, pieces, least, top_value):
    def one(dim, blocks):
        heights = jax.random.uniform(jax.random.fold_in(jax.random.fold_in(key, 6), dim), (blocks,), jnp.float32, least / len(pieces), top_value / len(pieces))
        return jnp.repeat(jnp.exp(heights), shape[dim] // blocks).reshape((-1,) + (1,) * (len(shape) - dim - 1))

    loudness = one(*pieces[0])
    for cut in pieces[1:]:
        loudness = loudness * one(*cut)
    return loudness


def noise(rng, extent, deviation, reach, shards=(), kind=jnp.bfloat16):
    values = jax.random.normal(rng, extent, jnp.float32) * deviation
    if len(shards) > 0:
        values = level_of(rng, extent, shards, -0.22, 0.18) * values
    return jnp.clip(values, min=-reach, max=reach).astype(kind)


def setup_inputs(seed: int = 0) -> dict:
    seeds = jax.random.split(jax.random.key(seed), 10)
    return {
        "atmos_fields": noise(seeds[0], (FIELDS, LEVELS, NLAT, NLON), 1.0, 6.0, ((1, 4), (2, 8))),
        "lat_points": draw_lat_points(jax.random.fold_in(seeds[9], 71), 0),
        "wave_order": jax.random.permutation(seeds[2], WAVES).astype(jnp.int32),
        "legendre": noise(seeds[3], (WAVES, NLAT, DEGREES), NLAT ** -0.5, 0.125, ((0, 8), (2, 4))),
        "column_weight": noise(seeds[4], (FIELDS, LEVELS), LEVELS ** -0.5, 1.25, ((1, 4),)),
        "block_remap": draw_block_remap(jax.random.fold_in(seeds[9], 71), 0),
        "ocean_temp": noise(seeds[6], (OROWS, OCOLS), 1.0, 6.0, ((0, 8),), jnp.float32),
        "ocean_salt": noise(seeds[7], (OROWS, OCOLS), 1.0, 6.0, ((0, 8),), jnp.float32),
        "sea_mask": plant((jax.random.randint(seeds[8], (OROWS, OCOLS // BLOCK), 0, 4) < 3).astype(jnp.int32), jax.random.fold_in(seeds[8], 1), 0, 1),
    }


FULL_TURN = 2.0 * math.pi
DIFFUSION = 0.2
COUPLING = 0.5

def fourier_table(wave_order, length):
    points = jnp.arange(length, dtype=jnp.int32)
    phase = wave_order[None, :] * points[:, None] % length
    angle = phase.astype(jnp.float32) * (FULL_TURN / length)
    table = jnp.concatenate([jnp.cos(angle), -jnp.sin(angle)], axis=1).astype(jnp.bfloat16)
    return (table, points)

def reference(atmos_fields, lat_points, wave_order, legendre, column_weight, block_remap, ocean_temp, ocean_salt, sea_mask):
    table, points = fourier_table(wave_order, NLON)
    point_mask = points[None, :] < lat_points[:, None]
    masked = jnp.where(point_mask[None, None], atmos_fields, jnp.zeros((), jnp.bfloat16))
    raw_sums = jnp.dot(masked.reshape(-1, NLON), table, preferred_element_type=jnp.float32)
    raw_sums = raw_sums.reshape(FIELDS, LEVELS, NLAT, 2, WAVES)
    inverse_root = 1.0 / jnp.sqrt(lat_points.astype(jnp.float32))
    weights = jnp.where(2 * wave_order[None, :] < lat_points[:, None], inverse_root[:, None], jnp.zeros((), jnp.float32))
    coeffs = (raw_sums * weights[None, None, :, None, :]).astype(jnp.bfloat16)
    coeffs = coeffs.transpose(4, 1, 0, 3, 2).reshape(WAVES, LEVELS * FIELDS * 2, NLAT)
    spectra = lax.map(lambda slot_pair: jnp.dot(slot_pair[0], slot_pair[1], preferred_element_type=jnp.float32), (coeffs, legendre))
    columns = jnp.stack([jnp.dot(column_weight[field_idx], masked[field_idx].reshape(LEVELS, -1), preferred_element_type=jnp.float32) for field_idx in range(FIELDS)])
    blocks = columns.reshape(FIELDS, NLAT, NLON // BLOCK, BLOCK).transpose(1, 2, 0, 3).reshape(-1, FIELDS * BLOCK)
    tile_sums = jax.ops.segment_sum(blocks, block_remap.reshape(-1), num_segments=TILES)
    forcing = tile_sums.reshape(OROWS, OCOLS // BLOCK, FIELDS, BLOCK).transpose(2, 0, 1, 3).reshape(FIELDS, OROWS, OCOLS)
    sea_cells = jnp.broadcast_to(sea_mask[:, :, None], (OROWS, OCOLS // BLOCK, BLOCK)).reshape(OROWS, OCOLS).astype(jnp.float32)
    ocean_state = jnp.stack([ocean_temp, ocean_salt])
    padded = jnp.pad(ocean_state, ((0, 0), (1, 1), (0, 0)))
    laplace = padded[:, 2:] + padded[:, :-2] + jnp.roll(ocean_state, 1, 2) + jnp.roll(ocean_state, -1, 2) - 4.0 * ocean_state
    updated = ocean_state + DIFFUSION * laplace + COUPLING * sea_cells[None] * forcing
    temp_next = updated[0]
    salt_next = updated[1]
    surface = temp_next.reshape(TILES, BLOCK)[block_remap.reshape(-1)].reshape(NLAT, NLON)
    surface_temp = jnp.where(point_mask, surface, jnp.zeros((), jnp.float32))
    return (spectra, temp_next, salt_next, surface_temp)
```

```python
import math

import jax
import jax.numpy as jnp
from jax import lax
from jax.experimental import pallas as pl
from jax.experimental.pallas import tpu as pltpu
from jax.sharding import PartitionSpec as P

FIELDS = 2
BLOCK = 128


FULL_TURN = 2.0 * math.pi
DIFFUSION = 0.2
COUPLING = 0.5


def with_halo(cells, sides, width):
    for axis, dim in sides:
        count = lax.axis_size(axis)
        ends = count - 1
        head = lax.slice_in_dim(cells, 0, width, axis=dim)
        tail = lax.slice_in_dim(cells, cells.shape[dim] - width, cells.shape[dim], axis=dim)
        cells = jnp.concatenate(
            [
                lax.ppermute(tail, axis, [(i, (i + 1) % count) for i in range(ends)]),
                cells,
                lax.ppermute(head, axis, [((i + 1) % count, i) for i in range(ends)]),
            ],
            axis=dim,
        )
    return cells


def fourier_table(wave_order, length):
    points = jnp.arange(length, dtype=jnp.int32)
    phase = wave_order[None, :] * points[:, None] % length
    angle = phase.astype(jnp.float32) * (FULL_TURN / length)
    table = jnp.concatenate([jnp.cos(angle), -jnp.sin(angle)], axis=1).astype(jnp.bfloat16)
    return (table, points)


def row_block(rows):
    for size in (32, 16):
        if rows % size == 0:
            return size
    return rows


def transform_kernel(points_ref, cells_ref, table_ref, weight_ref, slot_ref, sums_ref, acc_ref):
    step = pl.program_id(0)

    @pl.when(step == 0)
    def _():
        acc_ref[...] = jnp.zeros_like(acc_ref)

    nfields, nlev, rows, lon_count = cells_ref.shape
    nslot = acc_ref.shape[0]
    table = table_ref[...]
    inside = lax.broadcasted_iota(jnp.int32, (rows, lon_count), 1) < points_ref[...]
    cells = jnp.where(inside[None, None], cells_ref[...], jnp.zeros((), jnp.bfloat16))
    if rows % 16 == 0:
        sums = jnp.dot(
            cells.reshape(nfields * nlev * rows, lon_count), table, preferred_element_type=jnp.float32
        )
        sums_ref[...] = sums.reshape(sums_ref.shape)
    else:
        for f in range(nfields):
            for l in range(nlev):
                sums_ref[f, l] = jnp.dot(cells[f, l], table, preferred_element_type=jnp.float32)
    pieces = []
    for f in range(nfields):
        flux = weight_ref[f, 0] * cells[f, 0].astype(jnp.float32)
        for l in range(1, nlev):
            flux = flux + weight_ref[f, l] * cells[f, l].astype(jnp.float32)
        high = flux.astype(jnp.bfloat16).astype(jnp.float32)
        pieces.append(high)
        pieces.append(flux - high)
    nblocks = lon_count // BLOCK
    stacked = jnp.concatenate(
        [
            jnp.concatenate([p[:, b * BLOCK : (b + 1) * BLOCK] for p in pieces], axis=1)
            for b in range(nblocks)
        ],
        axis=0,
    ).astype(jnp.bfloat16)
    onehot = (
        lax.broadcasted_iota(jnp.int32, (nslot, nblocks * rows), 0) == slot_ref[0]
    ).astype(jnp.bfloat16)
    acc_ref[...] += jnp.dot(onehot, stacked, preferred_element_type=jnp.float32)


def fused_transform(atmos_fields, lat_points, table, column_weight, slots, nslot):
    nfields, nlev, lat_band, lon_count = atmos_fields.shape
    rows = row_block(lat_band)
    steps = lat_band // rows
    nblocks = lon_count // BLOCK
    wave2 = table.shape[1]
    slot_rows = slots.reshape(steps, rows, nblocks).transpose(0, 2, 1).reshape(steps, 1, nblocks * rows)
    return pl.pallas_call(
        transform_kernel,
        grid=(steps,),
        in_specs=[
            pl.BlockSpec((rows, 1), lambda r: (r, 0)),
            pl.BlockSpec((nfields, nlev, rows, lon_count), lambda r: (0, 0, r, 0)),
            pl.BlockSpec((lon_count, wave2), lambda r: (0, 0)),
            pl.BlockSpec(memory_space=pltpu.SMEM),
            pl.BlockSpec((1, 1, nblocks * rows), lambda r: (r, 0, 0)),
        ],
        out_specs=[
            pl.BlockSpec((nfields, nlev, rows, wave2), lambda r: (0, 0, r, 0)),
            pl.BlockSpec((nslot, 2 * nfields * BLOCK), lambda r: (0, 0)),
        ],
        out_shape=[
            jax.ShapeDtypeStruct((nfields, nlev, lat_band, wave2), jnp.float32),
            jax.ShapeDtypeStruct((nslot, 2 * nfields * BLOCK), jnp.float32),
        ],
        compiler_params=pltpu.CompilerParams(dimension_semantics=("arbitrary",)),
    )(lat_points[:, None], atmos_fields, table, column_weight.astype(jnp.float32), slot_rows)


def body(
    atmos_fields,
    lat_points,
    wave_order,
    legendre,
    column_weight,
    block_remap,
    ocean_temp,
    ocean_salt,
    sea_mask,
):
    nfields, lev_dev, lat_band, lon_count = atmos_fields.shape
    wave_count = wave_order.shape[0]
    table, points = fourier_table(wave_order, lon_count)
    inverse_root = 1.0 / jnp.sqrt(lat_points.astype(jnp.float32))
    weights = jnp.where(
        2 * wave_order[None, :] < lat_points[:, None],
        inverse_root[:, None],
        jnp.zeros((), jnp.float32),
    )
    field_count = nfields
    ocean_rows, ocean_cols = ocean_temp.shape
    tile_count = ocean_rows * ocean_cols // BLOCK
    band_index = lax.axis_index(("lat", "ocn"))

    def slot_of(targets):
        return (targets // tile_count - band_index + 1) * tile_count + targets % tile_count

    local_slot = slot_of(block_remap.reshape(-1))
    quarter = lon_count // lax.axis_size("lev")
    full_remap = lax.all_gather(block_remap, "lev", axis=1, tiled=True)
    every_slot = slot_of(full_remap)
    raw_sums, split_sums = fused_transform(
        atmos_fields, lat_points, table, column_weight, every_slot, 3 * tile_count
    )
    raw_sums = raw_sums.reshape(field_count, lev_dev, lat_band, 2, wave_count)
    coeffs = (raw_sums * weights[None, None, :, None, :]).astype(jnp.bfloat16)
    regrouped = lax.all_to_all(
        coeffs.transpose(4, 1, 0, 3, 2).reshape(wave_count, lev_dev * field_count * 2, lat_band),
        ("lat", "ocn"),
        split_axis=0,
        concat_axis=2,
        tiled=True,
    )
    spectra = jnp.einsum(
        "srj,sjd->srd",
        lax.all_gather(regrouped, "lev", axis=1, tiled=True),
        legendre,
        preferred_element_type=jnp.float32,
    )
    split_sums = split_sums.reshape(3 * tile_count, FIELDS, 2, BLOCK)
    outgoing = (split_sums[:, :, 0] + split_sums[:, :, 1]).reshape(3 * tile_count, FIELDS * BLOCK)
    widened = with_halo(outgoing, ((("lat", "ocn"), 0),), tile_count)
    arrived = (
        widened[:tile_count] + widened[2 * tile_count : 3 * tile_count] + widened[4 * tile_count :]
    )
    tile_sums = lax.psum(arrived, "lev")
    forcing = (
        tile_sums.reshape(ocean_rows, ocean_cols // BLOCK, FIELDS, BLOCK)
        .transpose(2, 0, 1, 3)
        .reshape(FIELDS, ocean_rows, ocean_cols)
    )
    sea_cells = (
        jnp.broadcast_to(sea_mask[:, :, None], (ocean_rows, ocean_cols // BLOCK, BLOCK))
        .reshape(ocean_rows, ocean_cols)
        .astype(jnp.float32)
    )
    ocean_state = jnp.stack([ocean_temp, ocean_salt])
    padded = with_halo(ocean_state, ((("lat", "ocn"), 1),), 1)
    laplace = (
        padded[:, 2:]
        + padded[:, :-2]
        + jnp.roll(ocean_state, 1, 2)
        + jnp.roll(ocean_state, -1, 2)
        - 4.0 * ocean_state
    )
    updated = ocean_state + DIFFUSION * laplace + COUPLING * sea_cells[None] * forcing
    temp_next = updated[0]
    salt_next = updated[1]
    returned = with_halo(temp_next, ((("lat", "ocn"), 0),), ocean_rows)
    tiles_near = returned.reshape(3 * tile_count, BLOCK)
    surface = jnp.take(tiles_near, local_slot, axis=0).reshape(lat_band, quarter)
    own_points = lax.axis_index("lev") * quarter + jnp.arange(quarter, dtype=jnp.int32)
    surface_temp = jnp.where(
        own_points[None, :] < lat_points[:, None], surface, jnp.zeros((), jnp.float32)
    )
    return (spectra, temp_next, salt_next, surface_temp)


def solution(mesh):
    placed = (
        P(None, "lev", ("lat", "ocn"), None),
        P(("lat", "ocn")),
        P(),
        P(("lat", "ocn"), None, "lev"),
        P(None, "lev"),
        P(("lat", "ocn"), "lev"),
        P(("lat", "ocn"), None),
        P(("lat", "ocn"), None),
        P(("lat", "ocn"), None),
    )
    return jax.shard_map(
        body,
        mesh=mesh,
        in_specs=placed,
        out_specs=(
            P(("lat", "ocn"), None, "lev"),
            P(("lat", "ocn"), None),
            P(("lat", "ocn"), None),
            P(("lat", "ocn"), "lev"),
        ),
        check_vma=False,
    )
```

```python
import math

import jax
import jax.numpy as jnp
from jax import lax
from jax.experimental import pallas as pl
from jax.experimental.pallas import tpu as pltpu
from jax.sharding import PartitionSpec as P

FIELDS = 2
BLOCK = 128


FULL_TURN = 2.0 * math.pi
DIFFUSION = 0.2
COUPLING = 0.5


def with_halo(cells, sides, width):
    for axis, dim in sides:
        count = lax.axis_size(axis)
        ends = count - 1
        head = lax.slice_in_dim(cells, 0, width, axis=dim)
        tail = lax.slice_in_dim(cells, cells.shape[dim] - width, cells.shape[dim], axis=dim)
        cells = jnp.concatenate(
            [
                lax.ppermute(tail, axis, [(i, (i + 1) % count) for i in range(ends)]),
                cells,
                lax.ppermute(head, axis, [((i + 1) % count, i) for i in range(ends)]),
            ],
            axis=dim,
        )
    return cells


def fourier_table(wave_order, length):
    points = jnp.arange(length, dtype=jnp.int32)
    phase = wave_order[:, None] * points[None, :] % length
    angle = phase.astype(jnp.float32) * (FULL_TURN / length)
    table = jnp.concatenate([jnp.cos(angle), -jnp.sin(angle)], axis=0).astype(jnp.bfloat16)
    return (table, points)


def lev_sum(values):
    count = lax.axis_size("lev")
    if count & (count - 1):
        return lax.psum(values, "lev")
    stride = 1
    while stride < count:
        values = values + lax.ppermute(values, "lev", [(i, i ^ stride) for i in range(count)])
        stride *= 2
    return values


def lev_gather(values, axis):
    count = lax.axis_size("lev")
    if count & (count - 1):
        return lax.all_gather(values, "lev", axis=axis, tiled=True)
    index = lax.axis_index("lev")
    stride = 1
    while stride < count:
        other = lax.ppermute(values, "lev", [(i, i ^ stride) for i in range(count)])
        upper = (index // stride) % 2 == 1
        values = jnp.where(
            upper,
            jnp.concatenate([other, values], axis=axis),
            jnp.concatenate([values, other], axis=axis),
        )
        stride *= 2
    return values


def row_block(rows):
    for size in (32, 16):
        if rows % size == 0:
            return size
    return rows


def transform_kernel(points_ref, cells_ref, table_ref, weight_ref, slot_ref, sums_ref, acc_ref):
    step = pl.program_id(0)

    @pl.when(step == 0)
    def _():
        acc_ref[...] = jnp.zeros_like(acc_ref)

    nfields, nlev, rows, lon_count = cells_ref.shape
    nslot = acc_ref.shape[0]
    table = table_ref[...]
    inside = lax.broadcasted_iota(jnp.int32, (rows, lon_count), 1) < points_ref[...]
    cells = jnp.where(inside[None, None], cells_ref[...], jnp.zeros((), jnp.bfloat16))
    if rows % 16 == 0:
        sums = lax.dot_general(
            cells.reshape(nfields * nlev * rows, lon_count),
            table,
            (((1,), (1,)), ((), ())),
            preferred_element_type=jnp.float32,
        )
        sums_ref[...] = sums.reshape(sums_ref.shape)
    else:
        for f in range(nfields):
            for l in range(nlev):
                sums_ref[f, l] = lax.dot_general(
                    cells[f, l], table, (((1,), (1,)), ((), ())), preferred_element_type=jnp.float32
                )
    pieces = []
    for f in range(nfields):
        flux = weight_ref[f, 0] * cells[f, 0].astype(jnp.float32)
        for l in range(1, nlev):
            flux = flux + weight_ref[f, l] * cells[f, l].astype(jnp.float32)
        high = flux.astype(jnp.bfloat16).astype(jnp.float32)
        pieces.append(high)
        pieces.append(flux - high)
    nblocks = lon_count // BLOCK
    stacked = jnp.concatenate(
        [
            jnp.concatenate([p[:, b * BLOCK : (b + 1) * BLOCK] for p in pieces], axis=1)
            for b in range(nblocks)
        ],
        axis=0,
    ).astype(jnp.bfloat16)
    onehot = (
        lax.broadcasted_iota(jnp.int32, (nslot, nblocks * rows), 0) == slot_ref[0]
    ).astype(jnp.bfloat16)
    acc_ref[...] += jnp.dot(onehot, stacked, preferred_element_type=jnp.float32)


def fused_transform(atmos_fields, lat_points, table, column_weight, slots, nslot):
    nfields, nlev, lat_band, lon_count = atmos_fields.shape
    rows = row_block(lat_band)
    steps = lat_band // rows
    nblocks = lon_count // BLOCK
    wave2 = table.shape[0]
    slot_rows = slots.reshape(steps, rows, nblocks).transpose(0, 2, 1).reshape(steps, 1, nblocks * rows)
    return pl.pallas_call(
        transform_kernel,
        grid=(steps,),
        in_specs=[
            pl.BlockSpec((rows, 1), lambda r: (r, 0)),
            pl.BlockSpec((nfields, nlev, rows, lon_count), lambda r: (0, 0, r, 0)),
            pl.BlockSpec((wave2, lon_count), lambda r: (0, 0)),
            pl.BlockSpec(memory_space=pltpu.SMEM),
            pl.BlockSpec((1, 1, nblocks * rows), lambda r: (r, 0, 0)),
        ],
        out_specs=[
            pl.BlockSpec((nfields, nlev, rows, wave2), lambda r: (0, 0, r, 0)),
            pl.BlockSpec((nslot, 2 * nfields * BLOCK), lambda r: (0, 0)),
        ],
        out_shape=[
            jax.ShapeDtypeStruct((nfields, nlev, lat_band, wave2), jnp.float32),
            jax.ShapeDtypeStruct((nslot, 2 * nfields * BLOCK), jnp.float32),
        ],
        compiler_params=pltpu.CompilerParams(dimension_semantics=("arbitrary",)),
    )(lat_points[:, None], atmos_fields, table, column_weight.astype(jnp.float32), slot_rows)


def body(
    atmos_fields,
    lat_points,
    wave_order,
    legendre,
    column_weight,
    block_remap,
    ocean_temp,
    ocean_salt,
    sea_mask,
):
    nfields, lev_dev, lat_band, lon_count = atmos_fields.shape
    wave_count = wave_order.shape[0]
    table, points = fourier_table(wave_order, lon_count)
    inverse_root = 1.0 / jnp.sqrt(lat_points.astype(jnp.float32))
    weights = jnp.where(
        2 * wave_order[None, :] < lat_points[:, None],
        inverse_root[:, None],
        jnp.zeros((), jnp.float32),
    )
    field_count = nfields
    ocean_rows, ocean_cols = ocean_temp.shape
    tile_count = ocean_rows * ocean_cols // BLOCK
    band_index = lax.axis_index(("lat", "ocn"))

    def slot_of(targets):
        return (targets // tile_count - band_index + 1) * tile_count + targets % tile_count

    local_slot = slot_of(block_remap.reshape(-1))
    quarter = lon_count // lax.axis_size("lev")
    full_remap = lev_gather(block_remap, 1)
    every_slot = slot_of(full_remap)
    raw_sums, split_sums = fused_transform(
        atmos_fields, lat_points, table, column_weight, every_slot, 3 * tile_count
    )
    raw_sums = raw_sums.reshape(field_count, lev_dev, lat_band, 2, wave_count)
    coeffs = (raw_sums * weights[None, None, :, None, :]).astype(jnp.bfloat16)
    regrouped = lax.all_to_all(
        coeffs.transpose(4, 1, 0, 3, 2).reshape(wave_count, lev_dev * field_count * 2, lat_band),
        ("lat", "ocn"),
        split_axis=0,
        concat_axis=2,
        tiled=True,
    )
    spectra = jnp.einsum(
        "srj,sjd->srd",
        lev_gather(regrouped, 1),
        legendre,
        preferred_element_type=jnp.float32,
    )
    split_sums = split_sums.reshape(3 * tile_count, FIELDS, 2, BLOCK)
    outgoing = (split_sums[:, :, 0] + split_sums[:, :, 1]).reshape(3 * tile_count, FIELDS * BLOCK)
    widened = with_halo(outgoing, ((("lat", "ocn"), 0),), tile_count)
    arrived = (
        widened[:tile_count] + widened[2 * tile_count : 3 * tile_count] + widened[4 * tile_count :]
    )
    tile_sums = lev_sum(arrived)
    forcing = (
        tile_sums.reshape(ocean_rows, ocean_cols // BLOCK, FIELDS, BLOCK)
        .transpose(2, 0, 1, 3)
        .reshape(FIELDS, ocean_rows, ocean_cols)
    )
    sea_cells = (
        jnp.broadcast_to(sea_mask[:, :, None], (ocean_rows, ocean_cols // BLOCK, BLOCK))
        .reshape(ocean_rows, ocean_cols)
        .astype(jnp.float32)
    )
    ocean_state = jnp.stack([ocean_temp, ocean_salt])
    padded = with_halo(ocean_state, ((("lat", "ocn"), 1),), 1)
    laplace = (
        padded[:, 2:]
        + padded[:, :-2]
        + jnp.roll(ocean_state, 1, 2)
        + jnp.roll(ocean_state, -1, 2)
        - 4.0 * ocean_state
    )
    updated = ocean_state + DIFFUSION * laplace + COUPLING * sea_cells[None] * forcing
    temp_next = updated[0]
    salt_next = updated[1]
    returned = with_halo(temp_next, ((("lat", "ocn"), 0),), ocean_rows)
    tiles_near = returned.reshape(3 * tile_count, BLOCK)
    surface = jnp.take(tiles_near, local_slot, axis=0).reshape(lat_band, quarter)
    own_points = lax.axis_index("lev") * quarter + jnp.arange(quarter, dtype=jnp.int32)
    surface_temp = jnp.where(
        own_points[None, :] < lat_points[:, None], surface, jnp.zeros((), jnp.float32)
    )
    return (spectra, temp_next, salt_next, surface_temp)


def solution(mesh):
    placed = (
        P(None, "lev", ("lat", "ocn"), None),
        P(("lat", "ocn")),
        P(),
        P(("lat", "ocn"), None, "lev"),
        P(None, "lev"),
        P(("lat", "ocn"), "lev"),
        P(("lat", "ocn"), None),
        P(("lat", "ocn"), None),
        P(("lat", "ocn"), None),
    )
    return jax.shard_map(
        body,
        mesh=mesh,
        in_specs=placed,
        out_specs=(
            P(("lat", "ocn"), None, "lev"),
            P(("lat", "ocn"), None),
            P(("lat", "ocn"), None),
            P(("lat", "ocn"), "lev"),
        ),
        check_vma=False,
    )
```

```python
import math

import jax
import jax.numpy as jnp
from jax import lax
from jax.experimental import pallas as pl
from jax.experimental.pallas import tpu as pltpu
from jax.sharding import PartitionSpec as P

FIELDS = 2
BLOCK = 128


FULL_TURN = 2.0 * math.pi
DIFFUSION = 0.2
COUPLING = 0.5


def with_halo(cells, sides, width):
    for axis, dim in sides:
        count = lax.axis_size(axis)
        ends = count - 1
        head = lax.slice_in_dim(cells, 0, width, axis=dim)
        tail = lax.slice_in_dim(cells, cells.shape[dim] - width, cells.shape[dim], axis=dim)
        cells = jnp.concatenate(
            [
                lax.ppermute(tail, axis, [(i, (i + 1) % count) for i in range(ends)]),
                cells,
                lax.ppermute(head, axis, [((i + 1) % count, i) for i in range(ends)]),
            ],
            axis=dim,
        )
    return cells


def fourier_table(wave_order, length):
    points = jnp.arange(length, dtype=jnp.int32)
    phase = wave_order[:, None] * points[None, :] % length
    angle = phase.astype(jnp.float32) * (FULL_TURN / length)
    table = jnp.concatenate([jnp.cos(angle), -jnp.sin(angle)], axis=0).astype(jnp.bfloat16)
    return (table, points)


def lev_sum(values):
    count = lax.axis_size("lev")
    if count != 4:
        return lax.psum(values, "lev")
    near, far, both = (
        lax.ppermute(values, "lev", [(i, i ^ d) for i in range(count)]) for d in (1, 2, 3)
    )
    return (values + near) + (far + both)


def lev_gather(values, axis):
    count = lax.axis_size("lev")
    if count & (count - 1):
        return lax.all_gather(values, "lev", axis=axis, tiled=True)
    index = lax.axis_index("lev")
    pieces = [values] + [
        lax.ppermute(values, "lev", [(i, i ^ d) for i in range(count)]) for d in range(1, count)
    ]
    stacked = jnp.stack(pieces)
    order = jnp.bitwise_xor(index, jnp.arange(count, dtype=jnp.int32))
    ordered = jnp.take(stacked, order, axis=0)
    return jnp.concatenate([ordered[i] for i in range(count)], axis=axis)


def row_block(rows):
    for size in (32, 16):
        if rows % size == 0:
            return size
    return rows


def transform_kernel(points_ref, cells_ref, table_ref, weight_ref, slot_ref, sums_ref, acc_ref):
    step = pl.program_id(0)

    @pl.when(step == 0)
    def _():
        acc_ref[...] = jnp.zeros_like(acc_ref)

    nfields, nlev, rows, lon_count = cells_ref.shape
    nslot = acc_ref.shape[0]
    table = table_ref[...]
    inside = lax.broadcasted_iota(jnp.int32, (rows, lon_count), 1) < points_ref[...]
    cells = jnp.where(inside[None, None], cells_ref[...], jnp.zeros((), jnp.bfloat16))
    if rows % 16 == 0:
        sums = lax.dot_general(
            cells.reshape(nfields * nlev * rows, lon_count),
            table,
            (((1,), (1,)), ((), ())),
            preferred_element_type=jnp.float32,
        )
        sums_ref[...] = sums.reshape(sums_ref.shape)
    else:
        for f in range(nfields):
            for l in range(nlev):
                sums_ref[f, l] = lax.dot_general(
                    cells[f, l], table, (((1,), (1,)), ((), ())), preferred_element_type=jnp.float32
                )
    pieces = []
    for f in range(nfields):
        flux = weight_ref[f, 0] * cells[f, 0].astype(jnp.float32)
        for l in range(1, nlev):
            flux = flux + weight_ref[f, l] * cells[f, l].astype(jnp.float32)
        high = flux.astype(jnp.bfloat16).astype(jnp.float32)
        pieces.append(high)
        pieces.append(flux - high)
    nblocks = lon_count // BLOCK
    stacked = jnp.concatenate(
        [
            jnp.concatenate([p[:, b * BLOCK : (b + 1) * BLOCK] for p in pieces], axis=1)
            for b in range(nblocks)
        ],
        axis=0,
    ).astype(jnp.bfloat16)
    onehot = (
        lax.broadcasted_iota(jnp.int32, (nslot, nblocks * rows), 0) == slot_ref[0]
    ).astype(jnp.bfloat16)
    acc_ref[...] += jnp.dot(onehot, stacked, preferred_element_type=jnp.float32)


def fused_transform(atmos_fields, lat_points, table, column_weight, slots, nslot):
    nfields, nlev, lat_band, lon_count = atmos_fields.shape
    rows = row_block(lat_band)
    steps = lat_band // rows
    nblocks = lon_count // BLOCK
    wave2 = table.shape[0]
    slot_rows = slots.reshape(steps, rows, nblocks).transpose(0, 2, 1).reshape(steps, 1, nblocks * rows)
    return pl.pallas_call(
        transform_kernel,
        grid=(steps,),
        in_specs=[
            pl.BlockSpec((rows, 1), lambda r: (r, 0)),
            pl.BlockSpec((nfields, nlev, rows, lon_count), lambda r: (0, 0, r, 0)),
            pl.BlockSpec((wave2, lon_count), lambda r: (0, 0)),
            pl.BlockSpec(memory_space=pltpu.SMEM),
            pl.BlockSpec((1, 1, nblocks * rows), lambda r: (r, 0, 0)),
        ],
        out_specs=[
            pl.BlockSpec((nfields, nlev, rows, wave2), lambda r: (0, 0, r, 0)),
            pl.BlockSpec((nslot, 2 * nfields * BLOCK), lambda r: (0, 0)),
        ],
        out_shape=[
            jax.ShapeDtypeStruct((nfields, nlev, lat_band, wave2), jnp.float32),
            jax.ShapeDtypeStruct((nslot, 2 * nfields * BLOCK), jnp.float32),
        ],
        compiler_params=pltpu.CompilerParams(dimension_semantics=("arbitrary",)),
    )(lat_points[:, None], atmos_fields, table, column_weight.astype(jnp.float32), slot_rows)


def body(
    atmos_fields,
    lat_points,
    wave_order,
    legendre,
    column_weight,
    block_remap,
    ocean_temp,
    ocean_salt,
    sea_mask,
):
    nfields, lev_dev, lat_band, lon_count = atmos_fields.shape
    wave_count = wave_order.shape[0]
    table, points = fourier_table(wave_order, lon_count)
    inverse_root = 1.0 / jnp.sqrt(lat_points.astype(jnp.float32))
    weights = jnp.where(
        2 * wave_order[None, :] < lat_points[:, None],
        inverse_root[:, None],
        jnp.zeros((), jnp.float32),
    )
    field_count = nfields
    ocean_rows, ocean_cols = ocean_temp.shape
    tile_count = ocean_rows * ocean_cols // BLOCK
    band_index = lax.axis_index(("lat", "ocn"))

    def slot_of(targets):
        return (targets // tile_count - band_index + 1) * tile_count + targets % tile_count

    local_slot = slot_of(block_remap.reshape(-1))
    quarter = lon_count // lax.axis_size("lev")
    full_remap = lev_gather(block_remap, 1)
    every_slot = slot_of(full_remap)
    raw_sums, split_sums = fused_transform(
        atmos_fields, lat_points, table, column_weight, every_slot, 3 * tile_count
    )
    raw_sums = raw_sums.reshape(field_count, lev_dev, lat_band, 2, wave_count)
    coeffs = (raw_sums * weights[None, None, :, None, :]).astype(jnp.bfloat16)
    regrouped = lax.all_to_all(
        coeffs.transpose(4, 1, 0, 3, 2).reshape(wave_count, lev_dev * field_count * 2, lat_band),
        ("lat", "ocn"),
        split_axis=0,
        concat_axis=2,
        tiled=True,
    )
    spectra = jnp.einsum(
        "srj,sjd->srd",
        lev_gather(regrouped, 1),
        legendre,
        preferred_element_type=jnp.float32,
    )
    split_sums = split_sums.reshape(3 * tile_count, FIELDS, 2, BLOCK)
    outgoing = (split_sums[:, :, 0] + split_sums[:, :, 1]).reshape(3 * tile_count, FIELDS * BLOCK)
    widened = with_halo(outgoing, ((("lat", "ocn"), 0),), tile_count)
    arrived = (
        widened[:tile_count] + widened[2 * tile_count : 3 * tile_count] + widened[4 * tile_count :]
    )
    tile_sums = lev_sum(arrived)
    forcing = (
        tile_sums.reshape(ocean_rows, ocean_cols // BLOCK, FIELDS, BLOCK)
        .transpose(2, 0, 1, 3)
        .reshape(FIELDS, ocean_rows, ocean_cols)
    )
    sea_cells = (
        jnp.broadcast_to(sea_mask[:, :, None], (ocean_rows, ocean_cols // BLOCK, BLOCK))
        .reshape(ocean_rows, ocean_cols)
        .astype(jnp.float32)
    )
    ocean_state = jnp.stack([ocean_temp, ocean_salt])
    padded = with_halo(ocean_state, ((("lat", "ocn"), 1),), 1)
    laplace = (
        padded[:, 2:]
        + padded[:, :-2]
        + jnp.roll(ocean_state, 1, 2)
        + jnp.roll(ocean_state, -1, 2)
        - 4.0 * ocean_state
    )
    updated = ocean_state + DIFFUSION * laplace + COUPLING * sea_cells[None] * forcing
    temp_next = updated[0]
    salt_next = updated[1]
    returned = with_halo(temp_next, ((("lat", "ocn"), 0),), ocean_rows)
    tiles_near = returned.reshape(3 * tile_count, BLOCK)
    surface = jnp.take(tiles_near, local_slot, axis=0).reshape(lat_band, quarter)
    own_points = lax.axis_index("lev") * quarter + jnp.arange(quarter, dtype=jnp.int32)
    surface_temp = jnp.where(
        own_points[None, :] < lat_points[:, None], surface, jnp.zeros((), jnp.float32)
    )
    return (spectra, temp_next, salt_next, surface_temp)


def solution(mesh):
    placed = (
        P(None, "lev", ("lat", "ocn"), None),
        P(("lat", "ocn")),
        P(),
        P(("lat", "ocn"), None, "lev"),
        P(None, "lev"),
        P(("lat", "ocn"), "lev"),
        P(("lat", "ocn"), None),
        P(("lat", "ocn"), None),
        P(("lat", "ocn"), None),
    )
    return jax.shard_map(
        body,
        mesh=mesh,
        in_specs=placed,
        out_specs=(
            P(("lat", "ocn"), None, "lev"),
            P(("lat", "ocn"), None),
            P(("lat", "ocn"), None),
            P(("lat", "ocn"), "lev"),
        ),
        check_vma=False,
    )
```

```python
import math

import jax
import jax.numpy as jnp
from jax import lax
from jax.experimental import pallas as pl
from jax.experimental.pallas import tpu as pltpu
from jax.sharding import PartitionSpec as P

FIELDS = 2
BLOCK = 128


FULL_TURN = 2.0 * math.pi
DIFFUSION = 0.2
COUPLING = 0.5


def with_halo(cells, sides, width):
    for axis, dim in sides:
        count = lax.axis_size(axis)
        ends = count - 1
        head = lax.slice_in_dim(cells, 0, width, axis=dim)
        tail = lax.slice_in_dim(cells, cells.shape[dim] - width, cells.shape[dim], axis=dim)
        cells = jnp.concatenate(
            [
                lax.ppermute(tail, axis, [(i, (i + 1) % count) for i in range(ends)]),
                cells,
                lax.ppermute(head, axis, [((i + 1) % count, i) for i in range(ends)]),
            ],
            axis=dim,
        )
    return cells


def fourier_table(wave_order, length):
    points = jnp.arange(length, dtype=jnp.int32)
    phase = wave_order[:, None] * points[None, :] % length
    angle = phase.astype(jnp.float32) * (FULL_TURN / length)
    table = jnp.concatenate([jnp.cos(angle), -jnp.sin(angle)], axis=0).astype(jnp.bfloat16)
    return (table, points)


def lev_sum(values):
    count = lax.axis_size("lev")
    if count & (count - 1):
        return lax.psum(values, "lev")
    stride = 1
    while stride < count:
        values = values + lax.ppermute(values, "lev", [(i, i ^ stride) for i in range(count)])
        stride *= 2
    return values


def lev_gather(values, axis):
    count = lax.axis_size("lev")
    if count & (count - 1):
        return lax.all_gather(values, "lev", axis=axis, tiled=True)
    index = lax.axis_index("lev")
    stride = 1
    while stride < count:
        other = lax.ppermute(values, "lev", [(i, i ^ stride) for i in range(count)])
        upper = (index // stride) % 2 == 1
        values = jnp.where(
            upper,
            jnp.concatenate([other, values], axis=axis),
            jnp.concatenate([values, other], axis=axis),
        )
        stride *= 2
    return values


def row_block(rows):
    for size in (64, 32, 16):
        if rows % size == 0:
            return size
    return rows


def transform_kernel(
    points_ref, cells_ref, table_ref, weight_ref, slot_ref, sums_ref, acc_ref, masked_ref, stacked_ref, onehot_ref
):
    step = pl.program_id(0)

    @pl.when(step == 0)
    def _():
        acc_ref[...] = jnp.zeros_like(acc_ref)

    nfields, nlev, rows, lon_count = cells_ref.shape
    nslot = acc_ref.shape[0]
    nblocks = lon_count // BLOCK
    limit = points_ref[...]

    def per_block(b, carry):
        start = pl.multiple_of(b * BLOCK, BLOCK)
        inside = lax.broadcasted_iota(jnp.int32, (rows, BLOCK), 1) + start < limit
        row0 = pl.multiple_of(b * rows, rows)
        for f in range(nfields):
            flux = None
            for l in range(nlev):
                kept = jnp.where(inside, cells_ref[f, l, :, pl.ds(start, BLOCK)], jnp.zeros((), jnp.bfloat16))
                masked_ref[f, l, :, pl.ds(start, BLOCK)] = kept
                term = weight_ref[f, l] * kept.astype(jnp.float32)
                flux = term if flux is None else flux + term
            high = flux.astype(jnp.bfloat16)
            low = flux - high.astype(jnp.float32)
            stacked_ref[pl.ds(row0, rows), 2 * f * BLOCK : (2 * f + 1) * BLOCK] = high.astype(stacked_ref.dtype)
            stacked_ref[pl.ds(row0, rows), (2 * f + 1) * BLOCK : (2 * f + 2) * BLOCK] = low.astype(
                stacked_ref.dtype
            )
        return carry

    lax.fori_loop(0, nblocks, per_block, 0)

    kdim = nblocks * rows
    chunk = BLOCK if kdim % BLOCK == 0 else kdim

    def per_chunk(c, carry):
        c0 = pl.multiple_of(c * chunk, chunk)
        ids = slot_ref[0, :, pl.ds(c0, chunk)]
        onehot_ref[:, pl.ds(c0, chunk)] = (
            lax.broadcasted_iota(jnp.int32, (nslot, chunk), 0) == ids
        ).astype(jnp.bfloat16)
        return carry

    lax.fori_loop(0, kdim // chunk, per_chunk, 0)

    table = table_ref[...]
    if rows % 16 == 0:
        sums = lax.dot_general(
            masked_ref[...].reshape(nfields * nlev * rows, lon_count),
            table,
            (((1,), (1,)), ((), ())),
            preferred_element_type=jnp.float32,
        )
        sums_ref[...] = sums.reshape(sums_ref.shape)
    else:
        for f in range(nfields):
            for l in range(nlev):
                sums_ref[f, l] = lax.dot_general(
                    masked_ref[f, l], table, (((1,), (1,)), ((), ())), preferred_element_type=jnp.float32
                )
    acc_ref[...] += jnp.dot(
        onehot_ref[...], stacked_ref[...].astype(jnp.bfloat16), preferred_element_type=jnp.float32
    )


def fused_transform(atmos_fields, lat_points, table, column_weight, slots, nslot):
    nfields, nlev, lat_band, lon_count = atmos_fields.shape
    rows = row_block(lat_band)
    steps = lat_band // rows
    nblocks = lon_count // BLOCK
    wave2 = table.shape[0]
    slot_rows = slots.reshape(steps, rows, nblocks).transpose(0, 2, 1).reshape(steps, 1, nblocks * rows)
    stacked_type = jnp.bfloat16 if rows % 16 == 0 else jnp.float32
    return pl.pallas_call(
        transform_kernel,
        grid=(steps,),
        in_specs=[
            pl.BlockSpec((rows, 1), lambda r: (r, 0)),
            pl.BlockSpec((nfields, nlev, rows, lon_count), lambda r: (0, 0, r, 0)),
            pl.BlockSpec((wave2, lon_count), lambda r: (0, 0)),
            pl.BlockSpec(memory_space=pltpu.SMEM),
            pl.BlockSpec((1, 1, nblocks * rows), lambda r: (r, 0, 0)),
        ],
        out_specs=[
            pl.BlockSpec((nfields, nlev, rows, wave2), lambda r: (0, 0, r, 0)),
            pl.BlockSpec((nslot, 2 * nfields * BLOCK), lambda r: (0, 0)),
        ],
        out_shape=[
            jax.ShapeDtypeStruct((nfields, nlev, lat_band, wave2), jnp.float32),
            jax.ShapeDtypeStruct((nslot, 2 * nfields * BLOCK), jnp.float32),
        ],
        scratch_shapes=[
            pltpu.VMEM((nfields, nlev, rows, lon_count), jnp.bfloat16),
            pltpu.VMEM((nblocks * rows, 2 * nfields * BLOCK), stacked_type),
            pltpu.VMEM((nslot, nblocks * rows), jnp.bfloat16),
        ],
        compiler_params=pltpu.CompilerParams(dimension_semantics=("arbitrary",)),
    )(lat_points[:, None], atmos_fields, table, column_weight.astype(jnp.float32), slot_rows)


def body(
    atmos_fields,
    lat_points,
    wave_order,
    legendre,
    column_weight,
    block_remap,
    ocean_temp,
    ocean_salt,
    sea_mask,
):
    nfields, lev_dev, lat_band, lon_count = atmos_fields.shape
    wave_count = wave_order.shape[0]
    table, points = fourier_table(wave_order, lon_count)
    inverse_root = 1.0 / jnp.sqrt(lat_points.astype(jnp.float32))
    weights = jnp.where(
        2 * wave_order[None, :] < lat_points[:, None],
        inverse_root[:, None],
        jnp.zeros((), jnp.float32),
    )
    field_count = nfields
    ocean_rows, ocean_cols = ocean_temp.shape
    tile_count = ocean_rows * ocean_cols // BLOCK
    band_index = lax.axis_index(("lat", "ocn"))

    def slot_of(targets):
        return (targets // tile_count - band_index + 1) * tile_count + targets % tile_count

    local_slot = slot_of(block_remap.reshape(-1))
    quarter = lon_count // lax.axis_size("lev")
    full_remap = lev_gather(block_remap, 1)
    every_slot = slot_of(full_remap)
    raw_sums, split_sums = fused_transform(
        atmos_fields, lat_points, table, column_weight, every_slot, 3 * tile_count
    )
    raw_sums = raw_sums.reshape(field_count, lev_dev, lat_band, 2, wave_count)
    coeffs = (raw_sums * weights[None, None, :, None, :]).astype(jnp.bfloat16)
    regrouped = lax.all_to_all(
        coeffs.transpose(4, 1, 0, 3, 2).reshape(wave_count, lev_dev * field_count * 2, lat_band),
        ("lat", "ocn"),
        split_axis=0,
        concat_axis=2,
        tiled=True,
    )
    spectra = jnp.einsum(
        "srj,sjd->srd",
        lev_gather(regrouped, 1),
        legendre,
        preferred_element_type=jnp.float32,
    )
    split_sums = split_sums.reshape(3 * tile_count, FIELDS, 2, BLOCK)
    outgoing = (split_sums[:, :, 0] + split_sums[:, :, 1]).reshape(3 * tile_count, FIELDS * BLOCK)
    widened = with_halo(outgoing, ((("lat", "ocn"), 0),), tile_count)
    arrived = (
        widened[:tile_count] + widened[2 * tile_count : 3 * tile_count] + widened[4 * tile_count :]
    )
    tile_sums = lev_sum(arrived)
    forcing = (
        tile_sums.reshape(ocean_rows, ocean_cols // BLOCK, FIELDS, BLOCK)
        .transpose(2, 0, 1, 3)
        .reshape(FIELDS, ocean_rows, ocean_cols)
    )
    sea_cells = (
        jnp.broadcast_to(sea_mask[:, :, None], (ocean_rows, ocean_cols // BLOCK, BLOCK))
        .reshape(ocean_rows, ocean_cols)
        .astype(jnp.float32)
    )
    ocean_state = jnp.stack([ocean_temp, ocean_salt])
    padded = with_halo(ocean_state, ((("lat", "ocn"), 1),), 1)
    laplace = (
        padded[:, 2:]
        + padded[:, :-2]
        + jnp.roll(ocean_state, 1, 2)
        + jnp.roll(ocean_state, -1, 2)
        - 4.0 * ocean_state
    )
    updated = ocean_state + DIFFUSION * laplace + COUPLING * sea_cells[None] * forcing
    temp_next = updated[0]
    salt_next = updated[1]
    returned = with_halo(temp_next, ((("lat", "ocn"), 0),), ocean_rows)
    tiles_near = returned.reshape(3 * tile_count, BLOCK)
    surface = jnp.take(tiles_near, local_slot, axis=0).reshape(lat_band, quarter)
    own_points = lax.axis_index("lev") * quarter + jnp.arange(quarter, dtype=jnp.int32)
    surface_temp = jnp.where(
        own_points[None, :] < lat_points[:, None], surface, jnp.zeros((), jnp.float32)
    )
    return (spectra, temp_next, salt_next, surface_temp)


def solution(mesh):
    placed = (
        P(None, "lev", ("lat", "ocn"), None),
        P(("lat", "ocn")),
        P(),
        P(("lat", "ocn"), None, "lev"),
        P(None, "lev"),
        P(("lat", "ocn"), "lev"),
        P(("lat", "ocn"), None),
        P(("lat", "ocn"), None),
        P(("lat", "ocn"), None),
    )
    return jax.shard_map(
        body,
        mesh=mesh,
        in_specs=placed,
        out_specs=(
            P(("lat", "ocn"), None, "lev"),
            P(("lat", "ocn"), None),
            P(("lat", "ocn"), None),
            P(("lat", "ocn"), "lev"),
        ),
        check_vma=False,
    )
```

```python
import math

import jax
import jax.numpy as jnp
from jax import lax
from jax.experimental import pallas as pl
from jax.experimental.pallas import tpu as pltpu
from jax.sharding import PartitionSpec as P

FIELDS = 2
BLOCK = 128


FULL_TURN = 2.0 * math.pi
DIFFUSION = 0.2
COUPLING = 0.5


def with_halo(cells, sides, width):
    for axis, dim in sides:
        count = lax.axis_size(axis)
        ends = count - 1
        head = lax.slice_in_dim(cells, 0, width, axis=dim)
        tail = lax.slice_in_dim(cells, cells.shape[dim] - width, cells.shape[dim], axis=dim)
        cells = jnp.concatenate(
            [
                lax.ppermute(tail, axis, [(i, (i + 1) % count) for i in range(ends)]),
                cells,
                lax.ppermute(head, axis, [((i + 1) % count, i) for i in range(ends)]),
            ],
            axis=dim,
        )
    return cells


def fourier_table(wave_order, length):
    points = jnp.arange(length, dtype=jnp.int32)
    phase = wave_order[:, None] * points[None, :] % length
    angle = phase.astype(jnp.float32) * (FULL_TURN / length)
    table = jnp.concatenate([jnp.cos(angle), -jnp.sin(angle)], axis=0).astype(jnp.bfloat16)
    return (table, points)


def lev_sum(values):
    count = lax.axis_size("lev")
    if count & (count - 1):
        return lax.psum(values, "lev")
    stride = 1
    while stride < count:
        values = values + lax.ppermute(values, "lev", [(i, i ^ stride) for i in range(count)])
        stride *= 2
    return values


def lev_gather(values, axis):
    count = lax.axis_size("lev")
    if count & (count - 1):
        return lax.all_gather(values, "lev", axis=axis, tiled=True)
    index = lax.axis_index("lev")
    stride = 1
    while stride < count:
        other = lax.ppermute(values, "lev", [(i, i ^ stride) for i in range(count)])
        upper = (index // stride) % 2 == 1
        values = jnp.where(
            upper,
            jnp.concatenate([other, values], axis=axis),
            jnp.concatenate([values, other], axis=axis),
        )
        stride *= 2
    return values


def row_block(rows):
    for size in (64, 32, 16):
        if rows % size == 0:
            return size
    return rows


def transform_kernel(points_ref, cells_ref, table_ref, weight_ref, slot_ref, sums_ref, acc_ref, *scratch):
    step = pl.program_id(0)

    @pl.when(step == 0)
    def _():
        acc_ref[...] = jnp.zeros_like(acc_ref)

    nfields, nlev, rows, lon_count = cells_ref.shape
    nslot = acc_ref.shape[0]
    nblocks = lon_count // BLOCK
    table = table_ref[...]
    keep = (lax.broadcasted_iota(jnp.int32, (rows, lon_count), 1) < points_ref[...]).astype(jnp.bfloat16)
    cells = cells_ref[...] * keep[None, None]
    if rows % 16 == 0:
        sums = lax.dot_general(
            cells.reshape(nfields * nlev * rows, lon_count),
            table,
            (((1,), (1,)), ((), ())),
            preferred_element_type=jnp.float32,
        )
        sums_ref[...] = sums.reshape(sums_ref.shape)
    else:
        for f in range(nfields):
            for l in range(nlev):
                sums_ref[f, l] = lax.dot_general(
                    cells[f, l], table, (((1,), (1,)), ((), ())), preferred_element_type=jnp.float32
                )
    pieces = []
    for f in range(nfields):
        flux = weight_ref[f, 0] * cells[f, 0].astype(jnp.float32)
        for l in range(1, nlev):
            flux = flux + weight_ref[f, l] * cells[f, l].astype(jnp.float32)
        high = flux.astype(jnp.bfloat16)
        pieces.append(high)
        pieces.append((flux - high.astype(jnp.float32)).astype(jnp.bfloat16))
    if scratch:
        (stacked_ref,) = scratch
        for b in range(nblocks):
            for p, piece in enumerate(pieces):
                stacked_ref[b * rows : (b + 1) * rows, p * BLOCK : (p + 1) * BLOCK] = piece[
                    :, b * BLOCK : (b + 1) * BLOCK
                ]
        stacked = stacked_ref[...]
    else:
        stacked = jnp.concatenate(
            [
                jnp.concatenate(
                    [p[:, b * BLOCK : (b + 1) * BLOCK].astype(jnp.float32) for p in pieces], axis=1
                )
                for b in range(nblocks)
            ],
            axis=0,
        ).astype(jnp.bfloat16)
    onehot = (
        lax.broadcasted_iota(jnp.int32, (nslot, nblocks * rows), 0) == slot_ref[0]
    ).astype(jnp.bfloat16)
    acc_ref[...] += jnp.dot(onehot, stacked, preferred_element_type=jnp.float32)


def fused_transform(atmos_fields, lat_points, table, column_weight, slots, nslot):
    nfields, nlev, lat_band, lon_count = atmos_fields.shape
    rows = row_block(lat_band)
    steps = lat_band // rows
    nblocks = lon_count // BLOCK
    wave2 = table.shape[0]
    slot_rows = slots.reshape(steps, rows, nblocks).transpose(0, 2, 1).reshape(steps, 1, nblocks * rows)
    scratch = []
    if rows % 16 == 0 and True:
        scratch = [pltpu.VMEM((nblocks * rows, 2 * nfields * BLOCK), jnp.bfloat16)]
    return pl.pallas_call(
        transform_kernel,
        grid=(steps,),
        in_specs=[
            pl.BlockSpec((rows, 1), lambda r: (r, 0)),
            pl.BlockSpec((nfields, nlev, rows, lon_count), lambda r: (0, 0, r, 0)),
            pl.BlockSpec((wave2, lon_count), lambda r: (0, 0)),
            pl.BlockSpec(memory_space=pltpu.SMEM),
            pl.BlockSpec((1, 1, nblocks * rows), lambda r: (r, 0, 0)),
        ],
        out_specs=[
            pl.BlockSpec((nfields, nlev, rows, wave2), lambda r: (0, 0, r, 0)),
            pl.BlockSpec((nslot, 2 * nfields * BLOCK), lambda r: (0, 0)),
        ],
        out_shape=[
            jax.ShapeDtypeStruct((nfields, nlev, lat_band, wave2), jnp.float32),
            jax.ShapeDtypeStruct((nslot, 2 * nfields * BLOCK), jnp.float32),
        ],
        scratch_shapes=scratch,
        compiler_params=pltpu.CompilerParams(dimension_semantics=("arbitrary",)),
    )(lat_points[:, None], atmos_fields, table, column_weight.astype(jnp.float32), slot_rows)


def body(
    atmos_fields,
    lat_points,
    wave_order,
    legendre,
    column_weight,
    block_remap,
    ocean_temp,
    ocean_salt,
    sea_mask,
):
    nfields, lev_dev, lat_band, lon_count = atmos_fields.shape
    wave_count = wave_order.shape[0]
    table, points = fourier_table(wave_order, lon_count)
    inverse_root = 1.0 / jnp.sqrt(lat_points.astype(jnp.float32))
    weights = jnp.where(
        2 * wave_order[None, :] < lat_points[:, None],
        inverse_root[:, None],
        jnp.zeros((), jnp.float32),
    )
    field_count = nfields
    ocean_rows, ocean_cols = ocean_temp.shape
    tile_count = ocean_rows * ocean_cols // BLOCK
    band_index = lax.axis_index(("lat", "ocn"))

    def slot_of(targets):
        return (targets // tile_count - band_index + 1) * tile_count + targets % tile_count

    local_slot = slot_of(block_remap.reshape(-1))
    quarter = lon_count // lax.axis_size("lev")
    full_remap = lev_gather(block_remap, 1)
    every_slot = slot_of(full_remap)
    raw_sums, split_sums = fused_transform(
        atmos_fields, lat_points, table, column_weight, every_slot, 3 * tile_count
    )
    raw_sums = raw_sums.reshape(field_count, lev_dev, lat_band, 2, wave_count)
    coeffs = (raw_sums * weights[None, None, :, None, :]).astype(jnp.bfloat16)
    regrouped = lax.all_to_all(
        coeffs.transpose(4, 1, 0, 3, 2).reshape(wave_count, lev_dev * field_count * 2, lat_band),
        ("lat", "ocn"),
        split_axis=0,
        concat_axis=2,
        tiled=True,
    )
    spectra = jnp.einsum(
        "srj,sjd->srd",
        lev_gather(regrouped, 1),
        legendre,
        preferred_element_type=jnp.float32,
    )
    split_sums = split_sums.reshape(3 * tile_count, FIELDS, 2, BLOCK)
    outgoing = (split_sums[:, :, 0] + split_sums[:, :, 1]).reshape(3 * tile_count, FIELDS * BLOCK)
    widened = with_halo(outgoing, ((("lat", "ocn"), 0),), tile_count)
    arrived = (
        widened[:tile_count] + widened[2 * tile_count : 3 * tile_count] + widened[4 * tile_count :]
    )
    tile_sums = lev_sum(arrived)
    forcing = (
        tile_sums.reshape(ocean_rows, ocean_cols // BLOCK, FIELDS, BLOCK)
        .transpose(2, 0, 1, 3)
        .reshape(FIELDS, ocean_rows, ocean_cols)
    )
    sea_cells = (
        jnp.broadcast_to(sea_mask[:, :, None], (ocean_rows, ocean_cols // BLOCK, BLOCK))
        .reshape(ocean_rows, ocean_cols)
        .astype(jnp.float32)
    )
    ocean_state = jnp.stack([ocean_temp, ocean_salt])
    padded = with_halo(ocean_state, ((("lat", "ocn"), 1),), 1)
    laplace = (
        padded[:, 2:]
        + padded[:, :-2]
        + jnp.roll(ocean_state, 1, 2)
        + jnp.roll(ocean_state, -1, 2)
        - 4.0 * ocean_state
    )
    updated = ocean_state + DIFFUSION * laplace + COUPLING * sea_cells[None] * forcing
    temp_next = updated[0]
    salt_next = updated[1]
    returned = with_halo(temp_next, ((("lat", "ocn"), 0),), ocean_rows)
    tiles_near = returned.reshape(3 * tile_count, BLOCK)
    surface = jnp.take(tiles_near, local_slot, axis=0).reshape(lat_band, quarter)
    own_points = lax.axis_index("lev") * quarter + jnp.arange(quarter, dtype=jnp.int32)
    surface_temp = jnp.where(
        own_points[None, :] < lat_points[:, None], surface, jnp.zeros((), jnp.float32)
    )
    return (spectra, temp_next, salt_next, surface_temp)


def solution(mesh):
    placed = (
        P(None, "lev", ("lat", "ocn"), None),
        P(("lat", "ocn")),
        P(),
        P(("lat", "ocn"), None, "lev"),
        P(None, "lev"),
        P(("lat", "ocn"), "lev"),
        P(("lat", "ocn"), None),
        P(("lat", "ocn"), None),
        P(("lat", "ocn"), None),
    )
    return jax.shard_map(
        body,
        mesh=mesh,
        in_specs=placed,
        out_specs=(
            P(("lat", "ocn"), None, "lev"),
            P(("lat", "ocn"), None),
            P(("lat", "ocn"), None),
            P(("lat", "ocn"), "lev"),
        ),
        check_vma=False,
    )
```

```python
import math

import jax
import jax.numpy as jnp
from jax import lax
from jax.experimental import pallas as pl
from jax.experimental.pallas import tpu as pltpu
from jax.sharding import PartitionSpec as P

FIELDS = 2
BLOCK = 128


FULL_TURN = 2.0 * math.pi
DIFFUSION = 0.2
COUPLING = 0.5


def with_halo(cells, sides, width):
    for axis, dim in sides:
        count = lax.axis_size(axis)
        ends = count - 1
        head = lax.slice_in_dim(cells, 0, width, axis=dim)
        tail = lax.slice_in_dim(cells, cells.shape[dim] - width, cells.shape[dim], axis=dim)
        cells = jnp.concatenate(
            [
                lax.ppermute(tail, axis, [(i, (i + 1) % count) for i in range(ends)]),
                cells,
                lax.ppermute(head, axis, [((i + 1) % count, i) for i in range(ends)]),
            ],
            axis=dim,
        )
    return cells


def fourier_table(wave_order, length):
    points = jnp.arange(length, dtype=jnp.int32)
    phase = wave_order[:, None] * points[None, :] % length
    angle = phase.astype(jnp.float32) * (FULL_TURN / length)
    table = jnp.concatenate([jnp.cos(angle), -jnp.sin(angle)], axis=0).astype(jnp.bfloat16)
    return (table, points)


def lev_sum(values):
    count = lax.axis_size("lev")
    if count & (count - 1):
        return lax.psum(values, "lev")
    stride = 1
    while stride < count:
        values = values + lax.ppermute(values, "lev", [(i, i ^ stride) for i in range(count)])
        stride *= 2
    return values


def lev_gather(values, axis):
    count = lax.axis_size("lev")
    if count & (count - 1):
        return lax.all_gather(values, "lev", axis=axis, tiled=True)
    index = lax.axis_index("lev")
    stride = 1
    while stride < count:
        other = lax.ppermute(values, "lev", [(i, i ^ stride) for i in range(count)])
        upper = (index // stride) % 2 == 1
        values = jnp.where(
            upper,
            jnp.concatenate([other, values], axis=axis),
            jnp.concatenate([values, other], axis=axis),
        )
        stride *= 2
    return values


def row_block(rows):
    for size in (64, 32, 16):
        if rows % size == 0:
            return size
    return rows


def transform_kernel(points_ref, cells_ref, table_ref, weight_ref, slot_ref, sums_ref, out_ref, acc_ref, *scratch):
    step = pl.program_id(0)

    @pl.when(step == 0)
    def _():
        acc_ref[...] = jnp.zeros_like(acc_ref)

    nfields, nlev, rows, lon_count = cells_ref.shape
    nslot = acc_ref.shape[0]
    nblocks = lon_count // BLOCK
    table = table_ref[...]
    keep = (lax.broadcasted_iota(jnp.int32, (rows, lon_count), 1) < points_ref[...]).astype(jnp.bfloat16)
    cells = cells_ref[...] * keep[None, None]
    if rows % 16 == 0:
        sums = lax.dot_general(
            cells.reshape(nfields * nlev * rows, lon_count),
            table,
            (((1,), (1,)), ((), ())),
            preferred_element_type=jnp.float32,
        )
        sums_ref[...] = sums.reshape(sums_ref.shape)
    else:
        for f in range(nfields):
            for l in range(nlev):
                sums_ref[f, l] = lax.dot_general(
                    cells[f, l], table, (((1,), (1,)), ((), ())), preferred_element_type=jnp.float32
                )
    pieces = []
    for f in range(nfields):
        flux = weight_ref[f, 0] * cells[f, 0].astype(jnp.float32)
        for l in range(1, nlev):
            flux = flux + weight_ref[f, l] * cells[f, l].astype(jnp.float32)
        high = flux.astype(jnp.bfloat16)
        pieces.append(high)
        pieces.append((flux - high.astype(jnp.float32)).astype(jnp.bfloat16))
    if scratch:
        (stacked_ref,) = scratch
        for b in range(nblocks):
            for p, piece in enumerate(pieces):
                stacked_ref[b * rows : (b + 1) * rows, p * BLOCK : (p + 1) * BLOCK] = piece[
                    :, b * BLOCK : (b + 1) * BLOCK
                ]
        stacked = stacked_ref[...]
    else:
        stacked = jnp.concatenate(
            [
                jnp.concatenate(
                    [p[:, b * BLOCK : (b + 1) * BLOCK].astype(jnp.float32) for p in pieces], axis=1
                )
                for b in range(nblocks)
            ],
            axis=0,
        ).astype(jnp.bfloat16)
    onehot = (
        lax.broadcasted_iota(jnp.int32, (nslot, nblocks * rows), 0) == slot_ref[0]
    ).astype(jnp.bfloat16)
    acc_ref[...] += jnp.dot(onehot, stacked, preferred_element_type=jnp.float32)

    @pl.when(step == pl.num_programs(0) - 1)
    def _():
        nsec, tiles, _ = out_ref.shape
        for s in range(nsec):
            for f in range(nfields):
                high = acc_ref[s * tiles : (s + 1) * tiles, 2 * f * BLOCK : (2 * f + 1) * BLOCK]
                low = acc_ref[s * tiles : (s + 1) * tiles, (2 * f + 1) * BLOCK : (2 * f + 2) * BLOCK]
                out_ref[s, :, f * BLOCK : (f + 1) * BLOCK] = high + low


def fused_transform(atmos_fields, lat_points, table, column_weight, slots, nslot):
    nfields, nlev, lat_band, lon_count = atmos_fields.shape
    rows = row_block(lat_band)
    steps = lat_band // rows
    nblocks = lon_count // BLOCK
    wave2 = table.shape[0]
    slot_rows = slots.reshape(steps, rows, nblocks).transpose(0, 2, 1).reshape(steps, 1, nblocks * rows)
    scratch = [pltpu.VMEM((nslot, 2 * nfields * BLOCK), jnp.float32)]
    if rows % 16 == 0:
        scratch.append(pltpu.VMEM((nblocks * rows, 2 * nfields * BLOCK), jnp.bfloat16))
    return pl.pallas_call(
        transform_kernel,
        grid=(steps,),
        in_specs=[
            pl.BlockSpec((rows, 1), lambda r: (r, 0)),
            pl.BlockSpec((nfields, nlev, rows, lon_count), lambda r: (0, 0, r, 0)),
            pl.BlockSpec((wave2, lon_count), lambda r: (0, 0)),
            pl.BlockSpec(memory_space=pltpu.SMEM),
            pl.BlockSpec((1, 1, nblocks * rows), lambda r: (r, 0, 0)),
        ],
        out_specs=[
            pl.BlockSpec((nfields, nlev, rows, wave2), lambda r: (0, 0, r, 0)),
            pl.BlockSpec((3, nslot // 3, nfields * BLOCK), lambda r: (0, 0, 0)),
        ],
        out_shape=[
            jax.ShapeDtypeStruct((nfields, nlev, lat_band, wave2), jnp.float32),
            jax.ShapeDtypeStruct((3, nslot // 3, nfields * BLOCK), jnp.float32),
        ],
        scratch_shapes=scratch,
        compiler_params=pltpu.CompilerParams(dimension_semantics=("arbitrary",)),
    )(lat_points[:, None], atmos_fields, table, column_weight.astype(jnp.float32), slot_rows)


def body(
    atmos_fields,
    lat_points,
    wave_order,
    legendre,
    column_weight,
    block_remap,
    ocean_temp,
    ocean_salt,
    sea_mask,
):
    nfields, lev_dev, lat_band, lon_count = atmos_fields.shape
    wave_count = wave_order.shape[0]
    table, points = fourier_table(wave_order, lon_count)
    inverse_root = 1.0 / jnp.sqrt(lat_points.astype(jnp.float32))
    weights = jnp.where(
        2 * wave_order[None, :] < lat_points[:, None],
        inverse_root[:, None],
        jnp.zeros((), jnp.float32),
    )
    field_count = nfields
    ocean_rows, ocean_cols = ocean_temp.shape
    tile_count = ocean_rows * ocean_cols // BLOCK
    band_index = lax.axis_index(("lat", "ocn"))

    def slot_of(targets):
        return (targets // tile_count - band_index + 1) * tile_count + targets % tile_count

    local_slot = slot_of(block_remap.T.reshape(-1))
    quarter = lon_count // lax.axis_size("lev")
    full_remap = lev_gather(block_remap, 1)
    every_slot = slot_of(full_remap)
    raw_sums, sections = fused_transform(
        atmos_fields, lat_points, table, column_weight, every_slot, 3 * tile_count
    )
    raw_sums = raw_sums.reshape(field_count, lev_dev, lat_band, 2, wave_count)
    coeffs = (raw_sums * weights[None, None, :, None, :]).astype(jnp.bfloat16)
    regrouped = lax.all_to_all(
        coeffs.transpose(4, 1, 0, 3, 2).reshape(wave_count, lev_dev * field_count * 2, lat_band),
        ("lat", "ocn"),
        split_axis=0,
        concat_axis=2,
        tiled=True,
    )
    spectra = jnp.einsum(
        "srj,sjd->srd",
        lev_gather(regrouped, 1),
        legendre,
        preferred_element_type=jnp.float32,
    )
    band_count = lax.axis_size(("lat", "ocn"))
    from_prev = lax.ppermute(
        sections[2], ("lat", "ocn"), [(i, i + 1) for i in range(band_count - 1)]
    )
    from_next = lax.ppermute(
        sections[0], ("lat", "ocn"), [(i + 1, i) for i in range(band_count - 1)]
    )
    arrived = (from_prev + sections[1]) + from_next
    tile_sums = lev_sum(arrived)
    forcing = (
        tile_sums.reshape(ocean_rows, ocean_cols // BLOCK, FIELDS, BLOCK)
        .transpose(2, 0, 1, 3)
        .reshape(FIELDS, ocean_rows, ocean_cols)
    )
    sea_cells = (
        jnp.broadcast_to(sea_mask[:, :, None], (ocean_rows, ocean_cols // BLOCK, BLOCK))
        .reshape(ocean_rows, ocean_cols)
        .astype(jnp.float32)
    )
    ocean_state = jnp.stack([ocean_temp, ocean_salt])
    padded = with_halo(ocean_state, ((("lat", "ocn"), 1),), 1)
    laplace = (
        padded[:, 2:]
        + padded[:, :-2]
        + jnp.roll(ocean_state, 1, 2)
        + jnp.roll(ocean_state, -1, 2)
        - 4.0 * ocean_state
    )
    updated = ocean_state + DIFFUSION * laplace + COUPLING * sea_cells[None] * forcing
    temp_next = updated[0]
    salt_next = updated[1]
    returned = with_halo(temp_next, ((("lat", "ocn"), 0),), ocean_rows)
    tiles_near = returned.reshape(3 * tile_count, BLOCK)
    nquarter = quarter // BLOCK
    gathered = jnp.take(tiles_near, local_slot, axis=0).reshape(nquarter, lat_band, BLOCK)
    own_points = (
        lax.axis_index("lev") * quarter
        + lax.broadcasted_iota(jnp.int32, (nquarter, 1, BLOCK), 0) * BLOCK
        + lax.broadcasted_iota(jnp.int32, (nquarter, 1, BLOCK), 2)
    )
    kept = jnp.where(
        own_points < lat_points[None, :, None], gathered, jnp.zeros((), jnp.float32)
    )
    surface_temp = kept.transpose(1, 0, 2).reshape(lat_band, quarter)
    return (spectra, temp_next, salt_next, surface_temp)


def solution(mesh):
    placed = (
        P(None, "lev", ("lat", "ocn"), None),
        P(("lat", "ocn")),
        P(),
        P(("lat", "ocn"), None, "lev"),
        P(None, "lev"),
        P(("lat", "ocn"), "lev"),
        P(("lat", "ocn"), None),
        P(("lat", "ocn"), None),
        P(("lat", "ocn"), None),
    )
    return jax.shard_map(
        body,
        mesh=mesh,
        in_specs=placed,
        out_specs=(
            P(("lat", "ocn"), None, "lev"),
            P(("lat", "ocn"), None),
            P(("lat", "ocn"), None),
            P(("lat", "ocn"), "lev"),
        ),
        check_vma=False,
    )
```

```python
import math

import jax
import jax.numpy as jnp
from jax import lax
from jax.experimental import pallas as pl
from jax.experimental.pallas import tpu as pltpu
from jax.sharding import PartitionSpec as P

FIELDS = 2
BLOCK = 128


FULL_TURN = 2.0 * math.pi
DIFFUSION = 0.2
COUPLING = 0.5


def with_halo(cells, sides, width):
    for axis, dim in sides:
        count = lax.axis_size(axis)
        ends = count - 1
        head = lax.slice_in_dim(cells, 0, width, axis=dim)
        tail = lax.slice_in_dim(cells, cells.shape[dim] - width, cells.shape[dim], axis=dim)
        cells = jnp.concatenate(
            [
                lax.ppermute(tail, axis, [(i, (i + 1) % count) for i in range(ends)]),
                cells,
                lax.ppermute(head, axis, [((i + 1) % count, i) for i in range(ends)]),
            ],
            axis=dim,
        )
    return cells


def fourier_table(wave_order, length):
    points = jnp.arange(length, dtype=jnp.int32)
    phase = wave_order[:, None] * points[None, :] % length
    angle = phase.astype(jnp.float32) * (FULL_TURN / length)
    table = jnp.concatenate([jnp.cos(angle), -jnp.sin(angle)], axis=0).astype(jnp.bfloat16)
    return (table, points)


def lev_sum(values):
    count = lax.axis_size("lev")
    if count & (count - 1):
        return lax.psum(values, "lev")
    stride = 1
    while stride < count:
        values = values + lax.ppermute(values, "lev", [(i, i ^ stride) for i in range(count)])
        stride *= 2
    return values


def lev_gather(values, axis):
    count = lax.axis_size("lev")
    if count & (count - 1):
        return lax.all_gather(values, "lev", axis=axis, tiled=True)
    index = lax.axis_index("lev")
    stride = 1
    while stride < count:
        other = lax.ppermute(values, "lev", [(i, i ^ stride) for i in range(count)])
        upper = (index // stride) % 2 == 1
        values = jnp.where(
            upper,
            jnp.concatenate([other, values], axis=axis),
            jnp.concatenate([values, other], axis=axis),
        )
        stride *= 2
    return values


def row_block(rows):
    for size in (64, 32, 16):
        if rows % size == 0:
            return size
    return rows


def transform_kernel(points_ref, cells_ref, table_ref, weight_ref, slot_ref, sums_ref, out_ref, acc_ref, *scratch):
    step = pl.program_id(0)

    @pl.when(step == 0)
    def _():
        acc_ref[...] = jnp.zeros_like(acc_ref)

    nfields, nlev, rows, lon_count = cells_ref.shape
    nslot = acc_ref.shape[0]
    nblocks = lon_count // BLOCK
    table = table_ref[...]
    keep = (lax.broadcasted_iota(jnp.int32, (rows, lon_count), 1) < points_ref[...]).astype(jnp.bfloat16)
    cells = cells_ref[...] * keep[None, None]
    if rows % 16 == 0:
        sums = lax.dot_general(
            cells.reshape(nfields * nlev * rows, lon_count),
            table,
            (((1,), (1,)), ((), ())),
            preferred_element_type=jnp.float32,
        )
        sums_ref[...] = sums.reshape(sums_ref.shape)
    else:
        for f in range(nfields):
            for l in range(nlev):
                sums_ref[f, l] = lax.dot_general(
                    cells[f, l], table, (((1,), (1,)), ((), ())), preferred_element_type=jnp.float32
                )
    pieces = []
    for f in range(nfields):
        flux = weight_ref[f, 0] * cells[f, 0].astype(jnp.float32)
        for l in range(1, nlev):
            flux = flux + weight_ref[f, l] * cells[f, l].astype(jnp.float32)
        high = flux.astype(jnp.bfloat16)
        pieces.append(high)
        pieces.append((flux - high.astype(jnp.float32)).astype(jnp.bfloat16))
    if scratch:
        (stacked_ref,) = scratch
        for b in range(nblocks):
            for p, piece in enumerate(pieces):
                stacked_ref[b * rows : (b + 1) * rows, p * BLOCK : (p + 1) * BLOCK] = piece[
                    :, b * BLOCK : (b + 1) * BLOCK
                ]
        stacked = stacked_ref[...]
    else:
        stacked = jnp.concatenate(
            [
                jnp.concatenate(
                    [p[:, b * BLOCK : (b + 1) * BLOCK].astype(jnp.float32) for p in pieces], axis=1
                )
                for b in range(nblocks)
            ],
            axis=0,
        ).astype(jnp.bfloat16)
    onehot = (
        lax.broadcasted_iota(jnp.int32, (nslot, nblocks * rows), 0) == slot_ref[0]
    ).astype(jnp.bfloat16)
    acc_ref[...] += jnp.dot(onehot, stacked, preferred_element_type=jnp.float32)

    @pl.when(step == pl.num_programs(0) - 1)
    def _():
        nsec, tiles, _ = out_ref.shape
        for s in range(nsec):
            for f in range(nfields):
                high = acc_ref[s * tiles : (s + 1) * tiles, 2 * f * BLOCK : (2 * f + 1) * BLOCK]
                low = acc_ref[s * tiles : (s + 1) * tiles, (2 * f + 1) * BLOCK : (2 * f + 2) * BLOCK]
                out_ref[s, :, f * BLOCK : (f + 1) * BLOCK] = high + low


def fused_transform(atmos_fields, lat_points, table, column_weight, slots, nslot):
    nfields, nlev, lat_band, lon_count = atmos_fields.shape
    rows = row_block(lat_band)
    steps = lat_band // rows
    nblocks = lon_count // BLOCK
    wave2 = table.shape[0]
    slot_rows = slots.reshape(steps, rows, nblocks).transpose(0, 2, 1).reshape(steps, 1, nblocks * rows)
    scratch = [pltpu.VMEM((nslot, 2 * nfields * BLOCK), jnp.float32)]
    if rows % 16 == 0:
        scratch.append(pltpu.VMEM((nblocks * rows, 2 * nfields * BLOCK), jnp.bfloat16))
    return pl.pallas_call(
        transform_kernel,
        grid=(steps,),
        in_specs=[
            pl.BlockSpec((rows, 1), lambda r: (r, 0)),
            pl.BlockSpec((nfields, nlev, rows, lon_count), lambda r: (0, 0, r, 0)),
            pl.BlockSpec((wave2, lon_count), lambda r: (0, 0)),
            pl.BlockSpec(memory_space=pltpu.SMEM),
            pl.BlockSpec((1, 1, nblocks * rows), lambda r: (r, 0, 0)),
        ],
        out_specs=[
            pl.BlockSpec((nfields, nlev, rows, wave2), lambda r: (0, 0, r, 0)),
            pl.BlockSpec((3, nslot // 3, nfields * BLOCK), lambda r: (0, 0, 0)),
        ],
        out_shape=[
            jax.ShapeDtypeStruct((nfields, nlev, lat_band, wave2), jnp.float32),
            jax.ShapeDtypeStruct((3, nslot // 3, nfields * BLOCK), jnp.float32),
        ],
        scratch_shapes=scratch,
        compiler_params=pltpu.CompilerParams(dimension_semantics=("arbitrary",)),
    )(lat_points[:, None], atmos_fields, table, column_weight.astype(jnp.float32), slot_rows)


def surface_kernel(slot_ref, base_ref, limit_ref, tiles_ref, out_ref):
    lat_band, quarter = out_ref.shape
    nquarter = quarter // BLOCK
    group = 8
    sublane = lax.broadcasted_iota(jnp.int32, (group, BLOCK), 0)

    def per_group(g, carry):
        row0 = pl.multiple_of(g * group, group)
        for b in range(nquarter):
            rows = jnp.zeros((group, BLOCK), jnp.float32)
            for r in range(group):
                tile = slot_ref[(row0 + r) * nquarter + b]
                picked = jnp.broadcast_to(tiles_ref[pl.ds(tile, 1), :], (group, BLOCK))
                rows = jnp.where(sublane == r, picked, rows)
            out_ref[pl.ds(row0, group), b * BLOCK : (b + 1) * BLOCK] = rows
        return carry

    lax.fori_loop(0, lat_band // group, per_group, 0)
    points = base_ref[0] + lax.broadcasted_iota(jnp.int32, (lat_band, quarter), 1)
    out_ref[...] = jnp.where(points < limit_ref[...], out_ref[...], 0.0)


def surface_gather(slots, base, lat_points, tiles, quarter):
    lat_band = lat_points.shape[0]
    return pl.pallas_call(
        surface_kernel,
        in_specs=[
            pl.BlockSpec(memory_space=pltpu.SMEM),
            pl.BlockSpec(memory_space=pltpu.SMEM),
            pl.BlockSpec(memory_space=pltpu.VMEM),
            pl.BlockSpec(memory_space=pltpu.VMEM),
        ],
        out_specs=pl.BlockSpec(memory_space=pltpu.VMEM),
        out_shape=jax.ShapeDtypeStruct((lat_band, quarter), jnp.float32),
    )(slots, base, lat_points[:, None], tiles)


def body(
    atmos_fields,
    lat_points,
    wave_order,
    legendre,
    column_weight,
    block_remap,
    ocean_temp,
    ocean_salt,
    sea_mask,
):
    nfields, lev_dev, lat_band, lon_count = atmos_fields.shape
    wave_count = wave_order.shape[0]
    table, points = fourier_table(wave_order, lon_count)
    inverse_root = 1.0 / jnp.sqrt(lat_points.astype(jnp.float32))
    weights = jnp.where(
        2 * wave_order[None, :] < lat_points[:, None],
        inverse_root[:, None],
        jnp.zeros((), jnp.float32),
    )
    field_count = nfields
    ocean_rows, ocean_cols = ocean_temp.shape
    tile_count = ocean_rows * ocean_cols // BLOCK
    band_index = lax.axis_index(("lat", "ocn"))

    def slot_of(targets):
        return (targets // tile_count - band_index + 1) * tile_count + targets % tile_count

    local_slot = slot_of(block_remap.reshape(-1))
    quarter = lon_count // lax.axis_size("lev")
    full_remap = lev_gather(block_remap, 1)
    every_slot = slot_of(full_remap)
    raw_sums, sections = fused_transform(
        atmos_fields, lat_points, table, column_weight, every_slot, 3 * tile_count
    )
    raw_sums = raw_sums.reshape(field_count, lev_dev, lat_band, 2, wave_count)
    coeffs = (raw_sums * weights[None, None, :, None, :]).astype(jnp.bfloat16)
    regrouped = lax.all_to_all(
        coeffs.transpose(4, 1, 0, 3, 2).reshape(wave_count, lev_dev * field_count * 2, lat_band),
        ("lat", "ocn"),
        split_axis=0,
        concat_axis=2,
        tiled=True,
    )
    spectra = jnp.einsum(
        "srj,sjd->srd",
        lev_gather(regrouped, 1),
        legendre,
        preferred_element_type=jnp.float32,
    )
    band_count = lax.axis_size(("lat", "ocn"))
    from_prev = lax.ppermute(
        sections[2], ("lat", "ocn"), [(i, i + 1) for i in range(band_count - 1)]
    )
    from_next = lax.ppermute(
        sections[0], ("lat", "ocn"), [(i + 1, i) for i in range(band_count - 1)]
    )
    arrived = (from_prev + sections[1]) + from_next
    tile_sums = lev_sum(arrived)
    forcing = (
        tile_sums.reshape(ocean_rows, ocean_cols // BLOCK, FIELDS, BLOCK)
        .transpose(2, 0, 1, 3)
        .reshape(FIELDS, ocean_rows, ocean_cols)
    )
    sea_cells = (
        jnp.broadcast_to(sea_mask[:, :, None], (ocean_rows, ocean_cols // BLOCK, BLOCK))
        .reshape(ocean_rows, ocean_cols)
        .astype(jnp.float32)
    )
    ocean_state = jnp.stack([ocean_temp, ocean_salt])
    padded = with_halo(ocean_state, ((("lat", "ocn"), 1),), 1)
    laplace = (
        padded[:, 2:]
        + padded[:, :-2]
        + jnp.roll(ocean_state, 1, 2)
        + jnp.roll(ocean_state, -1, 2)
        - 4.0 * ocean_state
    )
    updated = ocean_state + DIFFUSION * laplace + COUPLING * sea_cells[None] * forcing
    temp_next = updated[0]
    salt_next = updated[1]
    returned = with_halo(temp_next, ((("lat", "ocn"), 0),), ocean_rows)
    tiles_near = returned.reshape(3 * tile_count, BLOCK)
    base = (lax.axis_index("lev") * quarter).astype(jnp.int32).reshape(1)
    surface_temp = surface_gather(local_slot, base, lat_points, tiles_near, quarter)
    return (spectra, temp_next, salt_next, surface_temp)


def solution(mesh):
    placed = (
        P(None, "lev", ("lat", "ocn"), None),
        P(("lat", "ocn")),
        P(),
        P(("lat", "ocn"), None, "lev"),
        P(None, "lev"),
        P(("lat", "ocn"), "lev"),
        P(("lat", "ocn"), None),
        P(("lat", "ocn"), None),
        P(("lat", "ocn"), None),
    )
    return jax.shard_map(
        body,
        mesh=mesh,
        in_specs=placed,
        out_specs=(
            P(("lat", "ocn"), None, "lev"),
            P(("lat", "ocn"), None),
            P(("lat", "ocn"), None),
            P(("lat", "ocn"), "lev"),
        ),
        check_vma=False,
    )
```

```python
import math

import jax
import jax.numpy as jnp
from jax import lax
from jax.experimental import pallas as pl
from jax.experimental.pallas import tpu as pltpu
from jax.sharding import PartitionSpec as P

FIELDS = 2
BLOCK = 128


FULL_TURN = 2.0 * math.pi
DIFFUSION = 0.2
COUPLING = 0.5


def with_halo(cells, sides, width):
    for axis, dim in sides:
        count = lax.axis_size(axis)
        ends = count - 1
        head = lax.slice_in_dim(cells, 0, width, axis=dim)
        tail = lax.slice_in_dim(cells, cells.shape[dim] - width, cells.shape[dim], axis=dim)
        cells = jnp.concatenate(
            [
                lax.ppermute(tail, axis, [(i, (i + 1) % count) for i in range(ends)]),
                cells,
                lax.ppermute(head, axis, [((i + 1) % count, i) for i in range(ends)]),
            ],
            axis=dim,
        )
    return cells


def fourier_table(wave_order, length):
    points = jnp.arange(length, dtype=jnp.int32)
    phase = wave_order[:, None] * points[None, :] % length
    angle = phase.astype(jnp.float32) * (FULL_TURN / length)
    table = jnp.concatenate([jnp.cos(angle), -jnp.sin(angle)], axis=0).astype(jnp.bfloat16)
    return (table, points)


def lev_sum(values):
    count = lax.axis_size("lev")
    if count & (count - 1):
        return lax.psum(values, "lev")
    stride = 1
    while stride < count:
        values = values + lax.ppermute(values, "lev", [(i, i ^ stride) for i in range(count)])
        stride *= 2
    return values


def lev_gather(values, axis):
    count = lax.axis_size("lev")
    if count & (count - 1):
        return lax.all_gather(values, "lev", axis=axis, tiled=True)
    index = lax.axis_index("lev")
    stride = 1
    while stride < count:
        other = lax.ppermute(values, "lev", [(i, i ^ stride) for i in range(count)])
        upper = (index // stride) % 2 == 1
        values = jnp.where(
            upper,
            jnp.concatenate([other, values], axis=axis),
            jnp.concatenate([values, other], axis=axis),
        )
        stride *= 2
    return values


def spectra_of(regrouped, legendre):
    count = lax.axis_size("lev")
    if count != 4:
        return jnp.einsum(
            "srj,sjd->srd",
            lev_gather(regrouped, 1),
            legendre,
            preferred_element_type=jnp.float32,
        )
    index = lax.axis_index("lev")
    rows = regrouped.shape[1]
    other = lax.ppermute(regrouped, "lev", [(i, i ^ 2) for i in range(count)])
    pair = jnp.where(
        (index // 2) % 2 == 1,
        jnp.concatenate([other, regrouped], axis=1),
        jnp.concatenate([regrouped, other], axis=1),
    )
    far = lax.ppermute(pair, "lev", [(i, i ^ 1) for i in range(count)])
    near_part = jnp.einsum("srj,sjd->srd", pair, legendre, preferred_element_type=jnp.float32)
    far_part = jnp.einsum("srj,sjd->srd", far, legendre, preferred_element_type=jnp.float32)
    even = index % 2 == 0
    blocks = []
    for half in range(2):
        mine = near_part[:, half * rows : (half + 1) * rows]
        theirs = far_part[:, half * rows : (half + 1) * rows]
        blocks.append(jnp.where(even, mine, theirs))
        blocks.append(jnp.where(even, theirs, mine))
    return jnp.concatenate(blocks, axis=1)


def row_block(rows):
    for size in (64, 32, 16):
        if rows % size == 0:
            return size
    return rows


def transform_kernel(points_ref, cells_ref, table_ref, weight_ref, slot_ref, sums_ref, out_ref, acc_ref, *scratch):
    step = pl.program_id(0)

    @pl.when(step == 0)
    def _():
        acc_ref[...] = jnp.zeros_like(acc_ref)

    nfields, nlev, rows, lon_count = cells_ref.shape
    nslot = acc_ref.shape[0]
    nblocks = lon_count // BLOCK
    table = table_ref[...]
    keep = (lax.broadcasted_iota(jnp.int32, (rows, lon_count), 1) < points_ref[...]).astype(jnp.bfloat16)
    cells = cells_ref[...] * keep[None, None]
    if rows % 16 == 0:
        sums = lax.dot_general(
            cells.reshape(nfields * nlev * rows, lon_count),
            table,
            (((1,), (1,)), ((), ())),
            preferred_element_type=jnp.float32,
        )
        sums_ref[...] = sums.reshape(sums_ref.shape)
    else:
        for f in range(nfields):
            for l in range(nlev):
                sums_ref[f, l] = lax.dot_general(
                    cells[f, l], table, (((1,), (1,)), ((), ())), preferred_element_type=jnp.float32
                )
    pieces = []
    for f in range(nfields):
        flux = weight_ref[f, 0] * cells[f, 0].astype(jnp.float32)
        for l in range(1, nlev):
            flux = flux + weight_ref[f, l] * cells[f, l].astype(jnp.float32)
        high = flux.astype(jnp.bfloat16)
        pieces.append(high)
        pieces.append((flux - high.astype(jnp.float32)).astype(jnp.bfloat16))
    if scratch:
        (stacked_ref,) = scratch
        for b in range(nblocks):
            for p, piece in enumerate(pieces):
                stacked_ref[b * rows : (b + 1) * rows, p * BLOCK : (p + 1) * BLOCK] = piece[
                    :, b * BLOCK : (b + 1) * BLOCK
                ]
        stacked = stacked_ref[...]
    else:
        stacked = jnp.concatenate(
            [
                jnp.concatenate(
                    [p[:, b * BLOCK : (b + 1) * BLOCK].astype(jnp.float32) for p in pieces], axis=1
                )
                for b in range(nblocks)
            ],
            axis=0,
        ).astype(jnp.bfloat16)
    onehot = (
        lax.broadcasted_iota(jnp.int32, (nslot, nblocks * rows), 0) == slot_ref[0]
    ).astype(jnp.bfloat16)
    acc_ref[...] += jnp.dot(onehot, stacked, preferred_element_type=jnp.float32)

    @pl.when(step == pl.num_programs(0) - 1)
    def _():
        nsec, tiles, _ = out_ref.shape
        for s in range(nsec):
            for f in range(nfields):
                high = acc_ref[s * tiles : (s + 1) * tiles, 2 * f * BLOCK : (2 * f + 1) * BLOCK]
                low = acc_ref[s * tiles : (s + 1) * tiles, (2 * f + 1) * BLOCK : (2 * f + 2) * BLOCK]
                out_ref[s, :, f * BLOCK : (f + 1) * BLOCK] = high + low


def fused_transform(atmos_fields, lat_points, table, column_weight, slots, nslot):
    nfields, nlev, lat_band, lon_count = atmos_fields.shape
    rows = row_block(lat_band)
    steps = lat_band // rows
    nblocks = lon_count // BLOCK
    wave2 = table.shape[0]
    slot_rows = slots.reshape(steps, rows, nblocks).transpose(0, 2, 1).reshape(steps, 1, nblocks * rows)
    scratch = [pltpu.VMEM((nslot, 2 * nfields * BLOCK), jnp.float32)]
    if rows % 16 == 0:
        scratch.append(pltpu.VMEM((nblocks * rows, 2 * nfields * BLOCK), jnp.bfloat16))
    return pl.pallas_call(
        transform_kernel,
        grid=(steps,),
        in_specs=[
            pl.BlockSpec((rows, 1), lambda r: (r, 0)),
            pl.BlockSpec((nfields, nlev, rows, lon_count), lambda r: (0, 0, r, 0)),
            pl.BlockSpec((wave2, lon_count), lambda r: (0, 0)),
            pl.BlockSpec(memory_space=pltpu.SMEM),
            pl.BlockSpec((1, 1, nblocks * rows), lambda r: (r, 0, 0)),
        ],
        out_specs=[
            pl.BlockSpec((nfields, nlev, rows, wave2), lambda r: (0, 0, r, 0)),
            pl.BlockSpec((3, nslot // 3, nfields * BLOCK), lambda r: (0, 0, 0)),
        ],
        out_shape=[
            jax.ShapeDtypeStruct((nfields, nlev, lat_band, wave2), jnp.float32),
            jax.ShapeDtypeStruct((3, nslot // 3, nfields * BLOCK), jnp.float32),
        ],
        scratch_shapes=scratch,
        compiler_params=pltpu.CompilerParams(dimension_semantics=("arbitrary",)),
    )(lat_points[:, None], atmos_fields, table, column_weight.astype(jnp.float32), slot_rows)


def surface_kernel(slot_ref, base_ref, limit_ref, tiles_ref, out_ref):
    lat_band, quarter = out_ref.shape
    nquarter = quarter // BLOCK
    group = 8
    sublane = lax.broadcasted_iota(jnp.int32, (group, BLOCK), 0)

    def per_group(g, carry):
        row0 = pl.multiple_of(g * group, group)
        for b in range(nquarter):
            rows = jnp.zeros((group, BLOCK), jnp.float32)
            for r in range(group):
                tile = slot_ref[(row0 + r) * nquarter + b]
                picked = jnp.broadcast_to(tiles_ref[pl.ds(tile, 1), :], (group, BLOCK))
                rows = jnp.where(sublane == r, picked, rows)
            out_ref[pl.ds(row0, group), b * BLOCK : (b + 1) * BLOCK] = rows
        return carry

    lax.fori_loop(0, lat_band // group, per_group, 0)
    points = base_ref[0] + lax.broadcasted_iota(jnp.int32, (lat_band, quarter), 1)
    out_ref[...] = jnp.where(points < limit_ref[...], out_ref[...], 0.0)


def surface_gather(slots, base, lat_points, tiles, quarter):
    lat_band = lat_points.shape[0]
    return pl.pallas_call(
        surface_kernel,
        in_specs=[
            pl.BlockSpec(memory_space=pltpu.SMEM),
            pl.BlockSpec(memory_space=pltpu.SMEM),
            pl.BlockSpec(memory_space=pltpu.VMEM),
            pl.BlockSpec(memory_space=pltpu.VMEM),
        ],
        out_specs=pl.BlockSpec(memory_space=pltpu.VMEM),
        out_shape=jax.ShapeDtypeStruct((lat_band, quarter), jnp.float32),
    )(slots, base, lat_points[:, None], tiles)


def body(
    atmos_fields,
    lat_points,
    wave_order,
    legendre,
    column_weight,
    block_remap,
    ocean_temp,
    ocean_salt,
    sea_mask,
):
    nfields, lev_dev, lat_band, lon_count = atmos_fields.shape
    wave_count = wave_order.shape[0]
    table, points = fourier_table(wave_order, lon_count)
    inverse_root = 1.0 / jnp.sqrt(lat_points.astype(jnp.float32))
    weights = jnp.where(
        2 * wave_order[None, :] < lat_points[:, None],
        inverse_root[:, None],
        jnp.zeros((), jnp.float32),
    )
    field_count = nfields
    ocean_rows, ocean_cols = ocean_temp.shape
    tile_count = ocean_rows * ocean_cols // BLOCK
    band_index = lax.axis_index(("lat", "ocn"))

    def slot_of(targets):
        return (targets // tile_count - band_index + 1) * tile_count + targets % tile_count

    local_slot = slot_of(block_remap.reshape(-1))
    quarter = lon_count // lax.axis_size("lev")
    full_remap = lev_gather(block_remap, 1)
    every_slot = slot_of(full_remap)
    raw_sums, sections = fused_transform(
        atmos_fields, lat_points, table, column_weight, every_slot, 3 * tile_count
    )
    raw_sums = raw_sums.reshape(field_count, lev_dev, lat_band, 2, wave_count)
    coeffs = (raw_sums * weights[None, None, :, None, :]).astype(jnp.bfloat16)
    regrouped = lax.all_to_all(
        coeffs.transpose(4, 1, 0, 3, 2).reshape(wave_count, lev_dev * field_count * 2, lat_band),
        ("lat", "ocn"),
        split_axis=0,
        concat_axis=2,
        tiled=True,
    )
    spectra = spectra_of(regrouped, legendre)
    band_count = lax.axis_size(("lat", "ocn"))
    from_prev = lax.ppermute(
        sections[2], ("lat", "ocn"), [(i, i + 1) for i in range(band_count - 1)]
    )
    from_next = lax.ppermute(
        sections[0], ("lat", "ocn"), [(i + 1, i) for i in range(band_count - 1)]
    )
    arrived = (from_prev + sections[1]) + from_next
    tile_sums = lev_sum(arrived)
    forcing = (
        tile_sums.reshape(ocean_rows, ocean_cols // BLOCK, FIELDS, BLOCK)
        .transpose(2, 0, 1, 3)
        .reshape(FIELDS, ocean_rows, ocean_cols)
    )
    sea_cells = (
        jnp.broadcast_to(sea_mask[:, :, None], (ocean_rows, ocean_cols // BLOCK, BLOCK))
        .reshape(ocean_rows, ocean_cols)
        .astype(jnp.float32)
    )
    ocean_state = jnp.stack([ocean_temp, ocean_salt])
    padded = with_halo(ocean_state, ((("lat", "ocn"), 1),), 1)
    laplace = (
        padded[:, 2:]
        + padded[:, :-2]
        + jnp.roll(ocean_state, 1, 2)
        + jnp.roll(ocean_state, -1, 2)
        - 4.0 * ocean_state
    )
    updated = ocean_state + DIFFUSION * laplace + COUPLING * sea_cells[None] * forcing
    temp_next = updated[0]
    salt_next = updated[1]
    returned = with_halo(temp_next, ((("lat", "ocn"), 0),), ocean_rows)
    tiles_near = returned.reshape(3 * tile_count, BLOCK)
    base = (lax.axis_index("lev") * quarter).astype(jnp.int32).reshape(1)
    surface_temp = surface_gather(local_slot, base, lat_points, tiles_near, quarter)
    return (spectra, temp_next, salt_next, surface_temp)


def solution(mesh):
    placed = (
        P(None, "lev", ("lat", "ocn"), None),
        P(("lat", "ocn")),
        P(),
        P(("lat", "ocn"), None, "lev"),
        P(None, "lev"),
        P(("lat", "ocn"), "lev"),
        P(("lat", "ocn"), None),
        P(("lat", "ocn"), None),
        P(("lat", "ocn"), None),
    )
    return jax.shard_map(
        body,
        mesh=mesh,
        in_specs=placed,
        out_specs=(
            P(("lat", "ocn"), None, "lev"),
            P(("lat", "ocn"), None),
            P(("lat", "ocn"), None),
            P(("lat", "ocn"), "lev"),
        ),
        check_vma=False,
    )
```

```python
import math

import jax
import jax.numpy as jnp
from jax import lax
from jax.experimental import pallas as pl
from jax.experimental.pallas import tpu as pltpu
from jax.sharding import PartitionSpec as P

FIELDS = 2
BLOCK = 128


FULL_TURN = 2.0 * math.pi
DIFFUSION = 0.2
COUPLING = 0.5


def with_halo(cells, sides, width):
    for axis, dim in sides:
        count = lax.axis_size(axis)
        ends = count - 1
        head = lax.slice_in_dim(cells, 0, width, axis=dim)
        tail = lax.slice_in_dim(cells, cells.shape[dim] - width, cells.shape[dim], axis=dim)
        cells = jnp.concatenate(
            [
                lax.ppermute(tail, axis, [(i, (i + 1) % count) for i in range(ends)]),
                cells,
                lax.ppermute(head, axis, [((i + 1) % count, i) for i in range(ends)]),
            ],
            axis=dim,
        )
    return cells


def fourier_table(wave_order, length):
    points = jnp.arange(length, dtype=jnp.int32)
    phase = wave_order[:, None] * points[None, :] % length
    angle = phase.astype(jnp.float32) * (FULL_TURN / length)
    table = jnp.concatenate([jnp.cos(angle), -jnp.sin(angle)], axis=0).astype(jnp.bfloat16)
    return (table, points)


def lev_sum(values):
    count = lax.axis_size("lev")
    if count & (count - 1):
        return lax.psum(values, "lev")
    stride = 1
    while stride < count:
        values = values + lax.ppermute(values, "lev", [(i, i ^ stride) for i in range(count)])
        stride *= 2
    return values


def lev_gather(values, axis):
    count = lax.axis_size("lev")
    if count & (count - 1):
        return lax.all_gather(values, "lev", axis=axis, tiled=True)
    index = lax.axis_index("lev")
    stride = 1
    while stride < count:
        other = lax.ppermute(values, "lev", [(i, i ^ stride) for i in range(count)])
        upper = (index // stride) % 2 == 1
        values = jnp.where(
            upper,
            jnp.concatenate([other, values], axis=axis),
            jnp.concatenate([values, other], axis=axis),
        )
        stride *= 2
    return values


def row_block(rows):
    for size in (64, 32, 16):
        if rows % size == 0:
            return size
    return rows


def transform_kernel(points_ref, cells_ref, table_ref, weight_ref, slot_ref, sums_ref, out_ref, acc_ref, *scratch):
    step = pl.program_id(0)

    @pl.when(step == 0)
    def _():
        acc_ref[...] = jnp.zeros_like(acc_ref)

    nfields, nlev, rows, lon_count = cells_ref.shape
    nslot = acc_ref.shape[0]
    nblocks = lon_count // BLOCK
    table = table_ref[...]
    keep = (lax.broadcasted_iota(jnp.int32, (rows, lon_count), 1) < points_ref[...]).astype(jnp.bfloat16)
    cells = cells_ref[...] * keep[None, None]
    if rows % 16 == 0:
        sums = lax.dot_general(
            cells.reshape(nfields * nlev * rows, lon_count),
            table,
            (((1,), (1,)), ((), ())),
            preferred_element_type=jnp.float32,
        )
        sums_ref[...] = sums.reshape(sums_ref.shape)
    else:
        for f in range(nfields):
            for l in range(nlev):
                sums_ref[f, l] = lax.dot_general(
                    cells[f, l], table, (((1,), (1,)), ((), ())), preferred_element_type=jnp.float32
                )
    pieces = []
    for f in range(nfields):
        flux = weight_ref[f, 0] * cells[f, 0].astype(jnp.float32)
        for l in range(1, nlev):
            flux = flux + weight_ref[f, l] * cells[f, l].astype(jnp.float32)
        high = flux.astype(jnp.bfloat16)
        pieces.append(high)
        pieces.append((flux - high.astype(jnp.float32)).astype(jnp.bfloat16))
    if scratch:
        (stacked_ref,) = scratch
        for b in range(nblocks):
            for p, piece in enumerate(pieces):
                stacked_ref[b * rows : (b + 1) * rows, p * BLOCK : (p + 1) * BLOCK] = piece[
                    :, b * BLOCK : (b + 1) * BLOCK
                ]
        stacked = stacked_ref[...]
    else:
        stacked = jnp.concatenate(
            [
                jnp.concatenate(
                    [p[:, b * BLOCK : (b + 1) * BLOCK].astype(jnp.float32) for p in pieces], axis=1
                )
                for b in range(nblocks)
            ],
            axis=0,
        ).astype(jnp.bfloat16)
    onehot = (
        lax.broadcasted_iota(jnp.int32, (nslot, nblocks * rows), 0) == slot_ref[0]
    ).astype(jnp.bfloat16)
    acc_ref[...] += jnp.dot(onehot, stacked, preferred_element_type=jnp.float32)

    @pl.when(step == pl.num_programs(0) - 1)
    def _():
        nsec, tiles, _ = out_ref.shape
        for s in range(nsec):
            for f in range(nfields):
                high = acc_ref[s * tiles : (s + 1) * tiles, 2 * f * BLOCK : (2 * f + 1) * BLOCK]
                low = acc_ref[s * tiles : (s + 1) * tiles, (2 * f + 1) * BLOCK : (2 * f + 2) * BLOCK]
                out_ref[s, :, f * BLOCK : (f + 1) * BLOCK] = high + low


def fused_transform(atmos_fields, lat_points, table, column_weight, slots, nslot):
    nfields, nlev, lat_band, lon_count = atmos_fields.shape
    rows = row_block(lat_band)
    steps = lat_band // rows
    nblocks = lon_count // BLOCK
    wave2 = table.shape[0]
    slot_rows = slots.reshape(steps, rows, nblocks).transpose(0, 2, 1).reshape(steps, 1, nblocks * rows)
    scratch = [pltpu.VMEM((nslot, 2 * nfields * BLOCK), jnp.float32)]
    if rows % 16 == 0:
        scratch.append(pltpu.VMEM((nblocks * rows, 2 * nfields * BLOCK), jnp.bfloat16))
    return pl.pallas_call(
        transform_kernel,
        grid=(steps,),
        in_specs=[
            pl.BlockSpec((rows, 1), lambda r: (r, 0)),
            pl.BlockSpec((nfields, nlev, rows, lon_count), lambda r: (0, 0, r, 0)),
            pl.BlockSpec((wave2, lon_count), lambda r: (0, 0)),
            pl.BlockSpec(memory_space=pltpu.SMEM),
            pl.BlockSpec((1, 1, nblocks * rows), lambda r: (r, 0, 0)),
        ],
        out_specs=[
            pl.BlockSpec((nfields, nlev, rows, wave2), lambda r: (0, 0, r, 0)),
            pl.BlockSpec((3, nslot // 3, nfields * BLOCK), lambda r: (0, 0, 0)),
        ],
        out_shape=[
            jax.ShapeDtypeStruct((nfields, nlev, lat_band, wave2), jnp.float32),
            jax.ShapeDtypeStruct((3, nslot // 3, nfields * BLOCK), jnp.float32),
        ],
        scratch_shapes=scratch,
        compiler_params=pltpu.CompilerParams(dimension_semantics=("arbitrary",)),
    )(lat_points[:, None], atmos_fields, table, column_weight.astype(jnp.float32), slot_rows)


def surface_kernel(slot_ref, base_ref, limit_ref, tiles_ref, out_ref):
    lat_band, quarter = out_ref.shape
    nquarter = quarter // BLOCK
    group = 8
    sublane = lax.broadcasted_iota(jnp.int32, (group, BLOCK), 0)

    def per_group(g, carry):
        row0 = pl.multiple_of(g * group, group)
        for b in range(nquarter):
            rows = jnp.zeros((group, BLOCK), jnp.float32)
            for r in range(group):
                tile = slot_ref[(row0 + r) * nquarter + b]
                picked = jnp.broadcast_to(tiles_ref[pl.ds(tile, 1), :], (group, BLOCK))
                rows = jnp.where(sublane == r, picked, rows)
            out_ref[pl.ds(row0, group), b * BLOCK : (b + 1) * BLOCK] = rows
        return carry

    lax.fori_loop(0, lat_band // group, per_group, 0)
    points = base_ref[0] + lax.broadcasted_iota(jnp.int32, (lat_band, quarter), 1)
    out_ref[...] = jnp.where(points < limit_ref[...], out_ref[...], 0.0)


def surface_gather(slots, base, lat_points, tiles, quarter):
    lat_band = lat_points.shape[0]
    return pl.pallas_call(
        surface_kernel,
        in_specs=[
            pl.BlockSpec(memory_space=pltpu.SMEM),
            pl.BlockSpec(memory_space=pltpu.SMEM),
            pl.BlockSpec(memory_space=pltpu.VMEM),
            pl.BlockSpec(memory_space=pltpu.VMEM),
        ],
        out_specs=pl.BlockSpec(memory_space=pltpu.VMEM),
        out_shape=jax.ShapeDtypeStruct((lat_band, quarter), jnp.float32),
    )(slots, base, lat_points[:, None], tiles)


def body(
    atmos_fields,
    lat_points,
    wave_order,
    legendre,
    column_weight,
    block_remap,
    ocean_temp,
    ocean_salt,
    sea_mask,
):
    nfields, lev_dev, lat_band, lon_count = atmos_fields.shape
    wave_count = wave_order.shape[0]
    table, points = fourier_table(wave_order, lon_count)
    inverse_root = 1.0 / jnp.sqrt(lat_points.astype(jnp.float32))
    weights = jnp.where(
        2 * wave_order[None, :] < lat_points[:, None],
        inverse_root[:, None],
        jnp.zeros((), jnp.float32),
    )
    field_count = nfields
    ocean_rows, ocean_cols = ocean_temp.shape
    tile_count = ocean_rows * ocean_cols // BLOCK
    band_index = lax.axis_index(("lat", "ocn"))

    def slot_of(targets):
        return (targets // tile_count - band_index + 1) * tile_count + targets % tile_count

    local_slot = slot_of(block_remap.reshape(-1))
    quarter = lon_count // lax.axis_size("lev")
    full_remap = lev_gather(block_remap, 1)
    every_slot = slot_of(full_remap)
    raw_sums, sections = fused_transform(
        atmos_fields, lat_points, table, column_weight, every_slot, 3 * tile_count
    )
    raw_sums = raw_sums.reshape(field_count, lev_dev, lat_band, 2, wave_count)
    coeffs = (raw_sums * weights[None, None, :, None, :]).astype(jnp.bfloat16)
    regrouped = lax.all_to_all(
        coeffs.transpose(4, 1, 0, 3, 2).reshape(wave_count, lev_dev * field_count * 2, lat_band),
        ("lat", "ocn"),
        split_axis=0,
        concat_axis=2,
        tiled=True,
    )
    sections, regrouped = lax.optimization_barrier((sections, regrouped))
    spectra = jnp.einsum(
        "srj,sjd->srd",
        lev_gather(regrouped, 1),
        legendre,
        preferred_element_type=jnp.float32,
    )
    band_count = lax.axis_size(("lat", "ocn"))
    from_prev = lax.ppermute(
        sections[2], ("lat", "ocn"), [(i, i + 1) for i in range(band_count - 1)]
    )
    from_next = lax.ppermute(
        sections[0], ("lat", "ocn"), [(i + 1, i) for i in range(band_count - 1)]
    )
    arrived = (from_prev + sections[1]) + from_next
    tile_sums = lev_sum(arrived)
    forcing = (
        tile_sums.reshape(ocean_rows, ocean_cols // BLOCK, FIELDS, BLOCK)
        .transpose(2, 0, 1, 3)
        .reshape(FIELDS, ocean_rows, ocean_cols)
    )
    sea_cells = (
        jnp.broadcast_to(sea_mask[:, :, None], (ocean_rows, ocean_cols // BLOCK, BLOCK))
        .reshape(ocean_rows, ocean_cols)
        .astype(jnp.float32)
    )
    ocean_state = jnp.stack([ocean_temp, ocean_salt])
    padded = with_halo(ocean_state, ((("lat", "ocn"), 1),), 1)
    laplace = (
        padded[:, 2:]
        + padded[:, :-2]
        + jnp.roll(ocean_state, 1, 2)
        + jnp.roll(ocean_state, -1, 2)
        - 4.0 * ocean_state
    )
    updated = ocean_state + DIFFUSION * laplace + COUPLING * sea_cells[None] * forcing
    temp_next = updated[0]
    salt_next = updated[1]
    returned = with_halo(temp_next, ((("lat", "ocn"), 0),), ocean_rows)
    tiles_near = returned.reshape(3 * tile_count, BLOCK)
    base = (lax.axis_index("lev") * quarter).astype(jnp.int32).reshape(1)
    surface_temp = surface_gather(local_slot, base, lat_points, tiles_near, quarter)
    return (spectra, temp_next, salt_next, surface_temp)


def solution(mesh):
    placed = (
        P(None, "lev", ("lat", "ocn"), None),
        P(("lat", "ocn")),
        P(),
        P(("lat", "ocn"), None, "lev"),
        P(None, "lev"),
        P(("lat", "ocn"), "lev"),
        P(("lat", "ocn"), None),
        P(("lat", "ocn"), None),
        P(("lat", "ocn"), None),
    )
    return jax.shard_map(
        body,
        mesh=mesh,
        in_specs=placed,
        out_specs=(
            P(("lat", "ocn"), None, "lev"),
            P(("lat", "ocn"), None),
            P(("lat", "ocn"), None),
            P(("lat", "ocn"), "lev"),
        ),
        check_vma=False,
    )
```

```python
import math

import jax
import jax.numpy as jnp
from jax import lax
from jax.experimental import pallas as pl
from jax.experimental.pallas import tpu as pltpu
from jax.sharding import PartitionSpec as P

FIELDS = 2
BLOCK = 128


FULL_TURN = 2.0 * math.pi
DIFFUSION = 0.2
COUPLING = 0.5


def with_halo(cells, sides, width):
    for axis, dim in sides:
        count = lax.axis_size(axis)
        ends = count - 1
        head = lax.slice_in_dim(cells, 0, width, axis=dim)
        tail = lax.slice_in_dim(cells, cells.shape[dim] - width, cells.shape[dim], axis=dim)
        cells = jnp.concatenate(
            [
                lax.ppermute(tail, axis, [(i, (i + 1) % count) for i in range(ends)]),
                cells,
                lax.ppermute(head, axis, [((i + 1) % count, i) for i in range(ends)]),
            ],
            axis=dim,
        )
    return cells


def fourier_table(wave_order, length):
    points = jnp.arange(length, dtype=jnp.int32)
    phase = wave_order[:, None] * points[None, :] % length
    angle = phase.astype(jnp.float32) * (FULL_TURN / length)
    table = jnp.concatenate([jnp.cos(angle), -jnp.sin(angle)], axis=0).astype(jnp.bfloat16)
    return (table, points)


def lev_sum(values):
    count = lax.axis_size("lev")
    if count & (count - 1):
        return lax.psum(values, "lev")
    stride = 1
    while stride < count:
        values = values + lax.ppermute(values, "lev", [(i, i ^ stride) for i in range(count)])
        stride *= 2
    return values


def lev_gather(values, axis):
    count = lax.axis_size("lev")
    if count & (count - 1):
        return lax.all_gather(values, "lev", axis=axis, tiled=True)
    index = lax.axis_index("lev")
    stride = 1
    while stride < count:
        other = lax.ppermute(values, "lev", [(i, i ^ stride) for i in range(count)])
        upper = (index // stride) % 2 == 1
        values = jnp.where(
            upper,
            jnp.concatenate([other, values], axis=axis),
            jnp.concatenate([values, other], axis=axis),
        )
        stride *= 2
    return values


def lev_gather_far_first(values, axis):
    count = lax.axis_size("lev")
    if count != 4:
        return lev_gather(values, axis)
    index = lax.axis_index("lev")
    size = values.shape[axis]
    other = lax.ppermute(values, "lev", [(i, i ^ 2) for i in range(count)])
    pair = jnp.where(
        (index // 2) % 2 == 1,
        jnp.concatenate([other, values], axis=axis),
        jnp.concatenate([values, other], axis=axis),
    )
    far = lax.ppermute(pair, "lev", [(i, i ^ 1) for i in range(count)])
    even = index % 2 == 0
    first = jnp.where(even, pair, far)
    second = jnp.where(even, far, pair)
    parts = []
    for half in range(2):
        parts.append(lax.slice_in_dim(first, half * size, (half + 1) * size, axis=axis))
        parts.append(lax.slice_in_dim(second, half * size, (half + 1) * size, axis=axis))
    return jnp.concatenate(parts, axis=axis)


def row_block(rows):
    for size in (64, 32, 16):
        if rows % size == 0:
            return size
    return rows


def transform_kernel(points_ref, cells_ref, table_ref, weight_ref, slot_ref, sums_ref, out_ref, acc_ref, *scratch):
    step = pl.program_id(0)

    @pl.when(step == 0)
    def _():
        acc_ref[...] = jnp.zeros_like(acc_ref)

    nfields, nlev, rows, lon_count = cells_ref.shape
    nslot = acc_ref.shape[0]
    nblocks = lon_count // BLOCK
    table = table_ref[...]
    keep = (lax.broadcasted_iota(jnp.int32, (rows, lon_count), 1) < points_ref[...]).astype(jnp.bfloat16)
    cells = cells_ref[...] * keep[None, None]
    if rows % 16 == 0:
        sums = lax.dot_general(
            cells.reshape(nfields * nlev * rows, lon_count),
            table,
            (((1,), (1,)), ((), ())),
            preferred_element_type=jnp.float32,
        )
        sums_ref[...] = sums.reshape(sums_ref.shape)
    else:
        for f in range(nfields):
            for l in range(nlev):
                sums_ref[f, l] = lax.dot_general(
                    cells[f, l], table, (((1,), (1,)), ((), ())), preferred_element_type=jnp.float32
                )
    pieces = []
    for f in range(nfields):
        flux = weight_ref[f, 0] * cells[f, 0].astype(jnp.float32)
        for l in range(1, nlev):
            flux = flux + weight_ref[f, l] * cells[f, l].astype(jnp.float32)
        high = flux.astype(jnp.bfloat16)
        pieces.append(high)
        pieces.append((flux - high.astype(jnp.float32)).astype(jnp.bfloat16))
    if scratch:
        (stacked_ref,) = scratch
        for b in range(nblocks):
            for p, piece in enumerate(pieces):
                stacked_ref[b * rows : (b + 1) * rows, p * BLOCK : (p + 1) * BLOCK] = piece[
                    :, b * BLOCK : (b + 1) * BLOCK
                ]
        stacked = stacked_ref[...]
    else:
        stacked = jnp.concatenate(
            [
                jnp.concatenate(
                    [p[:, b * BLOCK : (b + 1) * BLOCK].astype(jnp.float32) for p in pieces], axis=1
                )
                for b in range(nblocks)
            ],
            axis=0,
        ).astype(jnp.bfloat16)
    onehot = (
        lax.broadcasted_iota(jnp.int32, (nslot, nblocks * rows), 0) == slot_ref[0]
    ).astype(jnp.bfloat16)
    acc_ref[...] += jnp.dot(onehot, stacked, preferred_element_type=jnp.float32)

    @pl.when(step == pl.num_programs(0) - 1)
    def _():
        nsec, tiles, _ = out_ref.shape
        for s in range(nsec):
            for f in range(nfields):
                high = acc_ref[s * tiles : (s + 1) * tiles, 2 * f * BLOCK : (2 * f + 1) * BLOCK]
                low = acc_ref[s * tiles : (s + 1) * tiles, (2 * f + 1) * BLOCK : (2 * f + 2) * BLOCK]
                out_ref[s, :, f * BLOCK : (f + 1) * BLOCK] = high + low


def fused_transform(atmos_fields, lat_points, table, column_weight, slots, nslot):
    nfields, nlev, lat_band, lon_count = atmos_fields.shape
    rows = row_block(lat_band)
    steps = lat_band // rows
    nblocks = lon_count // BLOCK
    wave2 = table.shape[0]
    slot_rows = slots.reshape(steps, rows, nblocks).transpose(0, 2, 1).reshape(steps, 1, nblocks * rows)
    scratch = [pltpu.VMEM((nslot, 2 * nfields * BLOCK), jnp.float32)]
    if rows % 16 == 0:
        scratch.append(pltpu.VMEM((nblocks * rows, 2 * nfields * BLOCK), jnp.bfloat16))
    return pl.pallas_call(
        transform_kernel,
        grid=(steps,),
        in_specs=[
            pl.BlockSpec((rows, 1), lambda r: (r, 0)),
            pl.BlockSpec((nfields, nlev, rows, lon_count), lambda r: (0, 0, r, 0)),
            pl.BlockSpec((wave2, lon_count), lambda r: (0, 0)),
            pl.BlockSpec(memory_space=pltpu.SMEM),
            pl.BlockSpec((1, 1, nblocks * rows), lambda r: (r, 0, 0)),
        ],
        out_specs=[
            pl.BlockSpec((nfields, nlev, rows, wave2), lambda r: (0, 0, r, 0)),
            pl.BlockSpec((3, nslot // 3, nfields * BLOCK), lambda r: (0, 0, 0)),
        ],
        out_shape=[
            jax.ShapeDtypeStruct((nfields, nlev, lat_band, wave2), jnp.float32),
            jax.ShapeDtypeStruct((3, nslot // 3, nfields * BLOCK), jnp.float32),
        ],
        scratch_shapes=scratch,
        compiler_params=pltpu.CompilerParams(dimension_semantics=("arbitrary",)),
    )(lat_points[:, None], atmos_fields, table, column_weight.astype(jnp.float32), slot_rows)


def surface_kernel(slot_ref, base_ref, limit_ref, tiles_ref, out_ref):
    lat_band, quarter = out_ref.shape
    nquarter = quarter // BLOCK
    group = 8
    sublane = lax.broadcasted_iota(jnp.int32, (group, BLOCK), 0)

    def per_group(g, carry):
        row0 = pl.multiple_of(g * group, group)
        for b in range(nquarter):
            rows = jnp.zeros((group, BLOCK), jnp.float32)
            for r in range(group):
                tile = slot_ref[(row0 + r) * nquarter + b]
                picked = jnp.broadcast_to(tiles_ref[pl.ds(tile, 1), :], (group, BLOCK))
                rows = jnp.where(sublane == r, picked, rows)
            out_ref[pl.ds(row0, group), b * BLOCK : (b + 1) * BLOCK] = rows
        return carry

    lax.fori_loop(0, lat_band // group, per_group, 0)
    points = base_ref[0] + lax.broadcasted_iota(jnp.int32, (lat_band, quarter), 1)
    out_ref[...] = jnp.where(points < limit_ref[...], out_ref[...], 0.0)


def surface_gather(slots, base, lat_points, tiles, quarter):
    lat_band = lat_points.shape[0]
    return pl.pallas_call(
        surface_kernel,
        in_specs=[
            pl.BlockSpec(memory_space=pltpu.SMEM),
            pl.BlockSpec(memory_space=pltpu.SMEM),
            pl.BlockSpec(memory_space=pltpu.VMEM),
            pl.BlockSpec(memory_space=pltpu.VMEM),
        ],
        out_specs=pl.BlockSpec(memory_space=pltpu.VMEM),
        out_shape=jax.ShapeDtypeStruct((lat_band, quarter), jnp.float32),
    )(slots, base, lat_points[:, None], tiles)


def body(
    atmos_fields,
    lat_points,
    wave_order,
    legendre,
    column_weight,
    block_remap,
    ocean_temp,
    ocean_salt,
    sea_mask,
):
    nfields, lev_dev, lat_band, lon_count = atmos_fields.shape
    wave_count = wave_order.shape[0]
    table, points = fourier_table(wave_order, lon_count)
    inverse_root = 1.0 / jnp.sqrt(lat_points.astype(jnp.float32))
    weights = jnp.where(
        2 * wave_order[None, :] < lat_points[:, None],
        inverse_root[:, None],
        jnp.zeros((), jnp.float32),
    )
    field_count = nfields
    ocean_rows, ocean_cols = ocean_temp.shape
    tile_count = ocean_rows * ocean_cols // BLOCK
    band_index = lax.axis_index(("lat", "ocn"))

    def slot_of(targets):
        return (targets // tile_count - band_index + 1) * tile_count + targets % tile_count

    local_slot = slot_of(block_remap.reshape(-1))
    quarter = lon_count // lax.axis_size("lev")
    full_remap = lev_gather(block_remap, 1)
    every_slot = slot_of(full_remap)
    raw_sums, sections = fused_transform(
        atmos_fields, lat_points, table, column_weight, every_slot, 3 * tile_count
    )
    raw_sums = raw_sums.reshape(field_count, lev_dev, lat_band, 2, wave_count)
    coeffs = (raw_sums * weights[None, None, :, None, :]).astype(jnp.bfloat16)
    regrouped = lax.all_to_all(
        coeffs.transpose(4, 1, 0, 3, 2).reshape(wave_count, lev_dev * field_count * 2, lat_band),
        ("lat", "ocn"),
        split_axis=0,
        concat_axis=2,
        tiled=True,
    )
    spectra = jnp.einsum(
        "srj,sjd->srd",
        lev_gather_far_first(regrouped, 1),
        legendre,
        preferred_element_type=jnp.float32,
    )
    band_count = lax.axis_size(("lat", "ocn"))
    from_prev = lax.ppermute(
        sections[2], ("lat", "ocn"), [(i, i + 1) for i in range(band_count - 1)]
    )
    from_next = lax.ppermute(
        sections[0], ("lat", "ocn"), [(i + 1, i) for i in range(band_count - 1)]
    )
    arrived = (from_prev + sections[1]) + from_next
    tile_sums = lev_sum(arrived)
    forcing = (
        tile_sums.reshape(ocean_rows, ocean_cols // BLOCK, FIELDS, BLOCK)
        .transpose(2, 0, 1, 3)
        .reshape(FIELDS, ocean_rows, ocean_cols)
    )
    sea_cells = (
        jnp.broadcast_to(sea_mask[:, :, None], (ocean_rows, ocean_cols // BLOCK, BLOCK))
        .reshape(ocean_rows, ocean_cols)
        .astype(jnp.float32)
    )
    ocean_state = jnp.stack([ocean_temp, ocean_salt])
    padded = with_halo(ocean_state, ((("lat", "ocn"), 1),), 1)
    laplace = (
        padded[:, 2:]
        + padded[:, :-2]
        + jnp.roll(ocean_state, 1, 2)
        + jnp.roll(ocean_state, -1, 2)
        - 4.0 * ocean_state
    )
    updated = ocean_state + DIFFUSION * laplace + COUPLING * sea_cells[None] * forcing
    temp_next = updated[0]
    salt_next = updated[1]
    returned = with_halo(temp_next, ((("lat", "ocn"), 0),), ocean_rows)
    tiles_near = returned.reshape(3 * tile_count, BLOCK)
    base = (lax.axis_index("lev") * quarter).astype(jnp.int32).reshape(1)
    surface_temp = surface_gather(local_slot, base, lat_points, tiles_near, quarter)
    return (spectra, temp_next, salt_next, surface_temp)


def solution(mesh):
    placed = (
        P(None, "lev", ("lat", "ocn"), None),
        P(("lat", "ocn")),
        P(),
        P(("lat", "ocn"), None, "lev"),
        P(None, "lev"),
        P(("lat", "ocn"), "lev"),
        P(("lat", "ocn"), None),
        P(("lat", "ocn"), None),
        P(("lat", "ocn"), None),
    )
    return jax.shard_map(
        body,
        mesh=mesh,
        in_specs=placed,
        out_specs=(
            P(("lat", "ocn"), None, "lev"),
            P(("lat", "ocn"), None),
            P(("lat", "ocn"), None),
            P(("lat", "ocn"), "lev"),
        ),
        check_vma=False,
    )
```

```python
import math

import jax
import jax.numpy as jnp
from jax import lax
from jax.experimental import pallas as pl
from jax.experimental.pallas import tpu as pltpu
from jax.sharding import PartitionSpec as P

FIELDS = 2
BLOCK = 128


FULL_TURN = 2.0 * math.pi
DIFFUSION = 0.2
COUPLING = 0.5


def with_halo(cells, sides, width):
    for axis, dim in sides:
        count = lax.axis_size(axis)
        ends = count - 1
        head = lax.slice_in_dim(cells, 0, width, axis=dim)
        tail = lax.slice_in_dim(cells, cells.shape[dim] - width, cells.shape[dim], axis=dim)
        cells = jnp.concatenate(
            [
                lax.ppermute(tail, axis, [(i, (i + 1) % count) for i in range(ends)]),
                cells,
                lax.ppermute(head, axis, [((i + 1) % count, i) for i in range(ends)]),
            ],
            axis=dim,
        )
    return cells


def fourier_table(wave_order, length):
    points = jnp.arange(length, dtype=jnp.int32)
    phase = wave_order[:, None] * points[None, :] % length
    angle = phase.astype(jnp.float32) * (FULL_TURN / length)
    table = jnp.concatenate([jnp.cos(angle), -jnp.sin(angle)], axis=0).astype(jnp.bfloat16)
    return (table, points)


def lev_sum(values):
    count = lax.axis_size("lev")
    if count & (count - 1):
        return lax.psum(values, "lev")
    stride = 1
    while stride < count:
        values = values + lax.ppermute(values, "lev", [(i, i ^ stride) for i in range(count)])
        stride *= 2
    return values


def lev_gather(values, axis):
    count = lax.axis_size("lev")
    if count & (count - 1):
        return lax.all_gather(values, "lev", axis=axis, tiled=True)
    index = lax.axis_index("lev")
    stride = 1
    while stride < count:
        other = lax.ppermute(values, "lev", [(i, i ^ stride) for i in range(count)])
        upper = (index // stride) % 2 == 1
        values = jnp.where(
            upper,
            jnp.concatenate([other, values], axis=axis),
            jnp.concatenate([values, other], axis=axis),
        )
        stride *= 2
    return values


def lev_pair_far(values):
    index = lax.axis_index("lev")
    other = lax.ppermute(values, "lev", [(i, i ^ 2) for i in range(4)])
    return jnp.where(
        (index // 2) % 2 == 1,
        jnp.concatenate([other, values], axis=1),
        jnp.concatenate([values, other], axis=1),
    )


def lev_pair_near(pair, size):
    index = lax.axis_index("lev")
    far = lax.ppermute(pair, "lev", [(i, i ^ 1) for i in range(4)])
    even = index % 2 == 0
    first = jnp.where(even, pair, far)
    second = jnp.where(even, far, pair)
    parts = []
    for half in range(2):
        parts.append(first[:, half * size : (half + 1) * size])
        parts.append(second[:, half * size : (half + 1) * size])
    return jnp.concatenate(parts, axis=1)


def row_block(rows):
    for size in (64, 32, 16):
        if rows % size == 0:
            return size
    return rows


def transform_kernel(points_ref, cells_ref, table_ref, weight_ref, slot_ref, sums_ref, out_ref, acc_ref, *scratch):
    step = pl.program_id(0)

    @pl.when(step == 0)
    def _():
        acc_ref[...] = jnp.zeros_like(acc_ref)

    nfields, nlev, rows, lon_count = cells_ref.shape
    nslot = acc_ref.shape[0]
    nblocks = lon_count // BLOCK
    table = table_ref[...]
    keep = (lax.broadcasted_iota(jnp.int32, (rows, lon_count), 1) < points_ref[...]).astype(jnp.bfloat16)
    cells = cells_ref[...] * keep[None, None]
    if rows % 16 == 0:
        sums = lax.dot_general(
            cells.reshape(nfields * nlev * rows, lon_count),
            table,
            (((1,), (1,)), ((), ())),
            preferred_element_type=jnp.float32,
        )
        sums_ref[...] = sums.reshape(sums_ref.shape)
    else:
        for f in range(nfields):
            for l in range(nlev):
                sums_ref[f, l] = lax.dot_general(
                    cells[f, l], table, (((1,), (1,)), ((), ())), preferred_element_type=jnp.float32
                )
    pieces = []
    for f in range(nfields):
        flux = weight_ref[f, 0] * cells[f, 0].astype(jnp.float32)
        for l in range(1, nlev):
            flux = flux + weight_ref[f, l] * cells[f, l].astype(jnp.float32)
        high = flux.astype(jnp.bfloat16)
        pieces.append(high)
        pieces.append((flux - high.astype(jnp.float32)).astype(jnp.bfloat16))
    if scratch:
        (stacked_ref,) = scratch
        for b in range(nblocks):
            for p, piece in enumerate(pieces):
                stacked_ref[b * rows : (b + 1) * rows, p * BLOCK : (p + 1) * BLOCK] = piece[
                    :, b * BLOCK : (b + 1) * BLOCK
                ]
        stacked = stacked_ref[...]
    else:
        stacked = jnp.concatenate(
            [
                jnp.concatenate(
                    [p[:, b * BLOCK : (b + 1) * BLOCK].astype(jnp.float32) for p in pieces], axis=1
                )
                for b in range(nblocks)
            ],
            axis=0,
        ).astype(jnp.bfloat16)
    onehot = (
        lax.broadcasted_iota(jnp.int32, (nslot, nblocks * rows), 0) == slot_ref[0]
    ).astype(jnp.bfloat16)
    acc_ref[...] += jnp.dot(onehot, stacked, preferred_element_type=jnp.float32)

    @pl.when(step == pl.num_programs(0) - 1)
    def _():
        nsec, tiles, _ = out_ref.shape
        for s in range(nsec):
            for f in range(nfields):
                high = acc_ref[s * tiles : (s + 1) * tiles, 2 * f * BLOCK : (2 * f + 1) * BLOCK]
                low = acc_ref[s * tiles : (s + 1) * tiles, (2 * f + 1) * BLOCK : (2 * f + 2) * BLOCK]
                out_ref[s, :, f * BLOCK : (f + 1) * BLOCK] = high + low


def fused_transform(atmos_fields, lat_points, table, column_weight, slots, nslot):
    nfields, nlev, lat_band, lon_count = atmos_fields.shape
    rows = row_block(lat_band)
    steps = lat_band // rows
    nblocks = lon_count // BLOCK
    wave2 = table.shape[0]
    slot_rows = slots.reshape(steps, rows, nblocks).transpose(0, 2, 1).reshape(steps, 1, nblocks * rows)
    scratch = [pltpu.VMEM((nslot, 2 * nfields * BLOCK), jnp.float32)]
    if rows % 16 == 0:
        scratch.append(pltpu.VMEM((nblocks * rows, 2 * nfields * BLOCK), jnp.bfloat16))
    return pl.pallas_call(
        transform_kernel,
        grid=(steps,),
        in_specs=[
            pl.BlockSpec((rows, 1), lambda r: (r, 0)),
            pl.BlockSpec((nfields, nlev, rows, lon_count), lambda r: (0, 0, r, 0)),
            pl.BlockSpec((wave2, lon_count), lambda r: (0, 0)),
            pl.BlockSpec(memory_space=pltpu.SMEM),
            pl.BlockSpec((1, 1, nblocks * rows), lambda r: (r, 0, 0)),
        ],
        out_specs=[
            pl.BlockSpec((nfields, nlev, rows, wave2), lambda r: (0, 0, r, 0)),
            pl.BlockSpec((3, nslot // 3, nfields * BLOCK), lambda r: (0, 0, 0)),
        ],
        out_shape=[
            jax.ShapeDtypeStruct((nfields, nlev, lat_band, wave2), jnp.float32),
            jax.ShapeDtypeStruct((3, nslot // 3, nfields * BLOCK), jnp.float32),
        ],
        scratch_shapes=scratch,
        compiler_params=pltpu.CompilerParams(dimension_semantics=("arbitrary",)),
    )(lat_points[:, None], atmos_fields, table, column_weight.astype(jnp.float32), slot_rows)


def surface_kernel(slot_ref, base_ref, limit_ref, tiles_ref, out_ref):
    lat_band, quarter = out_ref.shape
    nquarter = quarter // BLOCK
    group = 8
    sublane = lax.broadcasted_iota(jnp.int32, (group, BLOCK), 0)

    def per_group(g, carry):
        row0 = pl.multiple_of(g * group, group)
        for b in range(nquarter):
            rows = jnp.zeros((group, BLOCK), jnp.float32)
            for r in range(group):
                tile = slot_ref[(row0 + r) * nquarter + b]
                picked = jnp.broadcast_to(tiles_ref[pl.ds(tile, 1), :], (group, BLOCK))
                rows = jnp.where(sublane == r, picked, rows)
            out_ref[pl.ds(row0, group), b * BLOCK : (b + 1) * BLOCK] = rows
        return carry

    lax.fori_loop(0, lat_band // group, per_group, 0)
    points = base_ref[0] + lax.broadcasted_iota(jnp.int32, (lat_band, quarter), 1)
    out_ref[...] = jnp.where(points < limit_ref[...], out_ref[...], 0.0)


def surface_gather(slots, base, lat_points, tiles, quarter):
    lat_band = lat_points.shape[0]
    return pl.pallas_call(
        surface_kernel,
        in_specs=[
            pl.BlockSpec(memory_space=pltpu.SMEM),
            pl.BlockSpec(memory_space=pltpu.SMEM),
            pl.BlockSpec(memory_space=pltpu.VMEM),
            pl.BlockSpec(memory_space=pltpu.VMEM),
        ],
        out_specs=pl.BlockSpec(memory_space=pltpu.VMEM),
        out_shape=jax.ShapeDtypeStruct((lat_band, quarter), jnp.float32),
    )(slots, base, lat_points[:, None], tiles)


def body(
    atmos_fields,
    lat_points,
    wave_order,
    legendre,
    column_weight,
    block_remap,
    ocean_temp,
    ocean_salt,
    sea_mask,
):
    nfields, lev_dev, lat_band, lon_count = atmos_fields.shape
    wave_count = wave_order.shape[0]
    table, points = fourier_table(wave_order, lon_count)
    inverse_root = 1.0 / jnp.sqrt(lat_points.astype(jnp.float32))
    weights = jnp.where(
        2 * wave_order[None, :] < lat_points[:, None],
        inverse_root[:, None],
        jnp.zeros((), jnp.float32),
    )
    field_count = nfields
    ocean_rows, ocean_cols = ocean_temp.shape
    tile_count = ocean_rows * ocean_cols // BLOCK
    band_index = lax.axis_index(("lat", "ocn"))

    def slot_of(targets):
        return (targets // tile_count - band_index + 1) * tile_count + targets % tile_count

    local_slot = slot_of(block_remap.reshape(-1))
    quarter = lon_count // lax.axis_size("lev")
    full_remap = lev_gather(block_remap, 1)
    every_slot = slot_of(full_remap)
    raw_sums, sections = fused_transform(
        atmos_fields, lat_points, table, column_weight, every_slot, 3 * tile_count
    )
    raw_sums = raw_sums.reshape(field_count, lev_dev, lat_band, 2, wave_count)
    coeffs = (raw_sums * weights[None, None, :, None, :]).astype(jnp.bfloat16)
    regrouped = lax.all_to_all(
        coeffs.transpose(4, 1, 0, 3, 2).reshape(wave_count, lev_dev * field_count * 2, lat_band),
        ("lat", "ocn"),
        split_axis=0,
        concat_axis=2,
        tiled=True,
    )
    band_count = lax.axis_size(("lat", "ocn"))
    from_prev = lax.ppermute(
        sections[2], ("lat", "ocn"), [(i, i + 1) for i in range(band_count - 1)]
    )
    from_next = lax.ppermute(
        sections[0], ("lat", "ocn"), [(i + 1, i) for i in range(band_count - 1)]
    )
    arrived = (from_prev + sections[1]) + from_next
    tile_sums = lev_sum(arrived)
    forcing = (
        tile_sums.reshape(ocean_rows, ocean_cols // BLOCK, FIELDS, BLOCK)
        .transpose(2, 0, 1, 3)
        .reshape(FIELDS, ocean_rows, ocean_cols)
    )
    sea_cells = (
        jnp.broadcast_to(sea_mask[:, :, None], (ocean_rows, ocean_cols // BLOCK, BLOCK))
        .reshape(ocean_rows, ocean_cols)
        .astype(jnp.float32)
    )
    ocean_state = jnp.stack([ocean_temp, ocean_salt])
    padded = with_halo(ocean_state, ((("lat", "ocn"), 1),), 1)
    laplace = (
        padded[:, 2:]
        + padded[:, :-2]
        + jnp.roll(ocean_state, 1, 2)
        + jnp.roll(ocean_state, -1, 2)
        - 4.0 * ocean_state
    )
    updated = ocean_state + DIFFUSION * laplace + COUPLING * sea_cells[None] * forcing
    temp_next = updated[0]
    salt_next = updated[1]
    returned = with_halo(temp_next, ((("lat", "ocn"), 0),), ocean_rows)
    tiles_near = returned.reshape(3 * tile_count, BLOCK)
    base = (lax.axis_index("lev") * quarter).astype(jnp.int32).reshape(1)
    surface_temp = surface_gather(local_slot, base, lat_points, tiles_near, quarter)
    if lax.axis_size("lev") == 4:
        pair = lev_pair_far(regrouped)
        pair, surface_temp = lax.optimization_barrier((pair, surface_temp))
        gathered = lev_pair_near(pair, regrouped.shape[1])
    else:
        gathered = lev_gather(regrouped, 1)
    spectra = jnp.einsum(
        "srj,sjd->srd",
        gathered,
        legendre,
        preferred_element_type=jnp.float32,
    )
    return (spectra, temp_next, salt_next, surface_temp)


def solution(mesh):
    placed = (
        P(None, "lev", ("lat", "ocn"), None),
        P(("lat", "ocn")),
        P(),
        P(("lat", "ocn"), None, "lev"),
        P(None, "lev"),
        P(("lat", "ocn"), "lev"),
        P(("lat", "ocn"), None),
        P(("lat", "ocn"), None),
        P(("lat", "ocn"), None),
    )
    return jax.shard_map(
        body,
        mesh=mesh,
        in_specs=placed,
        out_specs=(
            P(("lat", "ocn"), None, "lev"),
            P(("lat", "ocn"), None),
            P(("lat", "ocn"), None),
            P(("lat", "ocn"), "lev"),
        ),
        check_vma=False,
    )
```

```python
import math

import jax
import jax.numpy as jnp
from jax import lax
from jax.experimental import pallas as pl
from jax.experimental.pallas import tpu as pltpu
from jax.sharding import PartitionSpec as P

FIELDS = 2
BLOCK = 128


FULL_TURN = 2.0 * math.pi
DIFFUSION = 0.2
COUPLING = 0.5


def with_halo(cells, sides, width):
    for axis, dim in sides:
        count = lax.axis_size(axis)
        ends = count - 1
        head = lax.slice_in_dim(cells, 0, width, axis=dim)
        tail = lax.slice_in_dim(cells, cells.shape[dim] - width, cells.shape[dim], axis=dim)
        cells = jnp.concatenate(
            [
                lax.ppermute(tail, axis, [(i, (i + 1) % count) for i in range(ends)]),
                cells,
                lax.ppermute(head, axis, [((i + 1) % count, i) for i in range(ends)]),
            ],
            axis=dim,
        )
    return cells


def fourier_table(wave_order, length):
    points = jnp.arange(length, dtype=jnp.int32)
    phase = wave_order[:, None] * points[None, :] % length
    angle = phase.astype(jnp.float32) * (FULL_TURN / length)
    table = jnp.concatenate([jnp.cos(angle), -jnp.sin(angle)], axis=0).astype(jnp.bfloat16)
    return (table, points)


def lev_sum(values):
    count = lax.axis_size("lev")
    if count & (count - 1):
        return lax.psum(values, "lev")
    stride = 1
    while stride < count:
        values = values + lax.ppermute(values, "lev", [(i, i ^ stride) for i in range(count)])
        stride *= 2
    return values


def lev_gather(values, axis):
    count = lax.axis_size("lev")
    if count & (count - 1):
        return lax.all_gather(values, "lev", axis=axis, tiled=True)
    index = lax.axis_index("lev")
    stride = 1
    while stride < count:
        other = lax.ppermute(values, "lev", [(i, i ^ stride) for i in range(count)])
        upper = (index // stride) % 2 == 1
        values = jnp.where(
            upper,
            jnp.concatenate([other, values], axis=axis),
            jnp.concatenate([values, other], axis=axis),
        )
        stride *= 2
    return values


def row_block(rows):
    for size in (64, 32, 16):
        if rows % size == 0:
            return size
    return rows


def transform_kernel(
    points_ref, cells_ref, table_ref, weight_ref, slot_ref, scale_ref, sums_ref, out_ref, acc_ref, *scratch
):
    step = pl.program_id(0)

    @pl.when(step == 0)
    def _():
        acc_ref[...] = jnp.zeros_like(acc_ref)

    nfields, nlev, rows, lon_count = cells_ref.shape
    nslot = acc_ref.shape[0]
    nblocks = lon_count // BLOCK
    table = table_ref[...]
    keep = (lax.broadcasted_iota(jnp.int32, (rows, lon_count), 1) < points_ref[...]).astype(jnp.bfloat16)
    cells = cells_ref[...] * keep[None, None]
    if rows % 16 == 0:
        sums = lax.dot_general(
            cells.reshape(nfields * nlev * rows, lon_count),
            table,
            (((1,), (1,)), ((), ())),
            preferred_element_type=jnp.float32,
        )
        sums_ref[...] = (sums.reshape(sums_ref.shape) * scale_ref[...][None, None]).astype(sums_ref.dtype)
    else:
        for f in range(nfields):
            for l in range(nlev):
                sums_ref[f, l] = (
                    lax.dot_general(
                        cells[f, l], table, (((1,), (1,)), ((), ())), preferred_element_type=jnp.float32
                    )
                    * scale_ref[...]
                ).astype(sums_ref.dtype)
    pieces = []
    for f in range(nfields):
        flux = weight_ref[f, 0] * cells[f, 0].astype(jnp.float32)
        for l in range(1, nlev):
            flux = flux + weight_ref[f, l] * cells[f, l].astype(jnp.float32)
        high = flux.astype(jnp.bfloat16)
        pieces.append(high)
        pieces.append((flux - high.astype(jnp.float32)).astype(jnp.bfloat16))
    if scratch:
        (stacked_ref,) = scratch
        for b in range(nblocks):
            for p, piece in enumerate(pieces):
                stacked_ref[b * rows : (b + 1) * rows, p * BLOCK : (p + 1) * BLOCK] = piece[
                    :, b * BLOCK : (b + 1) * BLOCK
                ]
        stacked = stacked_ref[...]
    else:
        stacked = jnp.concatenate(
            [
                jnp.concatenate(
                    [p[:, b * BLOCK : (b + 1) * BLOCK].astype(jnp.float32) for p in pieces], axis=1
                )
                for b in range(nblocks)
            ],
            axis=0,
        ).astype(jnp.bfloat16)
    onehot = (
        lax.broadcasted_iota(jnp.int32, (nslot, nblocks * rows), 0) == slot_ref[0]
    ).astype(jnp.bfloat16)
    acc_ref[...] += jnp.dot(onehot, stacked, preferred_element_type=jnp.float32)

    @pl.when(step == pl.num_programs(0) - 1)
    def _():
        nsec, tiles, _ = out_ref.shape
        for s in range(nsec):
            for f in range(nfields):
                high = acc_ref[s * tiles : (s + 1) * tiles, 2 * f * BLOCK : (2 * f + 1) * BLOCK]
                low = acc_ref[s * tiles : (s + 1) * tiles, (2 * f + 1) * BLOCK : (2 * f + 2) * BLOCK]
                out_ref[s, :, f * BLOCK : (f + 1) * BLOCK] = high + low


def fused_transform(atmos_fields, lat_points, table, column_weight, slots, scale, nslot):
    nfields, nlev, lat_band, lon_count = atmos_fields.shape
    rows = row_block(lat_band)
    steps = lat_band // rows
    nblocks = lon_count // BLOCK
    wave2 = table.shape[0]
    slot_rows = slots.reshape(steps, rows, nblocks).transpose(0, 2, 1).reshape(steps, 1, nblocks * rows)
    scratch = [pltpu.VMEM((nslot, 2 * nfields * BLOCK), jnp.float32)]
    if rows % 16 == 0:
        scratch.append(pltpu.VMEM((nblocks * rows, 2 * nfields * BLOCK), jnp.bfloat16))
    return pl.pallas_call(
        transform_kernel,
        grid=(steps,),
        in_specs=[
            pl.BlockSpec((rows, 1), lambda r: (r, 0)),
            pl.BlockSpec((nfields, nlev, rows, lon_count), lambda r: (0, 0, r, 0)),
            pl.BlockSpec((wave2, lon_count), lambda r: (0, 0)),
            pl.BlockSpec(memory_space=pltpu.SMEM),
            pl.BlockSpec((1, 1, nblocks * rows), lambda r: (r, 0, 0)),
            pl.BlockSpec((rows, wave2), lambda r: (r, 0)),
        ],
        out_specs=[
            pl.BlockSpec((nfields, nlev, rows, wave2), lambda r: (0, 0, r, 0)),
            pl.BlockSpec((3, nslot // 3, nfields * BLOCK), lambda r: (0, 0, 0)),
        ],
        out_shape=[
            jax.ShapeDtypeStruct((nfields, nlev, lat_band, wave2), jnp.bfloat16),
            jax.ShapeDtypeStruct((3, nslot // 3, nfields * BLOCK), jnp.float32),
        ],
        scratch_shapes=scratch,
        compiler_params=pltpu.CompilerParams(dimension_semantics=("arbitrary",)),
    )(lat_points[:, None], atmos_fields, table, column_weight.astype(jnp.float32), slot_rows, scale)


def surface_kernel(slot_ref, base_ref, limit_ref, tiles_ref, out_ref):
    lat_band, quarter = out_ref.shape
    nquarter = quarter // BLOCK
    group = 8
    sublane = lax.broadcasted_iota(jnp.int32, (group, BLOCK), 0)

    def per_group(g, carry):
        row0 = pl.multiple_of(g * group, group)
        for b in range(nquarter):
            rows = jnp.zeros((group, BLOCK), jnp.float32)
            for r in range(group):
                tile = slot_ref[(row0 + r) * nquarter + b]
                picked = jnp.broadcast_to(tiles_ref[pl.ds(tile, 1), :], (group, BLOCK))
                rows = jnp.where(sublane == r, picked, rows)
            out_ref[pl.ds(row0, group), b * BLOCK : (b + 1) * BLOCK] = rows
        return carry

    lax.fori_loop(0, lat_band // group, per_group, 0)
    points = base_ref[0] + lax.broadcasted_iota(jnp.int32, (lat_band, quarter), 1)
    out_ref[...] = jnp.where(points < limit_ref[...], out_ref[...], 0.0)


def surface_gather(slots, base, lat_points, tiles, quarter):
    lat_band = lat_points.shape[0]
    return pl.pallas_call(
        surface_kernel,
        in_specs=[
            pl.BlockSpec(memory_space=pltpu.SMEM),
            pl.BlockSpec(memory_space=pltpu.SMEM),
            pl.BlockSpec(memory_space=pltpu.VMEM),
            pl.BlockSpec(memory_space=pltpu.VMEM),
        ],
        out_specs=pl.BlockSpec(memory_space=pltpu.VMEM),
        out_shape=jax.ShapeDtypeStruct((lat_band, quarter), jnp.float32),
    )(slots, base, lat_points[:, None], tiles)


def body(
    atmos_fields,
    lat_points,
    wave_order,
    legendre,
    column_weight,
    block_remap,
    ocean_temp,
    ocean_salt,
    sea_mask,
):
    nfields, lev_dev, lat_band, lon_count = atmos_fields.shape
    wave_count = wave_order.shape[0]
    table, points = fourier_table(wave_order, lon_count)
    inverse_root = 1.0 / jnp.sqrt(lat_points.astype(jnp.float32))
    weights = jnp.where(
        2 * wave_order[None, :] < lat_points[:, None],
        inverse_root[:, None],
        jnp.zeros((), jnp.float32),
    )
    field_count = nfields
    ocean_rows, ocean_cols = ocean_temp.shape
    tile_count = ocean_rows * ocean_cols // BLOCK
    band_index = lax.axis_index(("lat", "ocn"))

    def slot_of(targets):
        return (targets // tile_count - band_index + 1) * tile_count + targets % tile_count

    local_slot = slot_of(block_remap.reshape(-1))
    quarter = lon_count // lax.axis_size("lev")
    full_remap = lev_gather(block_remap, 1)
    every_slot = slot_of(full_remap)
    raw_sums, sections = fused_transform(
        atmos_fields,
        lat_points,
        table,
        column_weight,
        every_slot,
        jnp.concatenate([weights, weights], axis=1),
        3 * tile_count,
    )
    raw_sums = raw_sums.reshape(field_count, lev_dev, lat_band, 2, wave_count)
    coeffs = raw_sums
    regrouped = lax.all_to_all(
        coeffs.transpose(4, 1, 0, 3, 2).reshape(wave_count, lev_dev * field_count * 2, lat_band),
        ("lat", "ocn"),
        split_axis=0,
        concat_axis=2,
        tiled=True,
    )
    spectra = jnp.einsum(
        "srj,sjd->srd",
        lev_gather(regrouped, 1),
        legendre,
        preferred_element_type=jnp.float32,
    )
    band_count = lax.axis_size(("lat", "ocn"))
    from_prev = lax.ppermute(
        sections[2], ("lat", "ocn"), [(i, i + 1) for i in range(band_count - 1)]
    )
    from_next = lax.ppermute(
        sections[0], ("lat", "ocn"), [(i + 1, i) for i in range(band_count - 1)]
    )
    arrived = (from_prev + sections[1]) + from_next
    tile_sums = lev_sum(arrived)
    forcing = (
        tile_sums.reshape(ocean_rows, ocean_cols // BLOCK, FIELDS, BLOCK)
        .transpose(2, 0, 1, 3)
        .reshape(FIELDS, ocean_rows, ocean_cols)
    )
    sea_cells = (
        jnp.broadcast_to(sea_mask[:, :, None], (ocean_rows, ocean_cols // BLOCK, BLOCK))
        .reshape(ocean_rows, ocean_cols)
        .astype(jnp.float32)
    )
    ocean_state = jnp.stack([ocean_temp, ocean_salt])
    padded = with_halo(ocean_state, ((("lat", "ocn"), 1),), 1)
    laplace = (
        padded[:, 2:]
        + padded[:, :-2]
        + jnp.roll(ocean_state, 1, 2)
        + jnp.roll(ocean_state, -1, 2)
        - 4.0 * ocean_state
    )
    updated = ocean_state + DIFFUSION * laplace + COUPLING * sea_cells[None] * forcing
    temp_next = updated[0]
    salt_next = updated[1]
    returned = with_halo(temp_next, ((("lat", "ocn"), 0),), ocean_rows)
    tiles_near = returned.reshape(3 * tile_count, BLOCK)
    base = (lax.axis_index("lev") * quarter).astype(jnp.int32).reshape(1)
    surface_temp = surface_gather(local_slot, base, lat_points, tiles_near, quarter)
    return (spectra, temp_next, salt_next, surface_temp)


def solution(mesh):
    placed = (
        P(None, "lev", ("lat", "ocn"), None),
        P(("lat", "ocn")),
        P(),
        P(("lat", "ocn"), None, "lev"),
        P(None, "lev"),
        P(("lat", "ocn"), "lev"),
        P(("lat", "ocn"), None),
        P(("lat", "ocn"), None),
        P(("lat", "ocn"), None),
    )
    return jax.shard_map(
        body,
        mesh=mesh,
        in_specs=placed,
        out_specs=(
            P(("lat", "ocn"), None, "lev"),
            P(("lat", "ocn"), None),
            P(("lat", "ocn"), None),
            P(("lat", "ocn"), "lev"),
        ),
        check_vma=False,
    )
```

```python
import math

import jax
import jax.numpy as jnp
from jax import lax
from jax.experimental import pallas as pl
from jax.experimental.pallas import tpu as pltpu
from jax.sharding import PartitionSpec as P

FIELDS = 2
BLOCK = 128


FULL_TURN = 2.0 * math.pi
DIFFUSION = 0.2
COUPLING = 0.5


def with_halo(cells, sides, width):
    for axis, dim in sides:
        count = lax.axis_size(axis)
        ends = count - 1
        head = lax.slice_in_dim(cells, 0, width, axis=dim)
        tail = lax.slice_in_dim(cells, cells.shape[dim] - width, cells.shape[dim], axis=dim)
        cells = jnp.concatenate(
            [
                lax.ppermute(tail, axis, [(i, (i + 1) % count) for i in range(ends)]),
                cells,
                lax.ppermute(head, axis, [((i + 1) % count, i) for i in range(ends)]),
            ],
            axis=dim,
        )
    return cells


def fourier_table(wave_order, length):
    points = jnp.arange(length, dtype=jnp.int32)
    phase = wave_order[:, None] * points[None, :] % length
    angle = phase.astype(jnp.float32) * (FULL_TURN / length)
    table = jnp.concatenate([jnp.cos(angle), -jnp.sin(angle)], axis=0).astype(jnp.bfloat16)
    return (table, points)


def lev_sum(values):
    count = lax.axis_size("lev")
    if count != 4 or values.shape[0] % 16:
        return lax.psum(values, "lev")
    index = lax.axis_index("lev")
    half = values.shape[0] // 2
    top, bottom = values[:half], values[half:]
    odd = index % 2 == 1
    kept = jnp.where(odd, bottom, top)
    sent = jnp.where(odd, top, bottom)
    pairs_near = [(i, i ^ 1) for i in range(count)]
    kept = kept + lax.ppermute(sent, "lev", pairs_near)
    kept = kept + lax.ppermute(kept, "lev", [(i, i ^ 2) for i in range(count)])
    other = lax.ppermute(kept, "lev", pairs_near)
    return jnp.where(
        odd,
        jnp.concatenate([other, kept], axis=0),
        jnp.concatenate([kept, other], axis=0),
    )


def lev_gather(values, axis):
    count = lax.axis_size("lev")
    if count & (count - 1):
        return lax.all_gather(values, "lev", axis=axis, tiled=True)
    index = lax.axis_index("lev")
    stride = 1
    while stride < count:
        other = lax.ppermute(values, "lev", [(i, i ^ stride) for i in range(count)])
        upper = (index // stride) % 2 == 1
        values = jnp.where(
            upper,
            jnp.concatenate([other, values], axis=axis),
            jnp.concatenate([values, other], axis=axis),
        )
        stride *= 2
    return values


def row_block(rows):
    for size in (64, 32, 16):
        if rows % size == 0:
            return size
    return rows


def transform_kernel(
    points_ref, cells_ref, table_ref, weight_ref, slot_ref, scale_ref, sums_ref, out_ref, acc_ref, *scratch
):
    step = pl.program_id(0)

    @pl.when(step == 0)
    def _():
        acc_ref[...] = jnp.zeros_like(acc_ref)

    nfields, nlev, rows, lon_count = cells_ref.shape
    nslot = acc_ref.shape[0]
    nblocks = lon_count // BLOCK
    table = table_ref[...]
    keep = (lax.broadcasted_iota(jnp.int32, (rows, lon_count), 1) < points_ref[...]).astype(jnp.bfloat16)
    cells = cells_ref[...] * keep[None, None]
    if rows % 16 == 0:
        sums = lax.dot_general(
            cells.reshape(nfields * nlev * rows, lon_count),
            table,
            (((1,), (1,)), ((), ())),
            preferred_element_type=jnp.float32,
        )
        sums_ref[...] = (sums.reshape(sums_ref.shape) * scale_ref[...][None, None]).astype(sums_ref.dtype)
    else:
        for f in range(nfields):
            for l in range(nlev):
                sums_ref[f, l] = (
                    lax.dot_general(
                        cells[f, l], table, (((1,), (1,)), ((), ())), preferred_element_type=jnp.float32
                    )
                    * scale_ref[...]
                ).astype(sums_ref.dtype)
    pieces = []
    for f in range(nfields):
        flux = weight_ref[f, 0] * cells[f, 0].astype(jnp.float32)
        for l in range(1, nlev):
            flux = flux + weight_ref[f, l] * cells[f, l].astype(jnp.float32)
        high = flux.astype(jnp.bfloat16)
        pieces.append(high)
        pieces.append((flux - high.astype(jnp.float32)).astype(jnp.bfloat16))
    if scratch:
        (stacked_ref,) = scratch
        for b in range(nblocks):
            for p, piece in enumerate(pieces):
                stacked_ref[b * rows : (b + 1) * rows, p * BLOCK : (p + 1) * BLOCK] = piece[
                    :, b * BLOCK : (b + 1) * BLOCK
                ]
        stacked = stacked_ref[...]
    else:
        stacked = jnp.concatenate(
            [
                jnp.concatenate(
                    [p[:, b * BLOCK : (b + 1) * BLOCK].astype(jnp.float32) for p in pieces], axis=1
                )
                for b in range(nblocks)
            ],
            axis=0,
        ).astype(jnp.bfloat16)
    onehot = (
        lax.broadcasted_iota(jnp.int32, (nslot, nblocks * rows), 0) == slot_ref[0]
    ).astype(jnp.bfloat16)
    acc_ref[...] += jnp.dot(onehot, stacked, preferred_element_type=jnp.float32)

    @pl.when(step == pl.num_programs(0) - 1)
    def _():
        nsec, tiles, _ = out_ref.shape
        for s in range(nsec):
            for f in range(nfields):
                high = acc_ref[s * tiles : (s + 1) * tiles, 2 * f * BLOCK : (2 * f + 1) * BLOCK]
                low = acc_ref[s * tiles : (s + 1) * tiles, (2 * f + 1) * BLOCK : (2 * f + 2) * BLOCK]
                out_ref[s, :, f * BLOCK : (f + 1) * BLOCK] = high + low


def fused_transform(atmos_fields, lat_points, table, column_weight, slots, scale, nslot):
    nfields, nlev, lat_band, lon_count = atmos_fields.shape
    rows = row_block(lat_band)
    steps = lat_band // rows
    nblocks = lon_count // BLOCK
    wave2 = table.shape[0]
    slot_rows = slots.reshape(steps, rows, nblocks).transpose(0, 2, 1).reshape(steps, 1, nblocks * rows)
    scratch = [pltpu.VMEM((nslot, 2 * nfields * BLOCK), jnp.float32)]
    if rows % 16 == 0:
        scratch.append(pltpu.VMEM((nblocks * rows, 2 * nfields * BLOCK), jnp.bfloat16))
    return pl.pallas_call(
        transform_kernel,
        grid=(steps,),
        in_specs=[
            pl.BlockSpec((rows, 1), lambda r: (r, 0)),
            pl.BlockSpec((nfields, nlev, rows, lon_count), lambda r: (0, 0, r, 0)),
            pl.BlockSpec((wave2, lon_count), lambda r: (0, 0)),
            pl.BlockSpec(memory_space=pltpu.SMEM),
            pl.BlockSpec((1, 1, nblocks * rows), lambda r: (r, 0, 0)),
            pl.BlockSpec((rows, wave2), lambda r: (r, 0)),
        ],
        out_specs=[
            pl.BlockSpec((nfields, nlev, rows, wave2), lambda r: (0, 0, r, 0)),
            pl.BlockSpec((3, nslot // 3, nfields * BLOCK), lambda r: (0, 0, 0)),
        ],
        out_shape=[
            jax.ShapeDtypeStruct((nfields, nlev, lat_band, wave2), jnp.bfloat16),
            jax.ShapeDtypeStruct((3, nslot // 3, nfields * BLOCK), jnp.float32),
        ],
        scratch_shapes=scratch,
        compiler_params=pltpu.CompilerParams(dimension_semantics=("arbitrary",)),
    )(lat_points[:, None], atmos_fields, table, column_weight.astype(jnp.float32), slot_rows, scale)


def surface_kernel(slot_ref, base_ref, limit_ref, tiles_ref, out_ref):
    lat_band, quarter = out_ref.shape
    nquarter = quarter // BLOCK
    group = 8
    sublane = lax.broadcasted_iota(jnp.int32, (group, BLOCK), 0)

    def per_group(g, carry):
        row0 = pl.multiple_of(g * group, group)
        for b in range(nquarter):
            rows = jnp.zeros((group, BLOCK), jnp.float32)
            for r in range(group):
                tile = slot_ref[(row0 + r) * nquarter + b]
                picked = jnp.broadcast_to(tiles_ref[pl.ds(tile, 1), :], (group, BLOCK))
                rows = jnp.where(sublane == r, picked, rows)
            out_ref[pl.ds(row0, group), b * BLOCK : (b + 1) * BLOCK] = rows
        return carry

    lax.fori_loop(0, lat_band // group, per_group, 0)
    points = base_ref[0] + lax.broadcasted_iota(jnp.int32, (lat_band, quarter), 1)
    out_ref[...] = jnp.where(points < limit_ref[...], out_ref[...], 0.0)


def surface_gather(slots, base, lat_points, tiles, quarter):
    lat_band = lat_points.shape[0]
    return pl.pallas_call(
        surface_kernel,
        in_specs=[
            pl.BlockSpec(memory_space=pltpu.SMEM),
            pl.BlockSpec(memory_space=pltpu.SMEM),
            pl.BlockSpec(memory_space=pltpu.VMEM),
            pl.BlockSpec(memory_space=pltpu.VMEM),
        ],
        out_specs=pl.BlockSpec(memory_space=pltpu.VMEM),
        out_shape=jax.ShapeDtypeStruct((lat_band, quarter), jnp.float32),
    )(slots, base, lat_points[:, None], tiles)


def body(
    atmos_fields,
    lat_points,
    wave_order,
    legendre,
    column_weight,
    block_remap,
    ocean_temp,
    ocean_salt,
    sea_mask,
):
    nfields, lev_dev, lat_band, lon_count = atmos_fields.shape
    wave_count = wave_order.shape[0]
    table, points = fourier_table(wave_order, lon_count)
    inverse_root = 1.0 / jnp.sqrt(lat_points.astype(jnp.float32))
    weights = jnp.where(
        2 * wave_order[None, :] < lat_points[:, None],
        inverse_root[:, None],
        jnp.zeros((), jnp.float32),
    )
    field_count = nfields
    ocean_rows, ocean_cols = ocean_temp.shape
    tile_count = ocean_rows * ocean_cols // BLOCK
    band_index = lax.axis_index(("lat", "ocn"))

    def slot_of(targets):
        return (targets // tile_count - band_index + 1) * tile_count + targets % tile_count

    local_slot = slot_of(block_remap.reshape(-1))
    quarter = lon_count // lax.axis_size("lev")
    full_remap = lev_gather(block_remap, 1)
    every_slot = slot_of(full_remap)
    raw_sums, sections = fused_transform(
        atmos_fields,
        lat_points,
        table,
        column_weight,
        every_slot,
        jnp.concatenate([weights, weights], axis=1),
        3 * tile_count,
    )
    raw_sums = raw_sums.reshape(field_count, lev_dev, lat_band, 2, wave_count)
    coeffs = raw_sums
    regrouped = lax.all_to_all(
        coeffs.transpose(4, 1, 0, 3, 2).reshape(wave_count, lev_dev * field_count * 2, lat_band),
        ("lat", "ocn"),
        split_axis=0,
        concat_axis=2,
        tiled=True,
    )
    spectra = jnp.einsum(
        "srj,sjd->srd",
        lev_gather(regrouped, 1),
        legendre,
        preferred_element_type=jnp.float32,
    )
    band_count = lax.axis_size(("lat", "ocn"))
    from_prev = lax.ppermute(
        sections[2], ("lat", "ocn"), [(i, i + 1) for i in range(band_count - 1)]
    )
    from_next = lax.ppermute(
        sections[0], ("lat", "ocn"), [(i + 1, i) for i in range(band_count - 1)]
    )
    arrived = (from_prev + sections[1]) + from_next
    tile_sums = lev_sum(arrived)
    forcing = (
        tile_sums.reshape(ocean_rows, ocean_cols // BLOCK, FIELDS, BLOCK)
        .transpose(2, 0, 1, 3)
        .reshape(FIELDS, ocean_rows, ocean_cols)
    )
    sea_cells = (
        jnp.broadcast_to(sea_mask[:, :, None], (ocean_rows, ocean_cols // BLOCK, BLOCK))
        .reshape(ocean_rows, ocean_cols)
        .astype(jnp.float32)
    )
    ocean_state = jnp.stack([ocean_temp, ocean_salt])
    padded = with_halo(ocean_state, ((("lat", "ocn"), 1),), 1)
    laplace = (
        padded[:, 2:]
        + padded[:, :-2]
        + jnp.roll(ocean_state, 1, 2)
        + jnp.roll(ocean_state, -1, 2)
        - 4.0 * ocean_state
    )
    updated = ocean_state + DIFFUSION * laplace + COUPLING * sea_cells[None] * forcing
    temp_next = updated[0]
    salt_next = updated[1]
    returned = with_halo(temp_next, ((("lat", "ocn"), 0),), ocean_rows)
    tiles_near = returned.reshape(3 * tile_count, BLOCK)
    base = (lax.axis_index("lev") * quarter).astype(jnp.int32).reshape(1)
    surface_temp = surface_gather(local_slot, base, lat_points, tiles_near, quarter)
    return (spectra, temp_next, salt_next, surface_temp)


def solution(mesh):
    placed = (
        P(None, "lev", ("lat", "ocn"), None),
        P(("lat", "ocn")),
        P(),
        P(("lat", "ocn"), None, "lev"),
        P(None, "lev"),
        P(("lat", "ocn"), "lev"),
        P(("lat", "ocn"), None),
        P(("lat", "ocn"), None),
        P(("lat", "ocn"), None),
    )
    return jax.shard_map(
        body,
        mesh=mesh,
        in_specs=placed,
        out_specs=(
            P(("lat", "ocn"), None, "lev"),
            P(("lat", "ocn"), None),
            P(("lat", "ocn"), None),
            P(("lat", "ocn"), "lev"),
        ),
        check_vma=False,
    )
```

```python
import math

import jax
import jax.numpy as jnp
from jax import lax
from jax.experimental import pallas as pl
from jax.experimental.pallas import tpu as pltpu
from jax.sharding import PartitionSpec as P

FIELDS = 2
BLOCK = 128


FULL_TURN = 2.0 * math.pi
DIFFUSION = 0.2
COUPLING = 0.5


def with_halo(cells, sides, width):
    for axis, dim in sides:
        count = lax.axis_size(axis)
        ends = count - 1
        head = lax.slice_in_dim(cells, 0, width, axis=dim)
        tail = lax.slice_in_dim(cells, cells.shape[dim] - width, cells.shape[dim], axis=dim)
        cells = jnp.concatenate(
            [
                lax.ppermute(tail, axis, [(i, (i + 1) % count) for i in range(ends)]),
                cells,
                lax.ppermute(head, axis, [((i + 1) % count, i) for i in range(ends)]),
            ],
            axis=dim,
        )
    return cells


def fourier_table(wave_order, length):
    points = jnp.arange(length, dtype=jnp.int32)
    phase = wave_order[:, None] * points[None, :] % length
    angle = phase.astype(jnp.float32) * (FULL_TURN / length)
    table = jnp.concatenate([jnp.cos(angle), -jnp.sin(angle)], axis=0).astype(jnp.bfloat16)
    return (table, points)


def lev_sum(values):
    count = lax.axis_size("lev")
    if count & (count - 1):
        return lax.psum(values, "lev")
    stride = 1
    while stride < count:
        values = values + lax.ppermute(values, "lev", [(i, i ^ stride) for i in range(count)])
        stride *= 2
    return values


def lev_gather(values, axis):
    count = lax.axis_size("lev")
    if count & (count - 1):
        return lax.all_gather(values, "lev", axis=axis, tiled=True)
    index = lax.axis_index("lev")
    stride = 1
    while stride < count:
        other = lax.ppermute(values, "lev", [(i, i ^ stride) for i in range(count)])
        upper = (index // stride) % 2 == 1
        values = jnp.where(
            upper,
            jnp.concatenate([other, values], axis=axis),
            jnp.concatenate([values, other], axis=axis),
        )
        stride *= 2
    return values


def row_block(rows):
    for size in (64, 32, 16):
        if rows % size == 0:
            return size
    return rows


def transform_kernel(
    points_ref, cells_ref, table_ref, weight_ref, slot_ref, scale_ref, sums_ref, out_ref, acc_ref, *scratch
):
    step = pl.program_id(0)

    @pl.when(step == 0)
    def _():
        acc_ref[...] = jnp.zeros_like(acc_ref)

    nfields, nlev, rows, lon_count = cells_ref.shape
    nslot = acc_ref.shape[0]
    nblocks = lon_count // BLOCK
    table = table_ref[...]
    keep = (lax.broadcasted_iota(jnp.int32, (rows, lon_count), 1) < points_ref[...]).astype(jnp.bfloat16)
    cells = cells_ref[...] * keep[None, None]
    if rows % 16 == 0:
        sums = lax.dot_general(
            cells.reshape(nfields * nlev * rows, lon_count),
            table,
            (((1,), (1,)), ((), ())),
            preferred_element_type=jnp.float32,
        )
        sums_ref[...] = (sums.reshape(sums_ref.shape) * scale_ref[...][None, None]).astype(sums_ref.dtype)
    else:
        for f in range(nfields):
            for l in range(nlev):
                sums_ref[f, l] = (
                    lax.dot_general(
                        cells[f, l], table, (((1,), (1,)), ((), ())), preferred_element_type=jnp.float32
                    )
                    * scale_ref[...]
                ).astype(sums_ref.dtype)
    pieces = []
    for f in range(nfields):
        flux = weight_ref[f, 0] * cells[f, 0].astype(jnp.float32)
        for l in range(1, nlev):
            flux = flux + weight_ref[f, l] * cells[f, l].astype(jnp.float32)
        high = flux.astype(jnp.bfloat16)
        pieces.append(high)
        pieces.append((flux - high.astype(jnp.float32)).astype(jnp.bfloat16))
    if scratch:
        (stacked_ref,) = scratch
        for b in range(nblocks):
            for p, piece in enumerate(pieces):
                stacked_ref[b * rows : (b + 1) * rows, p * BLOCK : (p + 1) * BLOCK] = piece[
                    :, b * BLOCK : (b + 1) * BLOCK
                ]
        stacked = stacked_ref[...]
    else:
        stacked = jnp.concatenate(
            [
                jnp.concatenate(
                    [p[:, b * BLOCK : (b + 1) * BLOCK].astype(jnp.float32) for p in pieces], axis=1
                )
                for b in range(nblocks)
            ],
            axis=0,
        ).astype(jnp.bfloat16)
    onehot = (
        lax.broadcasted_iota(jnp.int32, (nslot, nblocks * rows), 0) == slot_ref[0]
    ).astype(jnp.bfloat16)
    acc_ref[...] += jnp.dot(onehot, stacked, preferred_element_type=jnp.float32)

    @pl.when(step == pl.num_programs(0) - 1)
    def _():
        nsec, tiles, _ = out_ref.shape
        for s in range(nsec):
            for f in range(nfields):
                high = acc_ref[s * tiles : (s + 1) * tiles, 2 * f * BLOCK : (2 * f + 1) * BLOCK]
                low = acc_ref[s * tiles : (s + 1) * tiles, (2 * f + 1) * BLOCK : (2 * f + 2) * BLOCK]
                out_ref[s, :, f * BLOCK : (f + 1) * BLOCK] = high + low


def fused_transform(atmos_fields, lat_points, table, column_weight, slots, scale, nslot):
    nfields, nlev, lat_band, lon_count = atmos_fields.shape
    rows = row_block(lat_band)
    steps = lat_band // rows
    nblocks = lon_count // BLOCK
    wave2 = table.shape[0]
    slot_rows = slots.reshape(steps, rows, nblocks).transpose(0, 2, 1).reshape(steps, 1, nblocks * rows)
    scratch = [pltpu.VMEM((nslot, 2 * nfields * BLOCK), jnp.float32)]
    if rows % 16 == 0:
        scratch.append(pltpu.VMEM((nblocks * rows, 2 * nfields * BLOCK), jnp.bfloat16))
    return pl.pallas_call(
        transform_kernel,
        grid=(steps,),
        in_specs=[
            pl.BlockSpec((rows, 1), lambda r: (r, 0)),
            pl.BlockSpec((nfields, nlev, rows, lon_count), lambda r: (0, 0, r, 0)),
            pl.BlockSpec((wave2, lon_count), lambda r: (0, 0)),
            pl.BlockSpec(memory_space=pltpu.SMEM),
            pl.BlockSpec((1, 1, nblocks * rows), lambda r: (r, 0, 0)),
            pl.BlockSpec((rows, wave2), lambda r: (r, 0)),
        ],
        out_specs=[
            pl.BlockSpec((nfields, nlev, rows, wave2), lambda r: (0, 0, r, 0)),
            pl.BlockSpec((3, nslot // 3, nfields * BLOCK), lambda r: (0, 0, 0)),
        ],
        out_shape=[
            jax.ShapeDtypeStruct((nfields, nlev, lat_band, wave2), jnp.bfloat16),
            jax.ShapeDtypeStruct((3, nslot // 3, nfields * BLOCK), jnp.float32),
        ],
        scratch_shapes=scratch,
        compiler_params=pltpu.CompilerParams(dimension_semantics=("arbitrary",)),
    )(lat_points[:, None], atmos_fields, table, column_weight.astype(jnp.float32), slot_rows, scale)


def surface_kernel(slot_ref, base_ref, limit_ref, tiles_ref, out_ref):
    lat_band, quarter = out_ref.shape
    nquarter = quarter // BLOCK
    group = 8
    sublane = lax.broadcasted_iota(jnp.int32, (group, BLOCK), 0)

    def per_group(g, carry):
        row0 = pl.multiple_of(g * group, group)
        for b in range(nquarter):
            rows = jnp.zeros((group, BLOCK), jnp.float32)
            for r in range(group):
                tile = slot_ref[(row0 + r) * nquarter + b]
                picked = jnp.broadcast_to(tiles_ref[pl.ds(tile, 1), :], (group, BLOCK))
                rows = jnp.where(sublane == r, picked, rows)
            out_ref[pl.ds(row0, group), b * BLOCK : (b + 1) * BLOCK] = rows
        return carry

    lax.fori_loop(0, lat_band // group, per_group, 0, unroll=2 if (lat_band // group) % 2 == 0 else 1)
    points = base_ref[0] + lax.broadcasted_iota(jnp.int32, (lat_band, quarter), 1)
    out_ref[...] = jnp.where(points < limit_ref[...], out_ref[...], 0.0)


def surface_gather(slots, base, lat_points, tiles, quarter):
    lat_band = lat_points.shape[0]
    return pl.pallas_call(
        surface_kernel,
        in_specs=[
            pl.BlockSpec(memory_space=pltpu.SMEM),
            pl.BlockSpec(memory_space=pltpu.SMEM),
            pl.BlockSpec(memory_space=pltpu.VMEM),
            pl.BlockSpec(memory_space=pltpu.VMEM),
        ],
        out_specs=pl.BlockSpec(memory_space=pltpu.VMEM),
        out_shape=jax.ShapeDtypeStruct((lat_band, quarter), jnp.float32),
    )(slots, base, lat_points[:, None], tiles)


def body(
    atmos_fields,
    lat_points,
    wave_order,
    legendre,
    column_weight,
    block_remap,
    ocean_temp,
    ocean_salt,
    sea_mask,
):
    nfields, lev_dev, lat_band, lon_count = atmos_fields.shape
    wave_count = wave_order.shape[0]
    table, points = fourier_table(wave_order, lon_count)
    inverse_root = 1.0 / jnp.sqrt(lat_points.astype(jnp.float32))
    weights = jnp.where(
        2 * wave_order[None, :] < lat_points[:, None],
        inverse_root[:, None],
        jnp.zeros((), jnp.float32),
    )
    field_count = nfields
    ocean_rows, ocean_cols = ocean_temp.shape
    tile_count = ocean_rows * ocean_cols // BLOCK
    band_index = lax.axis_index(("lat", "ocn"))

    def slot_of(targets):
        return (targets // tile_count - band_index + 1) * tile_count + targets % tile_count

    local_slot = slot_of(block_remap.reshape(-1))
    quarter = lon_count // lax.axis_size("lev")
    full_remap = lev_gather(block_remap, 1)
    every_slot = slot_of(full_remap)
    raw_sums, sections = fused_transform(
        atmos_fields,
        lat_points,
        table,
        column_weight,
        every_slot,
        jnp.concatenate([weights, weights], axis=1),
        3 * tile_count,
    )
    raw_sums = raw_sums.reshape(field_count, lev_dev, lat_band, 2, wave_count)
    coeffs = raw_sums
    regrouped = lax.all_to_all(
        coeffs.transpose(4, 1, 0, 3, 2).reshape(wave_count, lev_dev * field_count * 2, lat_band),
        ("lat", "ocn"),
        split_axis=0,
        concat_axis=2,
        tiled=True,
    )
    spectra = jnp.einsum(
        "srj,sjd->srd",
        lev_gather(regrouped, 1),
        legendre,
        preferred_element_type=jnp.float32,
    )
    band_count = lax.axis_size(("lat", "ocn"))
    from_prev = lax.ppermute(
        sections[2], ("lat", "ocn"), [(i, i + 1) for i in range(band_count - 1)]
    )
    from_next = lax.ppermute(
        sections[0], ("lat", "ocn"), [(i + 1, i) for i in range(band_count - 1)]
    )
    arrived = (from_prev + sections[1]) + from_next
    tile_sums = lev_sum(arrived)
    forcing = (
        tile_sums.reshape(ocean_rows, ocean_cols // BLOCK, FIELDS, BLOCK)
        .transpose(2, 0, 1, 3)
        .reshape(FIELDS, ocean_rows, ocean_cols)
    )
    sea_cells = (
        jnp.broadcast_to(sea_mask[:, :, None], (ocean_rows, ocean_cols // BLOCK, BLOCK))
        .reshape(ocean_rows, ocean_cols)
        .astype(jnp.float32)
    )
    ocean_state = jnp.stack([ocean_temp, ocean_salt])
    padded = with_halo(ocean_state, ((("lat", "ocn"), 1),), 1)
    laplace = (
        padded[:, 2:]
        + padded[:, :-2]
        + jnp.roll(ocean_state, 1, 2)
        + jnp.roll(ocean_state, -1, 2)
        - 4.0 * ocean_state
    )
    updated = ocean_state + DIFFUSION * laplace + COUPLING * sea_cells[None] * forcing
    temp_next = updated[0]
    salt_next = updated[1]
    returned = with_halo(temp_next, ((("lat", "ocn"), 0),), ocean_rows)
    tiles_near = returned.reshape(3 * tile_count, BLOCK)
    base = (lax.axis_index("lev") * quarter).astype(jnp.int32).reshape(1)
    surface_temp = surface_gather(local_slot, base, lat_points, tiles_near, quarter)
    return (spectra, temp_next, salt_next, surface_temp)


def solution(mesh):
    placed = (
        P(None, "lev", ("lat", "ocn"), None),
        P(("lat", "ocn")),
        P(),
        P(("lat", "ocn"), None, "lev"),
        P(None, "lev"),
        P(("lat", "ocn"), "lev"),
        P(("lat", "ocn"), None),
        P(("lat", "ocn"), None),
        P(("lat", "ocn"), None),
    )
    return jax.shard_map(
        body,
        mesh=mesh,
        in_specs=placed,
        out_specs=(
            P(("lat", "ocn"), None, "lev"),
            P(("lat", "ocn"), None),
            P(("lat", "ocn"), None),
            P(("lat", "ocn"), "lev"),
        ),
        check_vma=False,
    )
```

```python
import math

import jax
import jax.numpy as jnp
from jax import lax
from jax.experimental import pallas as pl
from jax.experimental.pallas import tpu as pltpu
from jax.sharding import PartitionSpec as P

FIELDS = 2
BLOCK = 128


FULL_TURN = 2.0 * math.pi
DIFFUSION = 0.2
COUPLING = 0.5


def with_halo(cells, sides, width):
    for axis, dim in sides:
        count = lax.axis_size(axis)
        ends = count - 1
        head = lax.slice_in_dim(cells, 0, width, axis=dim)
        tail = lax.slice_in_dim(cells, cells.shape[dim] - width, cells.shape[dim], axis=dim)
        cells = jnp.concatenate(
            [
                lax.ppermute(tail, axis, [(i, (i + 1) % count) for i in range(ends)]),
                cells,
                lax.ppermute(head, axis, [((i + 1) % count, i) for i in range(ends)]),
            ],
            axis=dim,
        )
    return cells


def fourier_table(wave_order, length):
    points = jnp.arange(length, dtype=jnp.int32)
    phase = wave_order[:, None] * points[None, :] % length
    angle = phase.astype(jnp.float32) * (FULL_TURN / length)
    table = (jnp.cos(angle).astype(jnp.bfloat16), (-jnp.sin(angle)).astype(jnp.bfloat16))
    return (table, points)


def lev_sum(values):
    count = lax.axis_size("lev")
    if count & (count - 1):
        return lax.psum(values, "lev")
    stride = 1
    while stride < count:
        values = values + lax.ppermute(values, "lev", [(i, i ^ stride) for i in range(count)])
        stride *= 2
    return values


def lev_gather(values, axis):
    count = lax.axis_size("lev")
    if count & (count - 1):
        return lax.all_gather(values, "lev", axis=axis, tiled=True)
    index = lax.axis_index("lev")
    stride = 1
    while stride < count:
        other = lax.ppermute(values, "lev", [(i, i ^ stride) for i in range(count)])
        upper = (index // stride) % 2 == 1
        values = jnp.where(
            upper,
            jnp.concatenate([other, values], axis=axis),
            jnp.concatenate([values, other], axis=axis),
        )
        stride *= 2
    return values


def row_block(rows):
    for size in (64, 32, 16):
        if rows % size == 0:
            return size
    return rows


def transform_kernel(
    points_ref,
    cells_ref,
    cos_ref,
    sin_ref,
    weight_ref,
    slot_ref,
    scale_ref,
    sums_ref,
    out_ref,
    acc_ref,
    table_ref,
    *scratch,
):
    step = pl.program_id(0)

    @pl.when(step == 0)
    def _():
        acc_ref[...] = jnp.zeros_like(acc_ref)
        half = cos_ref.shape[0]
        table_ref[:half] = cos_ref[...]
        table_ref[half:] = sin_ref[...]

    nfields, nlev, rows, lon_count = cells_ref.shape
    nslot = acc_ref.shape[0]
    nblocks = lon_count // BLOCK
    table = table_ref[...]
    keep = (lax.broadcasted_iota(jnp.int32, (rows, lon_count), 1) < points_ref[...]).astype(jnp.bfloat16)
    cells = cells_ref[...] * keep[None, None]
    if rows % 16 == 0:
        sums = lax.dot_general(
            cells.reshape(nfields * nlev * rows, lon_count),
            table,
            (((1,), (1,)), ((), ())),
            preferred_element_type=jnp.float32,
        )
        sums_ref[...] = (sums.reshape(sums_ref.shape) * scale_ref[...][None, None]).astype(sums_ref.dtype)
    else:
        for f in range(nfields):
            for l in range(nlev):
                sums_ref[f, l] = (
                    lax.dot_general(
                        cells[f, l], table, (((1,), (1,)), ((), ())), preferred_element_type=jnp.float32
                    )
                    * scale_ref[...]
                ).astype(sums_ref.dtype)
    pieces = []
    for f in range(nfields):
        flux = weight_ref[f, 0] * cells[f, 0].astype(jnp.float32)
        for l in range(1, nlev):
            flux = flux + weight_ref[f, l] * cells[f, l].astype(jnp.float32)
        high = flux.astype(jnp.bfloat16)
        pieces.append(high)
        pieces.append((flux - high.astype(jnp.float32)).astype(jnp.bfloat16))
    if scratch:
        (stacked_ref,) = scratch
        for b in range(nblocks):
            for p, piece in enumerate(pieces):
                stacked_ref[b * rows : (b + 1) * rows, p * BLOCK : (p + 1) * BLOCK] = piece[
                    :, b * BLOCK : (b + 1) * BLOCK
                ]
        stacked = stacked_ref[...]
    else:
        stacked = jnp.concatenate(
            [
                jnp.concatenate(
                    [p[:, b * BLOCK : (b + 1) * BLOCK].astype(jnp.float32) for p in pieces], axis=1
                )
                for b in range(nblocks)
            ],
            axis=0,
        ).astype(jnp.bfloat16)
    onehot = (
        lax.broadcasted_iota(jnp.int32, (nslot, nblocks * rows), 0) == slot_ref[0]
    ).astype(jnp.bfloat16)
    acc_ref[...] += jnp.dot(onehot, stacked, preferred_element_type=jnp.float32)

    @pl.when(step == pl.num_programs(0) - 1)
    def _():
        nsec, tiles, _ = out_ref.shape
        for s in range(nsec):
            for f in range(nfields):
                high = acc_ref[s * tiles : (s + 1) * tiles, 2 * f * BLOCK : (2 * f + 1) * BLOCK]
                low = acc_ref[s * tiles : (s + 1) * tiles, (2 * f + 1) * BLOCK : (2 * f + 2) * BLOCK]
                out_ref[s, :, f * BLOCK : (f + 1) * BLOCK] = high + low


def fused_transform(atmos_fields, lat_points, table, column_weight, slots, scale, nslot):
    nfields, nlev, lat_band, lon_count = atmos_fields.shape
    rows = row_block(lat_band)
    steps = lat_band // rows
    nblocks = lon_count // BLOCK
    half = table[0].shape[0]
    wave2 = 2 * half
    slot_rows = slots.reshape(steps, rows, nblocks).transpose(0, 2, 1).reshape(steps, 1, nblocks * rows)
    scratch = [
        pltpu.VMEM((nslot, 2 * nfields * BLOCK), jnp.float32),
        pltpu.VMEM((wave2, lon_count), jnp.bfloat16),
    ]
    if rows % 16 == 0:
        scratch.append(pltpu.VMEM((nblocks * rows, 2 * nfields * BLOCK), jnp.bfloat16))
    return pl.pallas_call(
        transform_kernel,
        grid=(steps,),
        in_specs=[
            pl.BlockSpec((rows, 1), lambda r: (r, 0)),
            pl.BlockSpec((nfields, nlev, rows, lon_count), lambda r: (0, 0, r, 0)),
            pl.BlockSpec((half, lon_count), lambda r: (0, 0)),
            pl.BlockSpec((half, lon_count), lambda r: (0, 0)),
            pl.BlockSpec(memory_space=pltpu.SMEM),
            pl.BlockSpec((1, 1, nblocks * rows), lambda r: (r, 0, 0)),
            pl.BlockSpec((rows, wave2), lambda r: (r, 0)),
        ],
        out_specs=[
            pl.BlockSpec((nfields, nlev, rows, wave2), lambda r: (0, 0, r, 0)),
            pl.BlockSpec((3, nslot // 3, nfields * BLOCK), lambda r: (0, 0, 0)),
        ],
        out_shape=[
            jax.ShapeDtypeStruct((nfields, nlev, lat_band, wave2), jnp.bfloat16),
            jax.ShapeDtypeStruct((3, nslot // 3, nfields * BLOCK), jnp.float32),
        ],
        scratch_shapes=scratch,
        compiler_params=pltpu.CompilerParams(dimension_semantics=("arbitrary",)),
    )(lat_points[:, None], atmos_fields, *table, column_weight.astype(jnp.float32), slot_rows, scale)


def surface_kernel(slot_ref, base_ref, limit_ref, tiles_ref, out_ref):
    lat_band, quarter = out_ref.shape
    nquarter = quarter // BLOCK
    group = 8
    sublane = lax.broadcasted_iota(jnp.int32, (group, BLOCK), 0)

    def per_group(g, carry):
        row0 = pl.multiple_of(g * group, group)
        for b in range(nquarter):
            rows = jnp.zeros((group, BLOCK), jnp.float32)
            for r in range(group):
                tile = slot_ref[(row0 + r) * nquarter + b]
                picked = jnp.broadcast_to(tiles_ref[pl.ds(tile, 1), :], (group, BLOCK))
                rows = jnp.where(sublane == r, picked, rows)
            out_ref[pl.ds(row0, group), b * BLOCK : (b + 1) * BLOCK] = rows
        return carry

    lax.fori_loop(0, lat_band // group, per_group, 0, unroll=2 if (lat_band // group) % 2 == 0 else 1)
    points = base_ref[0] + lax.broadcasted_iota(jnp.int32, (lat_band, quarter), 1)
    out_ref[...] = jnp.where(points < limit_ref[...], out_ref[...], 0.0)


def surface_gather(slots, base, lat_points, tiles, quarter):
    lat_band = lat_points.shape[0]
    return pl.pallas_call(
        surface_kernel,
        in_specs=[
            pl.BlockSpec(memory_space=pltpu.SMEM),
            pl.BlockSpec(memory_space=pltpu.SMEM),
            pl.BlockSpec(memory_space=pltpu.VMEM),
            pl.BlockSpec(memory_space=pltpu.VMEM),
        ],
        out_specs=pl.BlockSpec(memory_space=pltpu.VMEM),
        out_shape=jax.ShapeDtypeStruct((lat_band, quarter), jnp.float32),
    )(slots, base, lat_points[:, None], tiles)


def body(
    atmos_fields,
    lat_points,
    wave_order,
    legendre,
    column_weight,
    block_remap,
    ocean_temp,
    ocean_salt,
    sea_mask,
):
    nfields, lev_dev, lat_band, lon_count = atmos_fields.shape
    wave_count = wave_order.shape[0]
    table, points = fourier_table(wave_order, lon_count)
    inverse_root = 1.0 / jnp.sqrt(lat_points.astype(jnp.float32))
    weights = jnp.where(
        2 * wave_order[None, :] < lat_points[:, None],
        inverse_root[:, None],
        jnp.zeros((), jnp.float32),
    )
    field_count = nfields
    ocean_rows, ocean_cols = ocean_temp.shape
    tile_count = ocean_rows * ocean_cols // BLOCK
    band_index = lax.axis_index(("lat", "ocn"))

    def slot_of(targets):
        return (targets // tile_count - band_index + 1) * tile_count + targets % tile_count

    local_slot = slot_of(block_remap.reshape(-1))
    quarter = lon_count // lax.axis_size("lev")
    full_remap = lev_gather(block_remap, 1)
    every_slot = slot_of(full_remap)
    raw_sums, sections = fused_transform(
        atmos_fields,
        lat_points,
        table,
        column_weight,
        every_slot,
        jnp.concatenate([weights, weights], axis=1),
        3 * tile_count,
    )
    raw_sums = raw_sums.reshape(field_count, lev_dev, lat_band, 2, wave_count)
    coeffs = raw_sums
    regrouped = lax.all_to_all(
        coeffs.transpose(4, 1, 0, 3, 2).reshape(wave_count, lev_dev * field_count * 2, lat_band),
        ("lat", "ocn"),
        split_axis=0,
        concat_axis=2,
        tiled=True,
    )
    spectra = jnp.einsum(
        "srj,sjd->srd",
        lev_gather(regrouped, 1),
        legendre,
        preferred_element_type=jnp.float32,
    )
    band_count = lax.axis_size(("lat", "ocn"))
    from_prev = lax.ppermute(
        sections[2], ("lat", "ocn"), [(i, i + 1) for i in range(band_count - 1)]
    )
    from_next = lax.ppermute(
        sections[0], ("lat", "ocn"), [(i + 1, i) for i in range(band_count - 1)]
    )
    arrived = (from_prev + sections[1]) + from_next
    tile_sums = lev_sum(arrived)
    forcing = (
        tile_sums.reshape(ocean_rows, ocean_cols // BLOCK, FIELDS, BLOCK)
        .transpose(2, 0, 1, 3)
        .reshape(FIELDS, ocean_rows, ocean_cols)
    )
    sea_cells = (
        jnp.broadcast_to(sea_mask[:, :, None], (ocean_rows, ocean_cols // BLOCK, BLOCK))
        .reshape(ocean_rows, ocean_cols)
        .astype(jnp.float32)
    )
    ocean_state = jnp.stack([ocean_temp, ocean_salt])
    padded = with_halo(ocean_state, ((("lat", "ocn"), 1),), 1)
    laplace = (
        padded[:, 2:]
        + padded[:, :-2]
        + jnp.roll(ocean_state, 1, 2)
        + jnp.roll(ocean_state, -1, 2)
        - 4.0 * ocean_state
    )
    updated = ocean_state + DIFFUSION * laplace + COUPLING * sea_cells[None] * forcing
    temp_next = updated[0]
    salt_next = updated[1]
    returned = with_halo(temp_next, ((("lat", "ocn"), 0),), ocean_rows)
    tiles_near = returned.reshape(3 * tile_count, BLOCK)
    base = (lax.axis_index("lev") * quarter).astype(jnp.int32).reshape(1)
    surface_temp = surface_gather(local_slot, base, lat_points, tiles_near, quarter)
    return (spectra, temp_next, salt_next, surface_temp)


def solution(mesh):
    placed = (
        P(None, "lev", ("lat", "ocn"), None),
        P(("lat", "ocn")),
        P(),
        P(("lat", "ocn"), None, "lev"),
        P(None, "lev"),
        P(("lat", "ocn"), "lev"),
        P(("lat", "ocn"), None),
        P(("lat", "ocn"), None),
        P(("lat", "ocn"), None),
    )
    return jax.shard_map(
        body,
        mesh=mesh,
        in_specs=placed,
        out_specs=(
            P(("lat", "ocn"), None, "lev"),
            P(("lat", "ocn"), None),
            P(("lat", "ocn"), None),
            P(("lat", "ocn"), "lev"),
        ),
        check_vma=False,
    )
```

```python
import math

import jax
import jax.numpy as jnp
from jax import lax
from jax.experimental import pallas as pl
from jax.experimental.pallas import tpu as pltpu
from jax.sharding import PartitionSpec as P

FIELDS = 2
BLOCK = 128


FULL_TURN = 2.0 * math.pi
DIFFUSION = 0.2
COUPLING = 0.5


def with_halo(cells, sides, width):
    for axis, dim in sides:
        count = lax.axis_size(axis)
        ends = count - 1
        head = lax.slice_in_dim(cells, 0, width, axis=dim)
        tail = lax.slice_in_dim(cells, cells.shape[dim] - width, cells.shape[dim], axis=dim)
        cells = jnp.concatenate(
            [
                lax.ppermute(tail, axis, [(i, (i + 1) % count) for i in range(ends)]),
                cells,
                lax.ppermute(head, axis, [((i + 1) % count, i) for i in range(ends)]),
            ],
            axis=dim,
        )
    return cells


def fourier_table(wave_order, length):
    points = jnp.arange(length, dtype=jnp.int32)
    phase = wave_order[:, None] * points[None, :] % length
    angle = phase.astype(jnp.float32) * (FULL_TURN / length)
    table = jnp.concatenate([jnp.cos(angle), -jnp.sin(angle)], axis=0).astype(jnp.bfloat16)
    return (table, points)


def lev_sum(values):
    count = lax.axis_size("lev")
    if count & (count - 1):
        return lax.psum(values, "lev")
    stride = 1
    while stride < count:
        values = values + lax.ppermute(values, "lev", [(i, i ^ stride) for i in range(count)])
        stride *= 2
    return values


def lev_gather(values, axis):
    count = lax.axis_size("lev")
    if count & (count - 1):
        return lax.all_gather(values, "lev", axis=axis, tiled=True)
    index = lax.axis_index("lev")
    stride = 1
    while stride < count:
        other = lax.ppermute(values, "lev", [(i, i ^ stride) for i in range(count)])
        upper = (index // stride) % 2 == 1
        values = jnp.where(
            upper,
            jnp.concatenate([other, values], axis=axis),
            jnp.concatenate([values, other], axis=axis),
        )
        stride *= 2
    return values


def row_block(rows):
    for size in (32, 16):
        if rows % size == 0:
            return size
    return rows


def transform_kernel(
    points_ref, cells_ref, table_ref, weight_ref, slot_ref, scale_ref, sums_ref, out_ref, acc_ref, *scratch
):
    step = pl.program_id(0)

    @pl.when(step == 0)
    def _():
        acc_ref[...] = jnp.zeros_like(acc_ref)

    nfields, nlev, rows, lon_count = cells_ref.shape
    nslot = acc_ref.shape[0]
    nblocks = lon_count // BLOCK
    table = table_ref[...]
    keep = (lax.broadcasted_iota(jnp.int32, (rows, lon_count), 1) < points_ref[...]).astype(jnp.bfloat16)
    cells = cells_ref[...] * keep[None, None]
    if rows % 16 == 0:
        sums = lax.dot_general(
            cells.reshape(nfields * nlev * rows, lon_count),
            table,
            (((1,), (1,)), ((), ())),
            preferred_element_type=jnp.float32,
        )
        sums_ref[...] = (sums.reshape(sums_ref.shape) * scale_ref[...][None, None]).astype(sums_ref.dtype)
    else:
        for f in range(nfields):
            for l in range(nlev):
                sums_ref[f, l] = (
                    lax.dot_general(
                        cells[f, l], table, (((1,), (1,)), ((), ())), preferred_element_type=jnp.float32
                    )
                    * scale_ref[...]
                ).astype(sums_ref.dtype)
    pieces = []
    for f in range(nfields):
        flux = weight_ref[f, 0] * cells[f, 0].astype(jnp.float32)
        for l in range(1, nlev):
            flux = flux + weight_ref[f, l] * cells[f, l].astype(jnp.float32)
        high = flux.astype(jnp.bfloat16)
        pieces.append(high)
        pieces.append((flux - high.astype(jnp.float32)).astype(jnp.bfloat16))
    if scratch:
        (stacked_ref,) = scratch
        for b in range(nblocks):
            for p, piece in enumerate(pieces):
                stacked_ref[b * rows : (b + 1) * rows, p * BLOCK : (p + 1) * BLOCK] = piece[
                    :, b * BLOCK : (b + 1) * BLOCK
                ]
        stacked = stacked_ref[...]
    else:
        stacked = jnp.concatenate(
            [
                jnp.concatenate(
                    [p[:, b * BLOCK : (b + 1) * BLOCK].astype(jnp.float32) for p in pieces], axis=1
                )
                for b in range(nblocks)
            ],
            axis=0,
        ).astype(jnp.bfloat16)
    onehot = (
        lax.broadcasted_iota(jnp.int32, (nslot, nblocks * rows), 0) == slot_ref[0]
    ).astype(jnp.bfloat16)
    acc_ref[...] += jnp.dot(onehot, stacked, preferred_element_type=jnp.float32)

    @pl.when(step == pl.num_programs(0) - 1)
    def _():
        nsec, tiles, _ = out_ref.shape
        for s in range(nsec):
            for f in range(nfields):
                high = acc_ref[s * tiles : (s + 1) * tiles, 2 * f * BLOCK : (2 * f + 1) * BLOCK]
                low = acc_ref[s * tiles : (s + 1) * tiles, (2 * f + 1) * BLOCK : (2 * f + 2) * BLOCK]
                out_ref[s, :, f * BLOCK : (f + 1) * BLOCK] = high + low


def fused_transform(atmos_fields, lat_points, table, column_weight, slots, scale, nslot):
    nfields, nlev, lat_band, lon_count = atmos_fields.shape
    rows = row_block(lat_band)
    steps = lat_band // rows
    nblocks = lon_count // BLOCK
    wave2 = table.shape[0]
    slot_rows = slots.reshape(steps, rows, nblocks).transpose(0, 2, 1).reshape(steps, 1, nblocks * rows)
    scratch = [pltpu.VMEM((nslot, 2 * nfields * BLOCK), jnp.float32)]
    if rows % 16 == 0:
        scratch.append(pltpu.VMEM((nblocks * rows, 2 * nfields * BLOCK), jnp.bfloat16))
    return pl.pallas_call(
        transform_kernel,
        grid=(steps,),
        in_specs=[
            pl.BlockSpec((rows, 1), lambda r: (r, 0)),
            pl.BlockSpec((nfields, nlev, rows, lon_count), lambda r: (0, 0, r, 0)),
            pl.BlockSpec((wave2, lon_count), lambda r: (0, 0)),
            pl.BlockSpec(memory_space=pltpu.SMEM),
            pl.BlockSpec((1, 1, nblocks * rows), lambda r: (r, 0, 0)),
            pl.BlockSpec((rows, wave2), lambda r: (r, 0)),
        ],
        out_specs=[
            pl.BlockSpec((nfields, nlev, rows, wave2), lambda r: (0, 0, r, 0)),
            pl.BlockSpec((3, nslot // 3, nfields * BLOCK), lambda r: (0, 0, 0)),
        ],
        out_shape=[
            jax.ShapeDtypeStruct((nfields, nlev, lat_band, wave2), jnp.bfloat16),
            jax.ShapeDtypeStruct((3, nslot // 3, nfields * BLOCK), jnp.float32),
        ],
        scratch_shapes=scratch,
        compiler_params=pltpu.CompilerParams(dimension_semantics=("arbitrary",)),
    )(lat_points[:, None], atmos_fields, table, column_weight.astype(jnp.float32), slot_rows, scale)


def surface_kernel(slot_ref, base_ref, limit_ref, tiles_ref, out_ref):
    lat_band, quarter = out_ref.shape
    nquarter = quarter // BLOCK
    group = 8
    sublane = lax.broadcasted_iota(jnp.int32, (group, BLOCK), 0)

    def per_group(g, carry):
        row0 = pl.multiple_of(g * group, group)
        for b in range(nquarter):
            rows = jnp.zeros((group, BLOCK), jnp.float32)
            for r in range(group):
                tile = slot_ref[(row0 + r) * nquarter + b]
                picked = jnp.broadcast_to(tiles_ref[pl.ds(tile, 1), :], (group, BLOCK))
                rows = jnp.where(sublane == r, picked, rows)
            out_ref[pl.ds(row0, group), b * BLOCK : (b + 1) * BLOCK] = rows
        return carry

    lax.fori_loop(0, lat_band // group, per_group, 0, unroll=2 if (lat_band // group) % 2 == 0 else 1)
    points = base_ref[0] + lax.broadcasted_iota(jnp.int32, (lat_band, quarter), 1)
    out_ref[...] = jnp.where(points < limit_ref[...], out_ref[...], 0.0)


def surface_gather(slots, base, lat_points, tiles, quarter):
    lat_band = lat_points.shape[0]
    return pl.pallas_call(
        surface_kernel,
        in_specs=[
            pl.BlockSpec(memory_space=pltpu.SMEM),
            pl.BlockSpec(memory_space=pltpu.SMEM),
            pl.BlockSpec(memory_space=pltpu.VMEM),
            pl.BlockSpec(memory_space=pltpu.VMEM),
        ],
        out_specs=pl.BlockSpec(memory_space=pltpu.VMEM),
        out_shape=jax.ShapeDtypeStruct((lat_band, quarter), jnp.float32),
    )(slots, base, lat_points[:, None], tiles)


def body(
    atmos_fields,
    lat_points,
    wave_order,
    legendre,
    column_weight,
    block_remap,
    ocean_temp,
    ocean_salt,
    sea_mask,
):
    nfields, lev_dev, lat_band, lon_count = atmos_fields.shape
    wave_count = wave_order.shape[0]
    table, points = fourier_table(wave_order, lon_count)
    inverse_root = 1.0 / jnp.sqrt(lat_points.astype(jnp.float32))
    weights = jnp.where(
        2 * wave_order[None, :] < lat_points[:, None],
        inverse_root[:, None],
        jnp.zeros((), jnp.float32),
    )
    field_count = nfields
    ocean_rows, ocean_cols = ocean_temp.shape
    tile_count = ocean_rows * ocean_cols // BLOCK
    band_index = lax.axis_index(("lat", "ocn"))

    def slot_of(targets):
        return (targets // tile_count - band_index + 1) * tile_count + targets % tile_count

    local_slot = slot_of(block_remap.reshape(-1))
    quarter = lon_count // lax.axis_size("lev")
    full_remap = lev_gather(block_remap, 1)
    every_slot = slot_of(full_remap)
    raw_sums, sections = fused_transform(
        atmos_fields,
        lat_points,
        table,
        column_weight,
        every_slot,
        jnp.concatenate([weights, weights], axis=1),
        3 * tile_count,
    )
    raw_sums = raw_sums.reshape(field_count, lev_dev, lat_band, 2, wave_count)
    coeffs = raw_sums
    regrouped = lax.all_to_all(
        coeffs.transpose(4, 1, 0, 3, 2).reshape(wave_count, lev_dev * field_count * 2, lat_band),
        ("lat", "ocn"),
        split_axis=0,
        concat_axis=2,
        tiled=True,
    )
    spectra = jnp.einsum(
        "srj,sjd->srd",
        lev_gather(regrouped, 1),
        legendre,
        preferred_element_type=jnp.float32,
    )
    band_count = lax.axis_size(("lat", "ocn"))
    from_prev = lax.ppermute(
        sections[2], ("lat", "ocn"), [(i, i + 1) for i in range(band_count - 1)]
    )
    from_next = lax.ppermute(
        sections[0], ("lat", "ocn"), [(i + 1, i) for i in range(band_count - 1)]
    )
    arrived = (from_prev + sections[1]) + from_next
    tile_sums = lev_sum(arrived)
    forcing = (
        tile_sums.reshape(ocean_rows, ocean_cols // BLOCK, FIELDS, BLOCK)
        .transpose(2, 0, 1, 3)
        .reshape(FIELDS, ocean_rows, ocean_cols)
    )
    sea_cells = (
        jnp.broadcast_to(sea_mask[:, :, None], (ocean_rows, ocean_cols // BLOCK, BLOCK))
        .reshape(ocean_rows, ocean_cols)
        .astype(jnp.float32)
    )
    ocean_state = jnp.stack([ocean_temp, ocean_salt])
    padded = with_halo(ocean_state, ((("lat", "ocn"), 1),), 1)
    laplace = (
        padded[:, 2:]
        + padded[:, :-2]
        + jnp.roll(ocean_state, 1, 2)
        + jnp.roll(ocean_state, -1, 2)
        - 4.0 * ocean_state
    )
    updated = ocean_state + DIFFUSION * laplace + COUPLING * sea_cells[None] * forcing
    temp_next = updated[0]
    salt_next = updated[1]
    returned = with_halo(temp_next, ((("lat", "ocn"), 0),), ocean_rows)
    tiles_near = returned.reshape(3 * tile_count, BLOCK)
    base = (lax.axis_index("lev") * quarter).astype(jnp.int32).reshape(1)
    surface_temp = surface_gather(local_slot, base, lat_points, tiles_near, quarter)
    return (spectra, temp_next, salt_next, surface_temp)


def solution(mesh):
    placed = (
        P(None, "lev", ("lat", "ocn"), None),
        P(("lat", "ocn")),
        P(),
        P(("lat", "ocn"), None, "lev"),
        P(None, "lev"),
        P(("lat", "ocn"), "lev"),
        P(("lat", "ocn"), None),
        P(("lat", "ocn"), None),
        P(("lat", "ocn"), None),
    )
    return jax.shard_map(
        body,
        mesh=mesh,
        in_specs=placed,
        out_specs=(
            P(("lat", "ocn"), None, "lev"),
            P(("lat", "ocn"), None),
            P(("lat", "ocn"), None),
            P(("lat", "ocn"), "lev"),
        ),
        check_vma=False,
    )
```
